32 devices in a mesh: mass: 8 (over y, x, core), scen: 4 (over z).
Axes of the slice: x: 2, y: 2, z: 4, core: 2. Of those that a mesh axis runs over, the one named last changes fastest.
Arguments:
- density: float32 [4, 524288], P('scen', 'mass'), may hold values from 0.01 to 68
- cotangent: float32 [4, 524288], P('scen', 'mass'), may hold values from -16.5 to 17.5
- rate: float32 [524288], P('mass'), may hold values from 0.2 to 2
Outputs:
- tendency: float32 [4, 524288], P('scen', 'mass')
- adjoint_density: float32 [4, 524288], P('scen', 'mass')
- rate_gradient: float32 [524288], P('mass')
The draws below stay inside these ranges and needn't reach their ends.
All inputs are finite; a program needn't handle non-finite values.
Results may differ from the reference program's by a relative error of at most 0.00008.
Values sent between devices are 32-bit elements; how exact they have to be, the bound alone decides.
No kernel may reach another device: no remote copies, remote signals or barrier semaphores. Data moves between devices by JAX's collectives and lax.ppermute only.
A program may use at most 64 MiB of HBM per device.

```python
import math
import jax
import jax.numpy as jnp
from jax import lax

C1 = 32
C2 = 128
ROWS = 16
NBIN = 524288
SCEN = 4


def peak_field(key, low_height, high_height, signed):
    cell_count = min(256, NBIN // 64)
    cell_width = NBIN // cell_count
    sigma_high = min(64.0, cell_width / 8.0)
    key_height = jax.random.fold_in(key, 11)
    key_center = jax.random.fold_in(key, 12)
    key_width = jax.random.fold_in(key, 13)
    key_sign = jax.random.fold_in(key, 14)
    shape = (SCEN, cell_count)
    heights = jnp.exp(jax.random.uniform(key_height, shape, jnp.float32, math.log(low_height), math.log(high_height)))
    if signed:
        signs = jnp.where(jax.random.uniform(key_sign, shape, jnp.float32) < 0.5, -1.0, 1.0)
        heights = heights * signs
    centers = cell_width * (0.375 + 0.25 * jax.random.uniform(key_center, shape, jnp.float32))
    widths = jnp.exp(jax.random.uniform(key_width, shape, jnp.float32, math.log(2.0), math.log(sigma_high)))
    positions = jnp.arange(NBIN, dtype=jnp.int32)
    cell_of = positions // cell_width
    within = (positions - cell_of * cell_width).astype(jnp.float32)
    height_at = heights[:, cell_of]
    center_at = centers[:, cell_of]
    width_at = widths[:, cell_of]
    scaled = (within[None, :] - center_at) / width_at
    return height_at * jnp.exp(-0.5 * scaled * scaled)


def shard_edges():
    positions = jnp.arange(NBIN, dtype=jnp.int32)
    edge = (positions + 1) % (ROWS * C1 * C2) == 0
    return jnp.where(edge, 60.0, 0.0).astype(jnp.float32)


def draw_density(key, part):
    key_back = jax.random.fold_in(key, 1)
    key_peak = jax.random.fold_in(key, 2)
    background = jnp.exp(jax.random.uniform(key_back, (SCEN, NBIN), jnp.float32, math.log(0.01), math.log(4.0)))
    peaks = peak_field(key_peak, 4.0, 64.0, False)
    return (background + peaks + shard_edges()[None, :]).astype(jnp.float32)


def draw_cotangent(key, part):
    key_back = jax.random.fold_in(key, 3)
    key_peak = jax.random.fold_in(key, 4)
    background = jax.random.uniform(key_back, (SCEN, NBIN), jnp.float32, -0.5, 1.5)
    peaks = peak_field(key_peak, 2.0, 16.0, True)
    return (background + peaks).astype(jnp.float32)


def block_scale(rng, extent, shards, smallest, high):
    def one(position, parts):
        draws = jax.random.uniform(jax.random.fold_in(jax.random.fold_in(rng, 6), position), (parts,), jnp.float32, smallest / len(shards), high / len(shards))
        return jnp.repeat(jnp.exp(draws), extent[position] // parts).reshape((-1,) + (1,) * (len(extent) - position - 1))

    loudness = one(*shards[0])
    for cut in shards[1:]:
        loudness = loudness * one(*cut)
    return loudness


def setup_inputs(seed: int = 0) -> dict:
    splits = jax.random.split(jax.random.key(seed), 4)
    return {
        "density": draw_density(jax.random.fold_in(splits[3], 71), 0),
        "cotangent": draw_cotangent(jax.random.fold_in(splits[3], 71), 0),
        "rate": jnp.clip(jnp.exp(math.log(2.0) - 2.3025851 * jax.random.uniform(splits[2], (NBIN,), jnp.float32) ** block_scale(splits[2], (NBIN,), ((0, 8),), -0.2, 0.2)), 0.2, 2.0),
    }


def reference(density, cotangent, rate):
    mass = (jnp.arange(NBIN, dtype=jnp.float32) + 0.5) / NBIN
    beta = 12.0 / NBIN
    length = 2 * NBIN

    def single(pair):
        numbers, adjoint_in = pair
        weighted = mass * numbers
        first = jnp.sum(weighted)
        cross = jnp.sum(adjoint_in * weighted)
        spectrum = jnp.fft.rfft(weighted, n=length)
        adj_spectrum = jnp.fft.rfft(adjoint_in, n=length)
        birth = jnp.fft.irfft(spectrum * spectrum, n=length)[:NBIN].astype(jnp.float32)
        corr = jnp.fft.irfft(adj_spectrum * jnp.conj(spectrum), n=length)[:NBIN].astype(jnp.float32)
        flux = rate * weighted
        inflow = jnp.concatenate([jnp.zeros((1,), jnp.float32), flux[:-1]])
        tendency = 0.5 * beta * birth - beta * first * weighted - flux + inflow
        following = jnp.concatenate([adjoint_in[1:], jnp.zeros((1,), jnp.float32)])
        adjoint = mass * (beta * corr - beta * first * adjoint_in - beta * cross - rate * adjoint_in + rate * following)
        gradient = weighted * (following - adjoint_in)
        return tendency, adjoint, gradient

    tendency, adjoint, gradient = lax.map(single, (density, cotangent))
    return tendency, adjoint, jnp.sum(gradient, axis=0)
```

```python
import math

import jax
import jax.numpy as jnp
from jax import lax
from jax.sharding import PartitionSpec as P

C1 = 32
C2 = 128


aggregation_coef = 12.0


def from_behind(value, axis, steps):
    count = lax.axis_size(axis)
    first, last = (max(0, -steps), min(count, count - steps))
    return lax.ppermute(value, axis, [(source, source + steps) for source in range(first, last)])


def phases(left, right, total):
    outer = left[:, None] * right[None, :] % total
    angle = outer.astype(jnp.float32) * (2.0 * math.pi / total)
    return (jnp.cos(angle), jnp.sin(angle))


def counting(count):
    return lax.iota(jnp.int32, count)


def complex_dot(form, table, values):
    table_re, table_im = table
    val_re, val_im = values
    high = lax.Precision.HIGHEST
    real_out = jnp.einsum(form, table_re, val_re, precision=high) - jnp.einsum(
        form, table_im, val_im, precision=high
    )
    imag_out = jnp.einsum(form, table_re, val_im, precision=high) + jnp.einsum(
        form, table_im, val_re, precision=high
    )
    return (real_out, imag_out)


def complex_mul(left, right):
    return (left[0] * right[0] - left[1] * right[1], left[0] * right[1] + left[1] * right[0])


def column_forward(values):
    lead = values[0].shape[:-1]
    shaped = (values[0].reshape(lead + (C1, C2)), values[1].reshape(lead + (C1, C2)))
    cos_one, sin_one = phases(counting(C1), counting(C1), C1)
    step_one = complex_dot("pa,...ab->...pb", (cos_one, -sin_one), shaped)
    tw_cos, tw_sin = phases(counting(C1), counting(C2), C1 * C2)
    turned = complex_mul(step_one, (tw_cos, -tw_sin))
    cos_two, sin_two = phases(counting(C2), counting(C2), C2)
    return complex_dot("qb,...pb->...pq", (cos_two, -sin_two), turned)


def column_inverse(values):
    lead = values[0].shape[:-2]
    cos_two, sin_two = phases(counting(C2), counting(C2), C2)
    step_one = complex_dot("qb,...pq->...pb", (cos_two, sin_two), values)
    tw_cos, tw_sin = phases(counting(C1), counting(C2), C1 * C2)
    turned = complex_mul(step_one, (tw_cos, tw_sin))
    cos_one, sin_one = phases(counting(C1), counting(C1), C1)
    result = complex_dot("pa,...pb->...ab", (cos_one, sin_one), turned)
    return (result[0].reshape(lead + (C1 * C2,)), result[1].reshape(lead + (C1 * C2,)))


def exchange(value):
    return lax.all_to_all(value, "mass", 0, 0, tiled=True)


def shards(density, cotangent, rate):
    high = lax.Precision.HIGHEST
    scen_dev, bin_dev = density.shape
    arrays = 2 * scen_dev
    parts = lax.axis_size("mass")
    place = lax.axis_index("mass")
    width = C1 * C2
    rows = bin_dev // width
    half_rows = rows * parts
    full_rows = 2 * half_rows
    cols = width // parts
    block = full_rows // parts
    nbin = half_rows * width
    nfft = 2 * nbin
    beta = aggregation_coef / nbin
    offset = place * bin_dev
    mass = ((offset + counting(bin_dev)).astype(jnp.float32) + 0.5) / nbin
    weighted = mass[None, :] * density
    moments = lax.psum(
        jnp.stack([jnp.sum(weighted, axis=1), jnp.sum(cotangent * weighted, axis=1)]), "mass"
    )
    first, cross = moments[0], moments[1]
    stacked = jnp.concatenate([weighted, cotangent], axis=0).reshape(arrays, rows, parts, cols)
    spread = exchange(stacked.transpose(2, 0, 1, 3))
    spread = spread.transpose(1, 0, 2, 3).reshape(arrays, half_rows, cols)
    cos_rows, sin_rows = phases(counting(full_rows), counting(half_rows), full_rows)
    freq_re = jnp.einsum("kr,srw->skw", cos_rows, spread, precision=high)
    freq_im = -jnp.einsum("kr,srw->skw", sin_rows, spread, precision=high)
    column_index = place * cols + counting(cols)
    tw_cos, tw_sin = phases(counting(full_rows), column_index, nfft)
    twisted = jnp.stack(complex_mul((freq_re, freq_im), (tw_cos, -tw_sin)))
    twisted = twisted.reshape(2, arrays, parts, block, cols).transpose(2, 0, 1, 3, 4)
    moved = exchange(twisted).transpose(1, 2, 3, 0, 4).reshape(2, arrays, block, width)
    spec_re, spec_im = column_forward((moved[0], moved[1]))
    dist_spec = (spec_re[:scen_dev], spec_im[:scen_dev])
    cot_spec = (spec_re[scen_dev:], spec_im[scen_dev:])
    birth_spec = complex_mul(dist_spec, dist_spec)
    adjoint_spec = complex_mul(cot_spec, (dist_spec[0], -dist_spec[1]))
    joined = (
        jnp.concatenate([birth_spec[0], adjoint_spec[0]], axis=0),
        jnp.concatenate([birth_spec[1], adjoint_spec[1]], axis=0),
    )
    inverted = column_inverse(joined)
    row_index = place * block + counting(block)
    back_cos, back_sin = phases(row_index, counting(width), nfft)
    untwisted = jnp.stack(complex_mul(inverted, (back_cos, back_sin)))
    untwisted = untwisted.reshape(2, arrays, block, parts, cols).transpose(3, 0, 1, 2, 4)
    returned = exchange(untwisted).transpose(1, 2, 0, 3, 4).reshape(2, arrays, full_rows, cols)
    inv_cos, inv_sin = phases(counting(half_rows), counting(full_rows), full_rows)
    real_part = jnp.einsum("rk,skw->srw", inv_cos, returned[0], precision=high) - jnp.einsum(
        "rk,skw->srw", inv_sin, returned[1], precision=high
    )
    real_part = real_part.reshape(arrays, parts, rows, cols).transpose(1, 0, 2, 3)
    gathered = exchange(real_part).transpose(1, 2, 0, 3).reshape(arrays, bin_dev) / nfft
    birth = gathered[:scen_dev]
    corr = gathered[scen_dev:]
    flux = rate[None, :] * weighted
    incoming = from_behind(flux[:, -1:], "mass", 1)
    inflow = jnp.concatenate([incoming, flux[:, :-1]], axis=1)
    tendency = 0.5 * beta * birth - beta * first[:, None] * weighted - flux + inflow
    arriving = from_behind(cotangent[:, :1], "mass", -1)
    following = jnp.concatenate([cotangent[:, 1:], arriving], axis=1)
    adjoint = mass[None, :] * (
        beta * corr
        - beta * first[:, None] * cotangent
        - beta * cross[:, None]
        - rate[None, :] * cotangent
        + rate[None, :] * following
    )
    local_grad = jnp.sum(weighted * (following - cotangent), axis=0)
    rate_gradient = lax.psum(local_grad, "scen")
    return (tendency, adjoint, rate_gradient)


def solution(mesh):
    in_specs = (P("scen", "mass"), P("scen", "mass"), P("mass"))
    out_specs = (P("scen", "mass"), P("scen", "mass"), P("mass"))
    return jax.shard_map(shards, mesh=mesh, in_specs=in_specs, out_specs=out_specs, check_vma=False)
```

```python
import math

import jax
import jax.numpy as jnp
from jax import lax
from jax.sharding import PartitionSpec as P

C1 = 32
C2 = 128


aggregation_coef = 12.0


def from_behind(value, axis, steps):
    count = lax.axis_size(axis)
    first, last = (max(0, -steps), min(count, count - steps))
    return lax.ppermute(value, axis, [(source, source + steps) for source in range(first, last)])


def phases(left, right, total):
    outer = left[:, None] * right[None, :] % total
    angle = outer.astype(jnp.float32) * (2.0 * math.pi / total)
    return (jnp.cos(angle), jnp.sin(angle))


def counting(count):
    return lax.iota(jnp.int32, count)


def complex_dot(form, table, values):
    table_re, table_im = table
    val_re, val_im = values
    high = lax.Precision.HIGHEST
    real_out = jnp.einsum(form, table_re, val_re, precision=high) - jnp.einsum(
        form, table_im, val_im, precision=high
    )
    imag_out = jnp.einsum(form, table_re, val_im, precision=high) + jnp.einsum(
        form, table_im, val_re, precision=high
    )
    return (real_out, imag_out)


def complex_mul(left, right):
    return (left[0] * right[0] - left[1] * right[1], left[0] * right[1] + left[1] * right[0])


def column_forward(values):
    lead = values[0].shape[:-1]
    shaped = (values[0].reshape(lead + (C1, C2)), values[1].reshape(lead + (C1, C2)))
    cos_one, sin_one = phases(counting(C1), counting(C1), C1)
    step_one = complex_dot("pa,...ab->...pb", (cos_one, -sin_one), shaped)
    tw_cos, tw_sin = phases(counting(C1), counting(C2), C1 * C2)
    turned = complex_mul(step_one, (tw_cos, -tw_sin))
    cos_two, sin_two = phases(counting(C2), counting(C2), C2)
    return complex_dot("qb,...pb->...pq", (cos_two, -sin_two), turned)


def column_inverse(values):
    lead = values[0].shape[:-2]
    cos_two, sin_two = phases(counting(C2), counting(C2), C2)
    step_one = complex_dot("qb,...pq->...pb", (cos_two, sin_two), values)
    tw_cos, tw_sin = phases(counting(C1), counting(C2), C1 * C2)
    turned = complex_mul(step_one, (tw_cos, tw_sin))
    cos_one, sin_one = phases(counting(C1), counting(C1), C1)
    result = complex_dot("pa,...pb->...ab", (cos_one, sin_one), turned)
    return (result[0].reshape(lead + (C1 * C2,)), result[1].reshape(lead + (C1 * C2,)))


def exchange(value):
    return lax.all_to_all(value, "mass", 0, 0, tiled=True)


def shards(density, cotangent, rate):
    high = lax.Precision.HIGHEST
    scen_dev, bin_dev = density.shape
    arrays = 2 * scen_dev
    parts = lax.axis_size("mass")
    place = lax.axis_index("mass")
    width = C1 * C2
    rows = bin_dev // width
    half_rows = rows * parts
    full_rows = 2 * half_rows
    cols = width // parts
    block = full_rows // parts
    nbin = half_rows * width
    nfft = 2 * nbin
    beta = aggregation_coef / nbin
    offset = place * bin_dev
    mass = ((offset + counting(bin_dev)).astype(jnp.float32) + 0.5) / nbin
    weighted = mass[None, :] * density
    partial = jnp.concatenate([jnp.sum(weighted, axis=1), jnp.sum(cotangent * weighted, axis=1)])
    tile = jnp.zeros((8, cols), jnp.float32).at[0, :arrays].set(partial)
    stacked = jnp.concatenate([weighted, cotangent], axis=0).reshape(arrays, rows, parts, cols)
    outgoing = stacked.transpose(2, 0, 1, 3).reshape(parts, arrays * rows, cols)
    outgoing = jnp.concatenate([outgoing, jnp.broadcast_to(tile, (parts, 8, cols))], axis=1)
    incoming_rows = exchange(outgoing)
    moments = jnp.sum(incoming_rows[:, arrays * rows, :arrays], axis=0)
    first, cross = moments[:scen_dev], moments[scen_dev:]
    spread = incoming_rows[:, : arrays * rows].reshape(parts, arrays, rows, cols)
    spread = spread.transpose(1, 0, 2, 3).reshape(arrays, half_rows, cols)
    cos_rows, sin_rows = phases(counting(full_rows), counting(half_rows), full_rows)
    freq_re = jnp.einsum("kr,srw->skw", cos_rows, spread, precision=high)
    freq_im = -jnp.einsum("kr,srw->skw", sin_rows, spread, precision=high)
    column_index = place * cols + counting(cols)
    tw_cos, tw_sin = phases(counting(full_rows), column_index, nfft)
    twisted = jnp.stack(complex_mul((freq_re, freq_im), (tw_cos, -tw_sin)))
    twisted = twisted.reshape(2, arrays, parts, block, cols).transpose(2, 0, 1, 3, 4)
    moved = exchange(twisted).transpose(1, 2, 3, 0, 4).reshape(2, arrays, block, width)
    spec_re, spec_im = column_forward((moved[0], moved[1]))
    dist_spec = (spec_re[:scen_dev], spec_im[:scen_dev])
    cot_spec = (spec_re[scen_dev:], spec_im[scen_dev:])
    birth_spec = complex_mul(dist_spec, dist_spec)
    adjoint_spec = complex_mul(cot_spec, (dist_spec[0], -dist_spec[1]))
    joined = (
        jnp.concatenate([birth_spec[0], adjoint_spec[0]], axis=0),
        jnp.concatenate([birth_spec[1], adjoint_spec[1]], axis=0),
    )
    inverted = column_inverse(joined)
    row_index = place * block + counting(block)
    back_cos, back_sin = phases(row_index, counting(width), nfft)
    untwisted = jnp.stack(complex_mul(inverted, (back_cos, back_sin)))
    untwisted = untwisted.reshape(2, arrays, block, parts, cols).transpose(3, 0, 1, 2, 4)
    returned = exchange(untwisted).transpose(1, 2, 0, 3, 4).reshape(2, arrays, full_rows, cols)
    inv_cos, inv_sin = phases(counting(half_rows), counting(full_rows), full_rows)
    real_part = jnp.einsum("rk,skw->srw", inv_cos, returned[0], precision=high) - jnp.einsum(
        "rk,skw->srw", inv_sin, returned[1], precision=high
    )
    real_part = real_part.reshape(arrays, parts, rows, cols).transpose(1, 0, 2, 3)
    gathered = exchange(real_part).transpose(1, 2, 0, 3).reshape(arrays, bin_dev) / nfft
    birth = gathered[:scen_dev]
    corr = gathered[scen_dev:]
    flux = rate[None, :] * weighted
    incoming = from_behind(flux[:, -1:], "mass", 1)
    inflow = jnp.concatenate([incoming, flux[:, :-1]], axis=1)
    tendency = 0.5 * beta * birth - beta * first[:, None] * weighted - flux + inflow
    arriving = from_behind(cotangent[:, :1], "mass", -1)
    following = jnp.concatenate([cotangent[:, 1:], arriving], axis=1)
    adjoint = mass[None, :] * (
        beta * corr
        - beta * first[:, None] * cotangent
        - beta * cross[:, None]
        - rate[None, :] * cotangent
        + rate[None, :] * following
    )
    local_grad = jnp.sum(weighted * (following - cotangent), axis=0)
    rate_gradient = lax.psum(local_grad, "scen")
    return (tendency, adjoint, rate_gradient)


def solution(mesh):
    in_specs = (P("scen", "mass"), P("scen", "mass"), P("mass"))
    out_specs = (P("scen", "mass"), P("scen", "mass"), P("mass"))
    return jax.shard_map(shards, mesh=mesh, in_specs=in_specs, out_specs=out_specs, check_vma=False)
```

```python
import math

import jax
import numpy as np
import jax.numpy as jnp
from jax import lax
from jax.sharding import PartitionSpec as P

C1 = 32
C2 = 128


aggregation_coef = 12.0


def from_behind(value, axis, steps):
    count = lax.axis_size(axis)
    first, last = (max(0, -steps), min(count, count - steps))
    return lax.ppermute(value, axis, [(source, source + steps) for source in range(first, last)])


def phases(left, right, total):
    outer = left[:, None] * right[None, :] % total
    angle = outer.astype(jnp.float32) * (2.0 * math.pi / total)
    return (jnp.cos(angle), jnp.sin(angle))


def counting(count):
    return lax.iota(jnp.int32, count)


def complex_dot(form, table, values):
    table_re, table_im = table
    val_re, val_im = values
    high = lax.Precision.HIGHEST
    real_out = jnp.einsum(form, table_re, val_re, precision=high) - jnp.einsum(
        form, table_im, val_im, precision=high
    )
    imag_out = jnp.einsum(form, table_re, val_im, precision=high) + jnp.einsum(
        form, table_im, val_re, precision=high
    )
    return (real_out, imag_out)


def complex_mul(left, right):
    return (left[0] * right[0] - left[1] * right[1], left[0] * right[1] + left[1] * right[0])


def column_forward(values):
    lead = values[0].shape[:-1]
    shaped = (values[0].reshape(lead + (C1, C2)), values[1].reshape(lead + (C1, C2)))
    cos_one, sin_one = phases(counting(C1), counting(C1), C1)
    step_one = complex_dot("pa,...ab->...pb", (cos_one, -sin_one), shaped)
    tw_cos, tw_sin = phases(counting(C1), counting(C2), C1 * C2)
    turned = complex_mul(step_one, (tw_cos, -tw_sin))
    cos_two, sin_two = phases(counting(C2), counting(C2), C2)
    return complex_dot("qb,...pb->...pq", (cos_two, -sin_two), turned)


def column_inverse(values):
    lead = values[0].shape[:-2]
    cos_two, sin_two = phases(counting(C2), counting(C2), C2)
    step_one = complex_dot("qb,...pq->...pb", (cos_two, sin_two), values)
    tw_cos, tw_sin = phases(counting(C1), counting(C2), C1 * C2)
    turned = complex_mul(step_one, (tw_cos, tw_sin))
    cos_one, sin_one = phases(counting(C1), counting(C1), C1)
    result = complex_dot("pa,...pb->...ab", (cos_one, sin_one), turned)
    return (result[0].reshape(lead + (C1 * C2,)), result[1].reshape(lead + (C1 * C2,)))


def exchange(value):
    return lax.all_to_all(value, "mass", 0, 0, tiled=True)


def shards(density, cotangent, rate):
    high = lax.Precision.HIGHEST
    scen_dev, bin_dev = density.shape
    arrays = 2 * scen_dev
    parts = lax.axis_size("mass")
    place = lax.axis_index("mass")
    width = C1 * C2
    rows = bin_dev // width
    half_rows = rows * parts
    full_rows = 2 * half_rows
    cols = width // parts
    block = full_rows // parts
    nbin = half_rows * width
    nfft = 2 * nbin
    beta = aggregation_coef / nbin
    offset = place * bin_dev
    mass = ((offset + counting(bin_dev)).astype(jnp.float32) + 0.5) / nbin
    weighted = mass[None, :] * density
    partial = jnp.concatenate([jnp.sum(weighted, axis=1), jnp.sum(cotangent * weighted, axis=1)])
    tile = jnp.zeros((8, cols), jnp.float32).at[0, :arrays].set(partial)
    stacked = jnp.concatenate([weighted, cotangent], axis=0).reshape(arrays, rows, parts, cols)
    outgoing = stacked.transpose(2, 0, 1, 3).reshape(parts, arrays * rows, cols)
    outgoing = jnp.concatenate([outgoing, jnp.broadcast_to(tile, (parts, 8, cols))], axis=1)
    incoming_rows = exchange(outgoing)
    moments = jnp.sum(incoming_rows[:, arrays * rows, :arrays], axis=0)
    first, cross = moments[:scen_dev], moments[scen_dev:]
    spread = incoming_rows[:, : arrays * rows].reshape(parts, arrays, rows, cols)
    spread = spread.transpose(1, 0, 2, 3).reshape(arrays, half_rows, cols)
    half = block // 2
    pos = counting(block)
    own_rows = jnp.where(pos < half, half * place + pos, (full_rows - half * place - (pos - half)) % full_rows)
    own_rows = jnp.where((place == 0) & (pos == half), full_rows // 2, own_rows)
    table = np.arange(block)[None, :]
    order = np.where(table < half, half * np.arange(parts)[:, None] + table,
                     (full_rows - half * np.arange(parts)[:, None] - (table - half)) % full_rows)
    order[0, half] = full_rows // 2
    order = jnp.asarray(order.reshape(-1), jnp.int32)
    row_cos, row_sin = phases(order, counting(half_rows), full_rows)
    forward_rows = jnp.stack([jnp.stack([row_cos, row_sin], axis=1), jnp.stack([-row_sin, row_cos], axis=1)])
    packed = spread.reshape(2, scen_dev, half_rows, cols)
    freq = jnp.einsum("okir,isrw->oskw", forward_rows, packed, precision=high)
    column_index = place * cols + counting(cols)
    tw_cos, tw_sin = phases(order, column_index, nfft)
    twisted = jnp.stack(complex_mul((freq[0], freq[1]), (tw_cos, -tw_sin)))
    twisted = twisted.reshape(2, scen_dev, parts, block, cols).transpose(2, 0, 1, 3, 4)
    moved = exchange(twisted).transpose(1, 2, 3, 0, 4).reshape(2, scen_dev, block, width)
    spec_re, spec_im = column_forward((moved[0], moved[1]))
    flip_re = jnp.roll(spec_re[:, :, ::-1, ::-1], half, axis=1)
    flip_im = jnp.roll(spec_im[:, :, ::-1, ::-1], half, axis=1)
    self_re = spec_re[:, half, ::-1, ::-1]
    self_im = spec_im[:, half, ::-1, ::-1]
    zero_re = jnp.roll(spec_re[:, 0, ::-1, ::-1], 1, axis=1)
    zero_im = jnp.roll(spec_im[:, 0, ::-1, ::-1], 1, axis=1)
    zero_re = zero_re.at[:, 0, :].set(jnp.roll(zero_re[:, 0, :], 1, axis=1))
    zero_im = zero_im.at[:, 0, :].set(jnp.roll(zero_im[:, 0, :], 1, axis=1))
    lead = place == 0
    mir_re = flip_re.at[:, 0].set(jnp.where(lead, zero_re, flip_re[:, 0]))
    mir_re = mir_re.at[:, half].set(jnp.where(lead, self_re, flip_re[:, half]))
    mir_im = flip_im.at[:, 0].set(jnp.where(lead, zero_im, flip_im[:, 0]))
    mir_im = mir_im.at[:, half].set(jnp.where(lead, self_im, flip_im[:, half]))
    dist_spec = (0.5 * (spec_re + mir_re), 0.5 * (spec_im - mir_im))
    cot_spec = (0.5 * (spec_im + mir_im), 0.5 * (mir_re - spec_re))
    birth_spec = complex_mul(dist_spec, dist_spec)
    adjoint_spec = complex_mul(cot_spec, (dist_spec[0], -dist_spec[1]))
    joined = (birth_spec[0] - adjoint_spec[1], birth_spec[1] + adjoint_spec[0])
    inverted = column_inverse(joined)
    back_cos, back_sin = phases(own_rows, counting(width), nfft)
    untwisted = jnp.stack(complex_mul(inverted, (back_cos, back_sin)))
    untwisted = untwisted.reshape(2, scen_dev, block, parts, cols).transpose(3, 0, 1, 2, 4)
    returned = exchange(untwisted).transpose(1, 2, 0, 3, 4).reshape(2, scen_dev, full_rows, cols)
    inv_cos, inv_sin = phases(counting(half_rows), order, full_rows)
    inverse_rows = jnp.stack([jnp.stack([inv_cos, -inv_sin], axis=1), jnp.stack([inv_sin, inv_cos], axis=1)])
    real_part = jnp.einsum("orik,iskw->osrw", inverse_rows, returned, precision=high)
    real_part = real_part.reshape(arrays, half_rows, cols)
    real_part = real_part.reshape(arrays, parts, rows, cols).transpose(1, 0, 2, 3)
    gathered = exchange(real_part).transpose(1, 2, 0, 3).reshape(arrays, bin_dev) / nfft
    birth = gathered[:scen_dev]
    corr = gathered[scen_dev:]
    flux = rate[None, :] * weighted
    incoming = from_behind(flux[:, -1:], "mass", 1)
    inflow = jnp.concatenate([incoming, flux[:, :-1]], axis=1)
    tendency = 0.5 * beta * birth - beta * first[:, None] * weighted - flux + inflow
    arriving = from_behind(cotangent[:, :1], "mass", -1)
    following = jnp.concatenate([cotangent[:, 1:], arriving], axis=1)
    adjoint = mass[None, :] * (
        beta * corr
        - beta * first[:, None] * cotangent
        - beta * cross[:, None]
        - rate[None, :] * cotangent
        + rate[None, :] * following
    )
    local_grad = jnp.sum(weighted * (following - cotangent), axis=0)
    rate_gradient = lax.psum(local_grad, "scen")
    return (tendency, adjoint, rate_gradient)


def solution(mesh):
    in_specs = (P("scen", "mass"), P("scen", "mass"), P("mass"))
    out_specs = (P("scen", "mass"), P("scen", "mass"), P("mass"))
    return jax.shard_map(shards, mesh=mesh, in_specs=in_specs, out_specs=out_specs, check_vma=False)
```

```python
import math

import jax
import numpy as np
import jax.numpy as jnp
from jax import lax
from jax.sharding import PartitionSpec as P

C1 = 32
C2 = 128


aggregation_coef = 12.0


def from_behind(value, axis, steps):
    count = lax.axis_size(axis)
    first, last = (max(0, -steps), min(count, count - steps))
    return lax.ppermute(value, axis, [(source, source + steps) for source in range(first, last)])


def phases(left, right, total):
    outer = left[:, None] * right[None, :] % total
    angle = outer.astype(jnp.float32) * (2.0 * math.pi / total)
    return (jnp.cos(angle), jnp.sin(angle))


def counting(count):
    return lax.iota(jnp.int32, count)


def complex_dot(form, table, values):
    table_re, table_im = table
    val_re, val_im = values
    high = lax.Precision.HIGHEST
    real_out = jnp.einsum(form, table_re, val_re, precision=high) - jnp.einsum(
        form, table_im, val_im, precision=high
    )
    imag_out = jnp.einsum(form, table_re, val_im, precision=high) + jnp.einsum(
        form, table_im, val_re, precision=high
    )
    return (real_out, imag_out)


def complex_mul(left, right):
    return (left[0] * right[0] - left[1] * right[1], left[0] * right[1] + left[1] * right[0])


def column_forward(values):
    lead = values[0].shape[:-1]
    shaped = (values[0].reshape(lead + (C1, C2)), values[1].reshape(lead + (C1, C2)))
    cos_one, sin_one = phases(counting(C1), counting(C1), C1)
    step_one = complex_dot("pa,...ab->...pb", (cos_one, -sin_one), shaped)
    tw_cos, tw_sin = phases(counting(C1), counting(C2), C1 * C2)
    turned = complex_mul(step_one, (tw_cos, -tw_sin))
    cos_two, sin_two = phases(counting(C2), counting(C2), C2)
    return complex_dot("qb,...pb->...pq", (cos_two, -sin_two), turned)


def column_inverse(values):
    lead = values[0].shape[:-2]
    cos_two, sin_two = phases(counting(C2), counting(C2), C2)
    step_one = complex_dot("qb,...pq->...pb", (cos_two, sin_two), values)
    tw_cos, tw_sin = phases(counting(C1), counting(C2), C1 * C2)
    turned = complex_mul(step_one, (tw_cos, tw_sin))
    cos_one, sin_one = phases(counting(C1), counting(C1), C1)
    result = complex_dot("pa,...pb->...ab", (cos_one, sin_one), turned)
    return (result[0].reshape(lead + (C1 * C2,)), result[1].reshape(lead + (C1 * C2,)))


def exchange(value):
    return lax.all_to_all(value, "mass", 0, 0, tiled=True)


def shards(density, cotangent, rate):
    high = lax.Precision.HIGHEST
    scen_dev, bin_dev = density.shape
    arrays = 2 * scen_dev
    parts = lax.axis_size("mass")
    place = lax.axis_index("mass")
    width = C1 * C2
    rows = bin_dev // width
    half_rows = rows * parts
    full_rows = 2 * half_rows
    cols = width // parts
    block = full_rows // parts
    nbin = half_rows * width
    nfft = 2 * nbin
    beta = aggregation_coef / nbin
    offset = place * bin_dev
    mass = ((offset + counting(bin_dev)).astype(jnp.float32) + 0.5) / nbin
    weighted = mass[None, :] * density
    partial = jnp.concatenate([jnp.sum(weighted, axis=1), jnp.sum(cotangent * weighted, axis=1)])
    tile = jnp.zeros((8, cols), jnp.float32).at[0, :arrays].set(partial)
    stacked = jnp.concatenate([weighted, cotangent], axis=0).reshape(arrays, rows, parts, cols)
    outgoing = stacked.transpose(2, 0, 1, 3).reshape(parts, arrays * rows, cols)
    outgoing = jnp.concatenate([outgoing, jnp.broadcast_to(tile, (parts, 8, cols))], axis=1)
    incoming_rows = exchange(outgoing)
    moments = jnp.sum(incoming_rows[:, arrays * rows, :arrays], axis=0)
    first, cross = moments[:scen_dev], moments[scen_dev:]
    spread = incoming_rows[:, : arrays * rows].reshape(parts, arrays, rows, cols)
    spread = spread.transpose(1, 0, 2, 3).reshape(arrays, half_rows, cols)
    half = block // 2
    pos = counting(block)
    own_rows = jnp.where(pos < half, half * place + pos, (full_rows - half * place - (pos - half)) % full_rows)
    own_rows = jnp.where((place == 0) & (pos == half), full_rows // 2, own_rows)
    table = np.arange(block)[None, :]
    order = np.where(table < half, half * np.arange(parts)[:, None] + table,
                     (full_rows - half * np.arange(parts)[:, None] - (table - half)) % full_rows)
    order[0, half] = full_rows // 2
    order = jnp.asarray(order.reshape(-1), jnp.int32)
    row_cos, row_sin = phases(order, counting(half_rows), full_rows)
    forward_rows = jnp.stack([jnp.stack([row_cos, row_sin], axis=1), jnp.stack([-row_sin, row_cos], axis=1)])
    packed = spread.reshape(2, scen_dev, half_rows, cols)
    freq = jnp.einsum("okir,isrw->oskw", forward_rows, packed, precision=high)
    column_index = place * cols + counting(cols)
    tw_cos, tw_sin = phases(order, column_index, nfft)
    twisted = jnp.stack(complex_mul((freq[0], freq[1]), (tw_cos, -tw_sin)))
    twisted = twisted.reshape(2, scen_dev, parts, block, cols).transpose(2, 0, 1, 3, 4)
    moved = exchange(twisted).transpose(1, 2, 3, 0, 4).reshape(2, scen_dev, block, width)
    lead = place == 0
    keep = (lead & ((pos == 0) | (pos == half)))[:, None]
    partner_re = jnp.where(keep, moved[0], jnp.roll(moved[0], half, axis=1))
    partner_im = jnp.where(keep, moved[1], jnp.roll(moved[1], half, axis=1))
    shift_cos, shift_sin = phases(jnp.ones((1,), jnp.int32), counting(width), width)
    plain = (lead & (pos == 0))[:, None]
    shift_cos = jnp.where(plain, 1.0, shift_cos)
    shift_sin = jnp.where(plain, 0.0, shift_sin)
    mirror_re = partner_re * shift_cos - partner_im * shift_sin
    mirror_im = -partner_re * shift_sin - partner_im * shift_cos
    split_re = jnp.concatenate([0.5 * (moved[0] + mirror_re), 0.5 * (moved[1] - mirror_im)], axis=0)
    split_im = jnp.concatenate([0.5 * (moved[1] + mirror_im), 0.5 * (mirror_re - moved[0])], axis=0)
    spec_re, spec_im = column_forward((split_re, split_im))
    dist_spec = (spec_re[:scen_dev], spec_im[:scen_dev])
    cot_spec = (spec_re[scen_dev:], spec_im[scen_dev:])
    birth_spec = complex_mul(dist_spec, dist_spec)
    adjoint_spec = complex_mul(cot_spec, (dist_spec[0], -dist_spec[1]))
    joined = (birth_spec[0] - adjoint_spec[1], birth_spec[1] + adjoint_spec[0])
    inverted = column_inverse(joined)
    back_cos, back_sin = phases(own_rows, counting(width), nfft)
    untwisted = jnp.stack(complex_mul(inverted, (back_cos, back_sin)))
    untwisted = untwisted.reshape(2, scen_dev, block, parts, cols).transpose(3, 0, 1, 2, 4)
    returned = exchange(untwisted).transpose(1, 2, 0, 3, 4).reshape(2, scen_dev, full_rows, cols)
    inv_cos, inv_sin = phases(counting(half_rows), order, full_rows)
    inverse_rows = jnp.stack([jnp.stack([inv_cos, -inv_sin], axis=1), jnp.stack([inv_sin, inv_cos], axis=1)])
    real_part = jnp.einsum("orik,iskw->osrw", inverse_rows, returned, precision=high)
    real_part = real_part.reshape(arrays, half_rows, cols)
    real_part = real_part.reshape(arrays, parts, rows, cols).transpose(1, 0, 2, 3)
    gathered = exchange(real_part).transpose(1, 2, 0, 3).reshape(arrays, bin_dev) / nfft
    birth = gathered[:scen_dev]
    corr = gathered[scen_dev:]
    flux = rate[None, :] * weighted
    incoming = from_behind(flux[:, -1:], "mass", 1)
    inflow = jnp.concatenate([incoming, flux[:, :-1]], axis=1)
    tendency = 0.5 * beta * birth - beta * first[:, None] * weighted - flux + inflow
    arriving = from_behind(cotangent[:, :1], "mass", -1)
    following = jnp.concatenate([cotangent[:, 1:], arriving], axis=1)
    adjoint = mass[None, :] * (
        beta * corr
        - beta * first[:, None] * cotangent
        - beta * cross[:, None]
        - rate[None, :] * cotangent
        + rate[None, :] * following
    )
    local_grad = jnp.sum(weighted * (following - cotangent), axis=0)
    rate_gradient = lax.psum(local_grad, "scen")
    return (tendency, adjoint, rate_gradient)


def solution(mesh):
    in_specs = (P("scen", "mass"), P("scen", "mass"), P("mass"))
    out_specs = (P("scen", "mass"), P("scen", "mass"), P("mass"))
    return jax.shard_map(shards, mesh=mesh, in_specs=in_specs, out_specs=out_specs, check_vma=False)
```

```python
import math

import jax
import numpy as np
import jax.numpy as jnp
from jax import lax
from jax.sharding import PartitionSpec as P

C1 = 32
C2 = 128


aggregation_coef = 12.0


def from_behind(value, axis, steps):
    count = lax.axis_size(axis)
    first, last = (max(0, -steps), min(count, count - steps))
    return lax.ppermute(value, axis, [(source, source + steps) for source in range(first, last)])


def phases(left, right, total):
    outer = left[:, None] * right[None, :] % total
    angle = outer.astype(jnp.float32) * (2.0 * math.pi / total)
    return (jnp.cos(angle), jnp.sin(angle))


def counting(count):
    return lax.iota(jnp.int32, count)


def complex_dot(form, table, values):
    table_re, table_im = table
    val_re, val_im = values
    high = lax.Precision.HIGHEST
    real_out = jnp.einsum(form, table_re, val_re, precision=high) - jnp.einsum(
        form, table_im, val_im, precision=high
    )
    imag_out = jnp.einsum(form, table_re, val_im, precision=high) + jnp.einsum(
        form, table_im, val_re, precision=high
    )
    return (real_out, imag_out)


def complex_mul(left, right):
    return (left[0] * right[0] - left[1] * right[1], left[0] * right[1] + left[1] * right[0])


def column_forward(values):
    lead = values[0].shape[:-1]
    shaped = (values[0].reshape(lead + (C1, C2)), values[1].reshape(lead + (C1, C2)))
    cos_one, sin_one = phases(counting(C1), counting(C1), C1)
    step_one = complex_dot("pa,...ab->...pb", (cos_one, -sin_one), shaped)
    tw_cos, tw_sin = phases(counting(C1), counting(C2), C1 * C2)
    turned = complex_mul(step_one, (tw_cos, -tw_sin))
    cos_two, sin_two = phases(counting(C2), counting(C2), C2)
    return complex_dot("qb,...pb->...pq", (cos_two, -sin_two), turned)


def column_inverse(values):
    lead = values[0].shape[:-2]
    cos_two, sin_two = phases(counting(C2), counting(C2), C2)
    step_one = complex_dot("qb,...pq->...pb", (cos_two, sin_two), values)
    tw_cos, tw_sin = phases(counting(C1), counting(C2), C1 * C2)
    turned = complex_mul(step_one, (tw_cos, tw_sin))
    cos_one, sin_one = phases(counting(C1), counting(C1), C1)
    result = complex_dot("pa,...pb->...ab", (cos_one, sin_one), turned)
    return (result[0].reshape(lead + (C1 * C2,)), result[1].reshape(lead + (C1 * C2,)))


def exchange(value):
    return lax.all_to_all(value, "mass", 0, 0, tiled=True)


def shards(density, cotangent, rate):
    high = lax.Precision.HIGHEST
    scen_dev, bin_dev = density.shape
    arrays = 2 * scen_dev
    parts = lax.axis_size("mass")
    place = lax.axis_index("mass")
    width = C1 * C2
    rows = bin_dev // width
    half_rows = rows * parts
    full_rows = 2 * half_rows
    cols = width // parts
    block = full_rows // parts
    nbin = half_rows * width
    nfft = 2 * nbin
    beta = aggregation_coef / nbin
    offset = place * bin_dev
    mass = ((offset + counting(bin_dev)).astype(jnp.float32) + 0.5) / nbin
    weighted = mass[None, :] * density
    partial = jnp.concatenate([jnp.sum(weighted, axis=1), jnp.sum(cotangent * weighted, axis=1)])
    tile = jnp.zeros((8, cols), jnp.float32).at[0, :arrays].set(partial)
    stacked = jnp.concatenate([weighted, cotangent], axis=0).reshape(arrays, rows, parts, cols)
    outgoing = stacked.transpose(2, 0, 1, 3).reshape(parts, arrays * rows, cols)
    outgoing = jnp.concatenate([outgoing, jnp.broadcast_to(tile, (parts, 8, cols))], axis=1)
    incoming_rows = exchange(outgoing)
    moments = jnp.sum(incoming_rows[:, arrays * rows, :arrays], axis=0)
    first, cross = moments[:scen_dev], moments[scen_dev:]
    spread = incoming_rows[:, : arrays * rows].reshape(parts, arrays, rows, cols)
    spread = spread.transpose(1, 0, 2, 3).reshape(arrays, half_rows, cols)
    half = block // 2
    pos = counting(block)
    own_rows = jnp.where(pos < half, half * place + pos, (full_rows - half * place - (pos - half)) % full_rows)
    own_rows = jnp.where((place == 0) & (pos == half), full_rows // 2, own_rows)
    table = np.arange(block)[None, :]
    order = np.where(table < half, half * np.arange(parts)[:, None] + table,
                     (full_rows - half * np.arange(parts)[:, None] - (table - half)) % full_rows)
    order[0, half] = full_rows // 2
    order = jnp.asarray(order.reshape(-1), jnp.int32)
    row_cos, row_sin = phases(order, counting(half_rows), full_rows)
    forward_rows = jnp.stack([jnp.stack([row_cos, row_sin], axis=1), jnp.stack([-row_sin, row_cos], axis=1)])
    packed = spread.reshape(2, scen_dev, half_rows, cols)
    freq = jnp.einsum("okir,isrw->oskw", forward_rows, packed, precision=high)
    column_index = place * cols + counting(cols)
    tw_cos, tw_sin = phases(order, column_index, nfft)
    twisted = jnp.stack(complex_mul((freq[0], freq[1]), (tw_cos, -tw_sin)))
    twisted = twisted.reshape(2, scen_dev, parts, block, cols).transpose(2, 0, 1, 3, 4)
    moved = exchange(twisted).transpose(1, 2, 3, 0, 4).reshape(2, scen_dev, block, width)
    lead = place == 0
    keep = (lead & ((pos == 0) | (pos == half)))[:, None]
    partner_re = jnp.where(keep, moved[0], jnp.roll(moved[0], half, axis=1))
    partner_im = jnp.where(keep, moved[1], jnp.roll(moved[1], half, axis=1))
    shift_cos, shift_sin = phases(jnp.ones((1,), jnp.int32), counting(width), width)
    plain = (lead & (pos == 0))[:, None]
    shift_cos = jnp.where(plain, 1.0, shift_cos)
    shift_sin = jnp.where(plain, 0.0, shift_sin)
    mirror_re = partner_re * shift_cos - partner_im * shift_sin
    mirror_im = -partner_re * shift_sin - partner_im * shift_cos
    split_re = jnp.concatenate([0.5 * (moved[0] + mirror_re), 0.5 * (moved[1] - mirror_im)], axis=0)
    split_im = jnp.concatenate([0.5 * (moved[1] + mirror_im), 0.5 * (mirror_re - moved[0])], axis=0)
    spec_re, spec_im = column_forward((split_re, split_im))
    dist_spec = (spec_re[:scen_dev], spec_im[:scen_dev])
    cot_spec = (spec_re[scen_dev:], spec_im[scen_dev:])
    birth_spec = complex_mul(dist_spec, dist_spec)
    adjoint_spec = complex_mul(cot_spec, (dist_spec[0], -dist_spec[1]))
    joined = (birth_spec[0] - adjoint_spec[1], birth_spec[1] + adjoint_spec[0])
    inverted = column_inverse(joined)
    back_cos, back_sin = phases(own_rows, counting(width), nfft)
    untwisted = jnp.stack(complex_mul(inverted, (back_cos, back_sin)))
    untwisted = untwisted.reshape(2, scen_dev, block, parts, cols).transpose(3, 0, 1, 2, 4)
    returned = exchange(untwisted).transpose(1, 2, 0, 3, 4).reshape(2, scen_dev, full_rows, cols)
    inv_cos, inv_sin = phases(counting(half_rows), order, full_rows)
    inverse_rows = jnp.stack([jnp.stack([inv_cos, -inv_sin], axis=1), jnp.stack([inv_sin, inv_cos], axis=1)])
    real_part = jnp.einsum("orik,iskw->osrw", inverse_rows, returned, precision=high)
    real_part = real_part.reshape(arrays, half_rows, cols)
    real_part = real_part.reshape(arrays, parts, rows, cols).transpose(1, 0, 2, 3)
    gathered = exchange(real_part).transpose(1, 2, 0, 3).reshape(arrays, bin_dev) / nfft
    birth = gathered[:scen_dev]
    corr = gathered[scen_dev:]
    flux = rate[None, :] * weighted
    incoming = from_behind(flux[:, -1:], "mass", 1)
    inflow = jnp.concatenate([incoming, flux[:, :-1]], axis=1)
    tendency = 0.5 * beta * birth - beta * first[:, None] * weighted - flux + inflow
    arriving = from_behind(cotangent[:, :1], "mass", -1)
    following = jnp.concatenate([cotangent[:, 1:], arriving], axis=1)
    adjoint = mass[None, :] * (
        beta * corr
        - beta * first[:, None] * cotangent
        - beta * cross[:, None]
        - rate[None, :] * cotangent
        + rate[None, :] * following
    )
    local_grad = jnp.sum(weighted * (following - cotangent), axis=0)
    rate_gradient = local_grad
    groups = lax.axis_size("scen")
    if groups & (groups - 1) == 0:
        step = 1
        while step < groups:
            pairs = [(source, source ^ step) for source in range(groups)]
            rate_gradient = rate_gradient + lax.ppermute(rate_gradient, "scen", pairs)
            step *= 2
    else:
        rate_gradient = lax.psum(local_grad, "scen")
    return (tendency, adjoint, rate_gradient)


def solution(mesh):
    in_specs = (P("scen", "mass"), P("scen", "mass"), P("mass"))
    out_specs = (P("scen", "mass"), P("scen", "mass"), P("mass"))
    return jax.shard_map(shards, mesh=mesh, in_specs=in_specs, out_specs=out_specs, check_vma=False)
```

```python
import math

import jax
import numpy as np
import jax.numpy as jnp
from jax import lax
from jax.sharding import PartitionSpec as P

C1 = 32
C2 = 128


aggregation_coef = 12.0


def from_behind(value, axis, steps):
    count = lax.axis_size(axis)
    first, last = (max(0, -steps), min(count, count - steps))
    return lax.ppermute(value, axis, [(source, source + steps) for source in range(first, last)])


def phases(left, right, total):
    outer = left[:, None] * right[None, :] % total
    angle = outer.astype(jnp.float32) * (2.0 * math.pi / total)
    return (jnp.cos(angle), jnp.sin(angle))


def counting(count):
    return lax.iota(jnp.int32, count)


def complex_dot(form, table, values):
    table_re, table_im = table
    val_re, val_im = values
    high = lax.Precision.HIGHEST
    real_out = jnp.einsum(form, table_re, val_re, precision=high) - jnp.einsum(
        form, table_im, val_im, precision=high
    )
    imag_out = jnp.einsum(form, table_re, val_im, precision=high) + jnp.einsum(
        form, table_im, val_re, precision=high
    )
    return (real_out, imag_out)


def complex_mul(left, right):
    return (left[0] * right[0] - left[1] * right[1], left[0] * right[1] + left[1] * right[0])


def column_forward(values):
    lead = values[0].shape[:-1]
    shaped = (values[0].reshape(lead + (C1, C2)), values[1].reshape(lead + (C1, C2)))
    cos_one, sin_one = phases(counting(C1), counting(C1), C1)
    step_one = complex_dot("pa,...ab->...pb", (cos_one, -sin_one), shaped)
    tw_cos, tw_sin = phases(counting(C1), counting(C2), C1 * C2)
    turned = complex_mul(step_one, (tw_cos, -tw_sin))
    cos_two, sin_two = phases(counting(C2), counting(C2), C2)
    return complex_dot("qb,...pb->...pq", (cos_two, -sin_two), turned)


def column_inverse(values):
    lead = values[0].shape[:-2]
    cos_two, sin_two = phases(counting(C2), counting(C2), C2)
    step_one = complex_dot("qb,...pq->...pb", (cos_two, sin_two), values)
    tw_cos, tw_sin = phases(counting(C1), counting(C2), C1 * C2)
    turned = complex_mul(step_one, (tw_cos, tw_sin))
    cos_one, sin_one = phases(counting(C1), counting(C1), C1)
    result = complex_dot("pa,...pb->...ab", (cos_one, sin_one), turned)
    return (result[0].reshape(lead + (C1 * C2,)), result[1].reshape(lead + (C1 * C2,)))


def exchange(value):
    return lax.all_to_all(value, "mass", 0, 0, tiled=True)


def shards(density, cotangent, rate):
    high = lax.Precision.HIGHEST
    scen_dev, bin_dev = density.shape
    arrays = 2 * scen_dev
    parts = lax.axis_size("mass")
    place = lax.axis_index("mass")
    width = C1 * C2
    rows = bin_dev // width
    half_rows = rows * parts
    full_rows = 2 * half_rows
    cols = width // parts
    block = full_rows // parts
    nbin = half_rows * width
    nfft = 2 * nbin
    beta = aggregation_coef / nbin
    offset = place * bin_dev
    mass = ((offset + counting(bin_dev)).astype(jnp.float32) + 0.5) / nbin
    weighted = mass[None, :] * density
    partial = jnp.concatenate([jnp.sum(weighted, axis=1), jnp.sum(cotangent * weighted, axis=1)])
    flux = rate[None, :] * weighted
    edges = jnp.concatenate([flux[:, -1], cotangent[:, 0]])
    tile = jnp.zeros((8, cols), jnp.float32).at[0, :arrays].set(partial).at[1, :arrays].set(edges)
    stacked = jnp.concatenate([weighted, cotangent], axis=0).reshape(arrays, rows, parts, cols)
    outgoing = stacked.transpose(2, 0, 1, 3).reshape(parts, arrays * rows, cols)
    outgoing = jnp.concatenate([outgoing, jnp.broadcast_to(tile, (parts, 8, cols))], axis=1)
    incoming_rows = exchange(outgoing)
    moments = jnp.sum(incoming_rows[:, arrays * rows, :arrays], axis=0)
    first, cross = moments[:scen_dev], moments[scen_dev:]
    neighbours = incoming_rows[:, arrays * rows + 1, :arrays]
    behind = lax.dynamic_index_in_dim(neighbours, (place + parts - 1) % parts, keepdims=False)
    ahead = lax.dynamic_index_in_dim(neighbours, (place + 1) % parts, keepdims=False)
    incoming = jnp.where(place > 0, behind[:scen_dev], 0.0)[:, None]
    arriving = jnp.where(place < parts - 1, ahead[scen_dev:], 0.0)[:, None]
    spread = incoming_rows[:, : arrays * rows].reshape(parts, arrays, rows, cols)
    spread = spread.transpose(1, 0, 2, 3).reshape(arrays, half_rows, cols)
    half = block // 2
    pos = counting(block)
    own_rows = jnp.where(pos < half, half * place + pos, (full_rows - half * place - (pos - half)) % full_rows)
    own_rows = jnp.where((place == 0) & (pos == half), full_rows // 2, own_rows)
    table = np.arange(block)[None, :]
    order = np.where(table < half, half * np.arange(parts)[:, None] + table,
                     (full_rows - half * np.arange(parts)[:, None] - (table - half)) % full_rows)
    order[0, half] = full_rows // 2
    order = jnp.asarray(order.reshape(-1), jnp.int32)
    row_cos, row_sin = phases(order, counting(half_rows), full_rows)
    forward_rows = jnp.stack([jnp.stack([row_cos, row_sin], axis=1), jnp.stack([-row_sin, row_cos], axis=1)])
    packed = spread.reshape(2, scen_dev, half_rows, cols)
    freq = jnp.einsum("okir,isrw->oskw", forward_rows, packed, precision=high)
    column_index = place * cols + counting(cols)
    tw_cos, tw_sin = phases(order, column_index, nfft)
    twisted = jnp.stack(complex_mul((freq[0], freq[1]), (tw_cos, -tw_sin)))
    twisted = twisted.reshape(2, scen_dev, parts, block, cols).transpose(2, 0, 1, 3, 4)
    moved = exchange(twisted).transpose(1, 2, 3, 0, 4).reshape(2, scen_dev, block, width)
    lead = place == 0
    keep = (lead & ((pos == 0) | (pos == half)))[:, None]
    partner_re = jnp.where(keep, moved[0], jnp.roll(moved[0], half, axis=1))
    partner_im = jnp.where(keep, moved[1], jnp.roll(moved[1], half, axis=1))
    shift_cos, shift_sin = phases(jnp.ones((1,), jnp.int32), counting(width), width)
    plain = (lead & (pos == 0))[:, None]
    shift_cos = jnp.where(plain, 1.0, shift_cos)
    shift_sin = jnp.where(plain, 0.0, shift_sin)
    mirror_re = partner_re * shift_cos - partner_im * shift_sin
    mirror_im = -partner_re * shift_sin - partner_im * shift_cos
    split_re = jnp.concatenate([0.5 * (moved[0] + mirror_re), 0.5 * (moved[1] - mirror_im)], axis=0)
    split_im = jnp.concatenate([0.5 * (moved[1] + mirror_im), 0.5 * (mirror_re - moved[0])], axis=0)
    spec_re, spec_im = column_forward((split_re, split_im))
    dist_spec = (spec_re[:scen_dev], spec_im[:scen_dev])
    cot_spec = (spec_re[scen_dev:], spec_im[scen_dev:])
    birth_spec = complex_mul(dist_spec, dist_spec)
    adjoint_spec = complex_mul(cot_spec, (dist_spec[0], -dist_spec[1]))
    joined = (birth_spec[0] - adjoint_spec[1], birth_spec[1] + adjoint_spec[0])
    inverted = column_inverse(joined)
    back_cos, back_sin = phases(own_rows, counting(width), nfft)
    untwisted = jnp.stack(complex_mul(inverted, (back_cos, back_sin)))
    untwisted = untwisted.reshape(2, scen_dev, block, parts, cols).transpose(3, 0, 1, 2, 4)
    returned = exchange(untwisted).transpose(1, 2, 0, 3, 4).reshape(2, scen_dev, full_rows, cols)
    inv_cos, inv_sin = phases(counting(half_rows), order, full_rows)
    inverse_rows = jnp.stack([jnp.stack([inv_cos, -inv_sin], axis=1), jnp.stack([inv_sin, inv_cos], axis=1)])
    real_part = jnp.einsum("orik,iskw->osrw", inverse_rows, returned, precision=high)
    real_part = real_part.reshape(arrays, half_rows, cols)
    real_part = real_part.reshape(arrays, parts, rows, cols).transpose(1, 0, 2, 3)
    gathered = exchange(real_part).transpose(1, 2, 0, 3).reshape(arrays, bin_dev) / nfft
    birth = gathered[:scen_dev]
    corr = gathered[scen_dev:]
    inflow = jnp.concatenate([incoming, flux[:, :-1]], axis=1)
    tendency = 0.5 * beta * birth - beta * first[:, None] * weighted - flux + inflow
    following = jnp.concatenate([cotangent[:, 1:], arriving], axis=1)
    adjoint = mass[None, :] * (
        beta * corr
        - beta * first[:, None] * cotangent
        - beta * cross[:, None]
        - rate[None, :] * cotangent
        + rate[None, :] * following
    )
    local_grad = jnp.sum(weighted * (following - cotangent), axis=0)
    rate_gradient = local_grad
    groups = lax.axis_size("scen")
    if groups & (groups - 1) == 0:
        step = 1
        while step < groups:
            pairs = [(source, source ^ step) for source in range(groups)]
            rate_gradient = rate_gradient + lax.ppermute(rate_gradient, "scen", pairs)
            step *= 2
    else:
        rate_gradient = lax.psum(local_grad, "scen")
    return (tendency, adjoint, rate_gradient)


def solution(mesh):
    in_specs = (P("scen", "mass"), P("scen", "mass"), P("mass"))
    out_specs = (P("scen", "mass"), P("scen", "mass"), P("mass"))
    return jax.shard_map(shards, mesh=mesh, in_specs=in_specs, out_specs=out_specs, check_vma=False)
```

```python
import math

import jax
import numpy as np
import jax.numpy as jnp
from jax import lax
from jax.sharding import PartitionSpec as P

C1 = 32
C2 = 128


aggregation_coef = 12.0


def from_behind(value, axis, steps):
    count = lax.axis_size(axis)
    first, last = (max(0, -steps), min(count, count - steps))
    return lax.ppermute(value, axis, [(source, source + steps) for source in range(first, last)])


def phases(left, right, total):
    outer = left[:, None] * right[None, :] % total
    angle = outer.astype(jnp.float32) * (2.0 * math.pi / total)
    return (jnp.cos(angle), jnp.sin(angle))


def counting(count):
    return lax.iota(jnp.int32, count)


def complex_dot(form, table, values):
    table_re, table_im = table
    val_re, val_im = values
    high = lax.Precision.HIGHEST
    real_out = jnp.einsum(form, table_re, val_re, precision=high) - jnp.einsum(
        form, table_im, val_im, precision=high
    )
    imag_out = jnp.einsum(form, table_re, val_im, precision=high) + jnp.einsum(
        form, table_im, val_re, precision=high
    )
    return (real_out, imag_out)


def complex_mul(left, right):
    return (left[0] * right[0] - left[1] * right[1], left[0] * right[1] + left[1] * right[0])


def column_forward(values):
    lead = values[0].shape[:-1]
    shaped = (values[0].reshape(lead + (C1, C2)), values[1].reshape(lead + (C1, C2)))
    cos_one, sin_one = phases(counting(C1), counting(C1), C1)
    step_one = complex_dot("pa,...ab->...pb", (cos_one, -sin_one), shaped)
    tw_cos, tw_sin = phases(counting(C1), counting(C2), C1 * C2)
    turned = complex_mul(step_one, (tw_cos, -tw_sin))
    cos_two, sin_two = phases(counting(C2), counting(C2), C2)
    return complex_dot("qb,...pb->...pq", (cos_two, -sin_two), turned)


def column_inverse(values):
    lead = values[0].shape[:-2]
    cos_two, sin_two = phases(counting(C2), counting(C2), C2)
    step_one = complex_dot("qb,...pq->...pb", (cos_two, sin_two), values)
    tw_cos, tw_sin = phases(counting(C1), counting(C2), C1 * C2)
    turned = complex_mul(step_one, (tw_cos, tw_sin))
    cos_one, sin_one = phases(counting(C1), counting(C1), C1)
    result = complex_dot("pa,...pb->...ab", (cos_one, sin_one), turned)
    return (result[0].reshape(lead + (C1 * C2,)), result[1].reshape(lead + (C1 * C2,)))


def exchange(value):
    return lax.all_to_all(value, "mass", 0, 0, tiled=True)


def shards(density, cotangent, rate):
    high = lax.Precision.HIGHEST
    scen_dev, bin_dev = density.shape
    arrays = 2 * scen_dev
    parts = lax.axis_size("mass")
    place = lax.axis_index("mass")
    width = C1 * C2
    rows = bin_dev // width
    half_rows = rows * parts
    full_rows = 2 * half_rows
    cols = width // parts
    block = full_rows // parts
    nbin = half_rows * width
    nfft = 2 * nbin
    beta = aggregation_coef / nbin
    offset = place * bin_dev
    mass = ((offset + counting(bin_dev)).astype(jnp.float32) + 0.5) / nbin
    weighted = mass[None, :] * density
    partial = jnp.concatenate([jnp.sum(weighted, axis=1), jnp.sum(cotangent * weighted, axis=1)])
    flux = rate[None, :] * weighted
    tile = jnp.zeros((8, cols), jnp.float32).at[0, :arrays].set(partial).at[1, :scen_dev].set(flux[:, -1])
    stacked = jnp.concatenate([weighted, cotangent], axis=0).reshape(arrays, rows, parts, cols)
    outgoing = stacked.transpose(2, 0, 1, 3).reshape(parts, arrays * rows, cols)
    outgoing = jnp.concatenate([outgoing, jnp.broadcast_to(tile, (parts, 8, cols))], axis=1)
    incoming_rows = exchange(outgoing)
    moments = jnp.sum(incoming_rows[:, arrays * rows, :arrays], axis=0)
    first, cross = moments[:scen_dev], moments[scen_dev:]
    neighbours = incoming_rows[:, arrays * rows + 1, :scen_dev]
    behind = lax.dynamic_index_in_dim(neighbours, (place + parts - 1) % parts, keepdims=False)
    incoming = jnp.where(place > 0, behind[:scen_dev], 0.0)[:, None]
    arriving = from_behind(cotangent[:, :1], "mass", -1)
    spread = incoming_rows[:, : arrays * rows].reshape(parts, arrays, rows, cols)
    spread = spread.transpose(1, 0, 2, 3).reshape(arrays, half_rows, cols)
    half = block // 2
    pos = counting(block)
    own_rows = jnp.where(pos < half, half * place + pos, (full_rows - half * place - (pos - half)) % full_rows)
    own_rows = jnp.where((place == 0) & (pos == half), full_rows // 2, own_rows)
    table = np.arange(block)[None, :]
    order = np.where(table < half, half * np.arange(parts)[:, None] + table,
                     (full_rows - half * np.arange(parts)[:, None] - (table - half)) % full_rows)
    order[0, half] = full_rows // 2
    order = jnp.asarray(order.reshape(-1), jnp.int32)
    row_cos, row_sin = phases(order, counting(half_rows), full_rows)
    forward_rows = jnp.stack([jnp.stack([row_cos, row_sin], axis=1), jnp.stack([-row_sin, row_cos], axis=1)])
    packed = spread.reshape(2, scen_dev, half_rows, cols)
    freq = jnp.einsum("okir,isrw->oskw", forward_rows, packed, precision=high)
    column_index = place * cols + counting(cols)
    tw_cos, tw_sin = phases(order, column_index, nfft)
    twisted = jnp.stack(complex_mul((freq[0], freq[1]), (tw_cos, -tw_sin)))
    twisted = twisted.reshape(2, scen_dev, parts, block, cols).transpose(2, 0, 1, 3, 4)
    moved = exchange(twisted).transpose(1, 2, 3, 0, 4).reshape(2, scen_dev, block, width)
    lead = place == 0
    keep = (lead & ((pos == 0) | (pos == half)))[:, None]
    partner_re = jnp.where(keep, moved[0], jnp.roll(moved[0], half, axis=1))
    partner_im = jnp.where(keep, moved[1], jnp.roll(moved[1], half, axis=1))
    shift_cos, shift_sin = phases(jnp.ones((1,), jnp.int32), counting(width), width)
    plain = (lead & (pos == 0))[:, None]
    shift_cos = jnp.where(plain, 1.0, shift_cos)
    shift_sin = jnp.where(plain, 0.0, shift_sin)
    mirror_re = partner_re * shift_cos - partner_im * shift_sin
    mirror_im = -partner_re * shift_sin - partner_im * shift_cos
    split_re = jnp.concatenate([0.5 * (moved[0] + mirror_re), 0.5 * (moved[1] - mirror_im)], axis=0)
    split_im = jnp.concatenate([0.5 * (moved[1] + mirror_im), 0.5 * (mirror_re - moved[0])], axis=0)
    spec_re, spec_im = column_forward((split_re, split_im))
    dist_spec = (spec_re[:scen_dev], spec_im[:scen_dev])
    cot_spec = (spec_re[scen_dev:], spec_im[scen_dev:])
    birth_spec = complex_mul(dist_spec, dist_spec)
    adjoint_spec = complex_mul(cot_spec, (dist_spec[0], -dist_spec[1]))
    joined = (birth_spec[0] - adjoint_spec[1], birth_spec[1] + adjoint_spec[0])
    inverted = column_inverse(joined)
    back_cos, back_sin = phases(own_rows, counting(width), nfft)
    untwisted = jnp.stack(complex_mul(inverted, (back_cos, back_sin)))
    untwisted = untwisted.reshape(2, scen_dev, block, parts, cols).transpose(3, 0, 1, 2, 4)
    returned = exchange(untwisted).transpose(1, 2, 0, 3, 4).reshape(2, scen_dev, full_rows, cols)
    inv_cos, inv_sin = phases(counting(half_rows), order, full_rows)
    inverse_rows = jnp.stack([jnp.stack([inv_cos, -inv_sin], axis=1), jnp.stack([inv_sin, inv_cos], axis=1)])
    real_part = jnp.einsum("orik,iskw->osrw", inverse_rows, returned, precision=high)
    real_part = real_part.reshape(arrays, half_rows, cols)
    real_part = real_part.reshape(arrays, parts, rows, cols).transpose(1, 0, 2, 3)
    gathered = exchange(real_part).transpose(1, 2, 0, 3).reshape(arrays, bin_dev) / nfft
    birth = gathered[:scen_dev]
    corr = gathered[scen_dev:]
    inflow = jnp.concatenate([incoming, flux[:, :-1]], axis=1)
    tendency = 0.5 * beta * birth - beta * first[:, None] * weighted - flux + inflow
    following = jnp.concatenate([cotangent[:, 1:], arriving], axis=1)
    adjoint = mass[None, :] * (
        beta * corr
        - beta * first[:, None] * cotangent
        - beta * cross[:, None]
        - rate[None, :] * cotangent
        + rate[None, :] * following
    )
    local_grad = jnp.sum(weighted * (following - cotangent), axis=0)
    rate_gradient = local_grad
    groups = lax.axis_size("scen")
    if groups & (groups - 1) == 0:
        step = 1
        while step < groups:
            pairs = [(source, source ^ step) for source in range(groups)]
            rate_gradient = rate_gradient + lax.ppermute(rate_gradient, "scen", pairs)
            step *= 2
    else:
        rate_gradient = lax.psum(local_grad, "scen")
    return (tendency, adjoint, rate_gradient)


def solution(mesh):
    in_specs = (P("scen", "mass"), P("scen", "mass"), P("mass"))
    out_specs = (P("scen", "mass"), P("scen", "mass"), P("mass"))
    return jax.shard_map(shards, mesh=mesh, in_specs=in_specs, out_specs=out_specs, check_vma=False)
```

```python
import math

import jax
import numpy as np
import jax.numpy as jnp
from jax import lax
from jax.experimental import pallas as pl
from jax.experimental.pallas import tpu as pltpu
from jax.sharding import PartitionSpec as P

C1 = 32
C2 = 128


aggregation_coef = 12.0


def from_behind(value, axis, steps):
    count = lax.axis_size(axis)
    first, last = (max(0, -steps), min(count, count - steps))
    return lax.ppermute(value, axis, [(source, source + steps) for source in range(first, last)])


def phases(left, right, total):
    outer = left[:, None] * right[None, :] % total
    angle = outer.astype(jnp.float32) * (2.0 * math.pi / total)
    return (jnp.cos(angle), jnp.sin(angle))


def counting(count):
    return lax.iota(jnp.int32, count)


def complex_dot(form, table, values):
    table_re, table_im = table
    val_re, val_im = values
    high = lax.Precision.HIGHEST
    real_out = jnp.einsum(form, table_re, val_re, precision=high) - jnp.einsum(
        form, table_im, val_im, precision=high
    )
    imag_out = jnp.einsum(form, table_re, val_im, precision=high) + jnp.einsum(
        form, table_im, val_re, precision=high
    )
    return (real_out, imag_out)


def complex_mul(left, right):
    return (left[0] * right[0] - left[1] * right[1], left[0] * right[1] + left[1] * right[0])


def column_forward(values):
    lead = values[0].shape[:-1]
    shaped = (values[0].reshape(lead + (C1, C2)), values[1].reshape(lead + (C1, C2)))
    cos_one, sin_one = phases(counting(C1), counting(C1), C1)
    step_one = complex_dot("pa,...ab->...pb", (cos_one, -sin_one), shaped)
    tw_cos, tw_sin = phases(counting(C1), counting(C2), C1 * C2)
    turned = complex_mul(step_one, (tw_cos, -tw_sin))
    cos_two, sin_two = phases(counting(C2), counting(C2), C2)
    return complex_dot("qb,...pb->...pq", (cos_two, -sin_two), turned)


def column_inverse(values):
    lead = values[0].shape[:-2]
    cos_two, sin_two = phases(counting(C2), counting(C2), C2)
    step_one = complex_dot("qb,...pq->...pb", (cos_two, sin_two), values)
    tw_cos, tw_sin = phases(counting(C1), counting(C2), C1 * C2)
    turned = complex_mul(step_one, (tw_cos, tw_sin))
    cos_one, sin_one = phases(counting(C1), counting(C1), C1)
    result = complex_dot("pa,...pb->...ab", (cos_one, sin_one), turned)
    return (result[0].reshape(lead + (C1 * C2,)), result[1].reshape(lead + (C1 * C2,)))


LANES = 128


def butterfly(values, sign):
    count = len(values)
    if count == 1:
        return list(values)
    even = butterfly(values[0::2], sign)
    odd = butterfly(values[1::2], sign)
    out = [None] * count
    for k in range(count // 2):
        o_re, o_im = odd[k]
        if k == 0:
            t = (o_re, o_im)
        elif 4 * k == count:
            t = (-sign * o_im, sign * o_re)
        else:
            c = math.cos(2.0 * math.pi * k / count)
            s = sign * math.sin(2.0 * math.pi * k / count)
            t = (o_re * c - o_im * s, o_re * s + o_im * c)
        e_re, e_im = even[k]
        out[k] = (e_re + t[0], e_im + t[1])
        out[k + count // 2] = (e_re - t[0], e_im - t[1])
    return out


def column_kernel(x_ref, phi_ref, tw1_ref, tw2_ref, back_ref, flag_ref, dft_ref, o_ref):
    parts, _, scen_dev, block, cols = x_ref.shape
    tiles = cols // LANES
    half = block // 2
    high = lax.Precision.HIGHEST
    keep = flag_ref[0] > 0.5
    plain = flag_ref[1] > 0.5
    dft_cos = dft_ref[0]
    dft_sin = dft_ref[1]

    def cmul(a, b):
        return (a[0] * b[0] - a[1] * b[1], a[0] * b[1] + a[1] * b[0])

    def transform(grid, sign):
        stage = [butterfly([grid[src][t] for src in range(parts)], sign) for t in range(tiles)]
        turned = []
        for k1 in range(parts):
            row = []
            for t in range(tiles):
                w = (tw1_ref[0, k1 * tiles + t], sign * tw1_ref[1, k1 * tiles + t])
                row.append(cmul(stage[t][k1], w))
            mixed = butterfly(row, sign)
            turned.append([cmul(mixed[m1], (tw2_ref[0, m1], sign * tw2_ref[1, m1])) for m1 in range(tiles)])
        flat_re = jnp.concatenate([turned[k][m][0] for k in range(parts) for m in range(tiles)], axis=0)
        flat_im = jnp.concatenate([turned[k][m][1] for k in range(parts) for m in range(tiles)], axis=0)
        dot = lambda a, b: jnp.dot(a, b, precision=high, preferred_element_type=jnp.float32)
        out_re = dot(flat_re, dft_cos) - sign * dot(flat_im, dft_sin)
        out_im = dot(flat_im, dft_cos) + sign * dot(flat_re, dft_sin)
        return out_re, out_im

    def inverse(flat, sign):
        dot = lambda a, b: jnp.dot(a, b, precision=high, preferred_element_type=jnp.float32)
        f_re, f_im = flat
        b_re = dot(f_re, dft_cos) - sign * dot(f_im, dft_sin)
        b_im = dot(f_im, dft_cos) + sign * dot(f_re, dft_sin)
        piece = lambda a, k, m: a[(k * tiles + m) * block:(k * tiles + m + 1) * block]
        stage = []
        for k1 in range(parts):
            row = [cmul((piece(b_re, k1, m), piece(b_im, k1, m)), (tw2_ref[0, m], sign * tw2_ref[1, m]))
                   for m in range(tiles)]
            mixed = butterfly(row, sign)
            stage.append([cmul(mixed[t], (tw1_ref[0, k1 * tiles + t], sign * tw1_ref[1, k1 * tiles + t]))
                          for t in range(tiles)])
        grid = [butterfly([stage[k1][t] for k1 in range(parts)], sign) for t in range(tiles)]
        return grid

    for sc in range(scen_dev):
        w_grid, c_grid = [], []
        for src in range(parts):
            w_row, c_row = [], []
            for t in range(tiles):
                lanes = slice(t * LANES, (t + 1) * LANES)
                t_re = x_ref[src, 0, sc, :, lanes]
                t_im = x_ref[src, 1, sc, :, lanes]
                swap_re = jnp.concatenate([t_re[half:], t_re[:half]], axis=0)
                swap_im = jnp.concatenate([t_im[half:], t_im[:half]], axis=0)
                p_re = jnp.where(keep, t_re, swap_re)
                p_im = jnp.where(keep, t_im, swap_im)
                f_re = jnp.where(plain, 1.0, phi_ref[0, src * tiles + t])
                f_im = jnp.where(plain, 0.0, -phi_ref[1, src * tiles + t])
                u_re = p_re * f_re + p_im * f_im
                u_im = p_re * f_im - p_im * f_re
                w_row.append((0.5 * (t_re + u_re), 0.5 * (t_im + u_im)))
                c_row.append((0.5 * (t_im - u_im), 0.5 * (u_re - t_re)))
            w_grid.append(w_row)
            c_grid.append(c_row)
        dist = transform(w_grid, -1.0)
        cot = transform(c_grid, -1.0)
        birth = cmul(dist, dist)
        adjoint = cmul(cot, (dist[0], -dist[1]))
        joined = (birth[0] - adjoint[1], birth[1] + adjoint[0])
        grid = inverse(joined, 1.0)
        for src in range(parts):
            for t in range(tiles):
                lanes = slice(t * LANES, (t + 1) * LANES)
                value = cmul(grid[t][src], (back_ref[0, src * tiles + t], back_ref[1, src * tiles + t]))
                o_ref[src, 0, sc, :, lanes] = value[0]
                o_ref[src, 1, sc, :, lanes] = value[1]


def column_stage(received, own_rows, place, nfft):
    parts, _, scen_dev, block, cols = received.shape
    tiles = cols // LANES
    width = parts * cols
    half = block // 2
    pos = counting(block)
    lane = counting(LANES)
    chunk = counting(parts * tiles)
    base = (chunk * LANES)[:, None] + lane[None, :]
    phi = jnp.stack(phases(jnp.ones((1,), jnp.int32), base.reshape(-1), width)).reshape(2, parts * tiles, 1, LANES)
    k1 = chunk // tiles
    within = (chunk % tiles) * LANES
    tw1 = jnp.stack(phases(jnp.ones((1,), jnp.int32), ((within[:, None] + lane[None, :]) * k1[:, None]).reshape(-1), width))
    tw1 = tw1.reshape(2, parts * tiles, 1, LANES)
    tw2 = jnp.stack(phases(counting(tiles), lane, cols)).reshape(2, tiles, 1, LANES)
    back = jnp.stack(phases(own_rows, counting(width), nfft))
    back = back.reshape(2, block, parts * tiles, LANES).transpose(0, 2, 1, 3)
    lead = place == 0
    keep = jnp.broadcast_to((lead & ((pos == 0) | (pos == half)))[:, None], (block, LANES))
    plain = jnp.broadcast_to((lead & (pos == 0))[:, None], (block, LANES))
    flags = jnp.stack([keep, plain]).astype(jnp.float32)
    dft = jnp.stack(phases(lane, lane, LANES))
    vmem = pl.BlockSpec(memory_space=pltpu.VMEM)
    return pl.pallas_call(
        column_kernel,
        out_shape=jax.ShapeDtypeStruct(received.shape, jnp.float32),
        in_specs=[vmem] * 7,
        out_specs=vmem,
    )(received, phi, tw1, tw2, back, flags, dft)


def exchange(value):
    return lax.all_to_all(value, "mass", 0, 0, tiled=True)


def shards(density, cotangent, rate):
    high = lax.Precision.HIGHEST
    scen_dev, bin_dev = density.shape
    arrays = 2 * scen_dev
    parts = lax.axis_size("mass")
    place = lax.axis_index("mass")
    width = C1 * C2
    rows = bin_dev // width
    half_rows = rows * parts
    full_rows = 2 * half_rows
    cols = width // parts
    block = full_rows // parts
    nbin = half_rows * width
    nfft = 2 * nbin
    beta = aggregation_coef / nbin
    offset = place * bin_dev
    mass = ((offset + counting(bin_dev)).astype(jnp.float32) + 0.5) / nbin
    weighted = mass[None, :] * density
    partial = jnp.concatenate([jnp.sum(weighted, axis=1), jnp.sum(cotangent * weighted, axis=1)])
    tile = jnp.zeros((8, cols), jnp.float32).at[0, :arrays].set(partial)
    stacked = jnp.concatenate([weighted, cotangent], axis=0).reshape(arrays, rows, parts, cols)
    outgoing = stacked.transpose(2, 0, 1, 3).reshape(parts, arrays * rows, cols)
    outgoing = jnp.concatenate([outgoing, jnp.broadcast_to(tile, (parts, 8, cols))], axis=1)
    incoming_rows = exchange(outgoing)
    moments = jnp.sum(incoming_rows[:, arrays * rows, :arrays], axis=0)
    first, cross = moments[:scen_dev], moments[scen_dev:]
    spread = incoming_rows[:, : arrays * rows].reshape(parts, arrays, rows, cols)
    spread = spread.transpose(1, 0, 2, 3).reshape(arrays, half_rows, cols)
    half = block // 2
    pos = counting(block)
    own_rows = jnp.where(pos < half, half * place + pos, (full_rows - half * place - (pos - half)) % full_rows)
    own_rows = jnp.where((place == 0) & (pos == half), full_rows // 2, own_rows)
    table = np.arange(block)[None, :]
    order = np.where(table < half, half * np.arange(parts)[:, None] + table,
                     (full_rows - half * np.arange(parts)[:, None] - (table - half)) % full_rows)
    order[0, half] = full_rows // 2
    order = jnp.asarray(order.reshape(-1), jnp.int32)
    row_cos, row_sin = phases(order, counting(half_rows), full_rows)
    forward_rows = jnp.stack([jnp.stack([row_cos, row_sin], axis=1), jnp.stack([-row_sin, row_cos], axis=1)])
    packed = spread.reshape(2, scen_dev, half_rows, cols)
    freq = jnp.einsum("okir,isrw->oskw", forward_rows, packed, precision=high)
    column_index = place * cols + counting(cols)
    tw_cos, tw_sin = phases(order, column_index, nfft)
    twisted = jnp.stack(complex_mul((freq[0], freq[1]), (tw_cos, -tw_sin)))
    twisted = twisted.reshape(2, scen_dev, parts, block, cols).transpose(2, 0, 1, 3, 4)
    untwisted = column_stage(exchange(twisted), own_rows, place, nfft)
    returned = exchange(untwisted).transpose(1, 2, 0, 3, 4).reshape(2, scen_dev, full_rows, cols)
    inv_cos, inv_sin = phases(counting(half_rows), order, full_rows)
    inverse_rows = jnp.stack([jnp.stack([inv_cos, -inv_sin], axis=1), jnp.stack([inv_sin, inv_cos], axis=1)])
    real_part = jnp.einsum("orik,iskw->osrw", inverse_rows, returned, precision=high)
    real_part = real_part.reshape(arrays, half_rows, cols)
    real_part = real_part.reshape(arrays, parts, rows, cols).transpose(1, 0, 2, 3)
    gathered = exchange(real_part).transpose(1, 2, 0, 3).reshape(arrays, bin_dev) / nfft
    birth = gathered[:scen_dev]
    corr = gathered[scen_dev:]
    flux = rate[None, :] * weighted
    incoming = from_behind(flux[:, -1:], "mass", 1)
    inflow = jnp.concatenate([incoming, flux[:, :-1]], axis=1)
    tendency = 0.5 * beta * birth - beta * first[:, None] * weighted - flux + inflow
    arriving = from_behind(cotangent[:, :1], "mass", -1)
    following = jnp.concatenate([cotangent[:, 1:], arriving], axis=1)
    adjoint = mass[None, :] * (
        beta * corr
        - beta * first[:, None] * cotangent
        - beta * cross[:, None]
        - rate[None, :] * cotangent
        + rate[None, :] * following
    )
    local_grad = jnp.sum(weighted * (following - cotangent), axis=0)
    rate_gradient = local_grad
    groups = lax.axis_size("scen")
    if groups & (groups - 1) == 0:
        step = 1
        while step < groups:
            pairs = [(source, source ^ step) for source in range(groups)]
            rate_gradient = rate_gradient + lax.ppermute(rate_gradient, "scen", pairs)
            step *= 2
    else:
        rate_gradient = lax.psum(local_grad, "scen")
    return (tendency, adjoint, rate_gradient)


def solution(mesh):
    in_specs = (P("scen", "mass"), P("scen", "mass"), P("mass"))
    out_specs = (P("scen", "mass"), P("scen", "mass"), P("mass"))
    return jax.shard_map(shards, mesh=mesh, in_specs=in_specs, out_specs=out_specs, check_vma=False)
```

```python
import math

import jax
import numpy as np
import jax.numpy as jnp
from jax import lax
from jax.experimental import pallas as pl
from jax.experimental.pallas import tpu as pltpu
from jax.sharding import PartitionSpec as P

C1 = 32
C2 = 128


aggregation_coef = 12.0


def from_behind(value, axis, steps):
    count = lax.axis_size(axis)
    first, last = (max(0, -steps), min(count, count - steps))
    return lax.ppermute(value, axis, [(source, source + steps) for source in range(first, last)])


def phases(left, right, total):
    outer = left[:, None] * right[None, :] % total
    angle = outer.astype(jnp.float32) * (2.0 * math.pi / total)
    return (jnp.cos(angle), jnp.sin(angle))


def counting(count):
    return lax.iota(jnp.int32, count)


def complex_dot(form, table, values):
    table_re, table_im = table
    val_re, val_im = values
    high = lax.Precision.HIGHEST
    real_out = jnp.einsum(form, table_re, val_re, precision=high) - jnp.einsum(
        form, table_im, val_im, precision=high
    )
    imag_out = jnp.einsum(form, table_re, val_im, precision=high) + jnp.einsum(
        form, table_im, val_re, precision=high
    )
    return (real_out, imag_out)


def complex_mul(left, right):
    return (left[0] * right[0] - left[1] * right[1], left[0] * right[1] + left[1] * right[0])


def column_forward(values):
    lead = values[0].shape[:-1]
    shaped = (values[0].reshape(lead + (C1, C2)), values[1].reshape(lead + (C1, C2)))
    cos_one, sin_one = phases(counting(C1), counting(C1), C1)
    step_one = complex_dot("pa,...ab->...pb", (cos_one, -sin_one), shaped)
    tw_cos, tw_sin = phases(counting(C1), counting(C2), C1 * C2)
    turned = complex_mul(step_one, (tw_cos, -tw_sin))
    cos_two, sin_two = phases(counting(C2), counting(C2), C2)
    return complex_dot("qb,...pb->...pq", (cos_two, -sin_two), turned)


def column_inverse(values):
    lead = values[0].shape[:-2]
    cos_two, sin_two = phases(counting(C2), counting(C2), C2)
    step_one = complex_dot("qb,...pq->...pb", (cos_two, sin_two), values)
    tw_cos, tw_sin = phases(counting(C1), counting(C2), C1 * C2)
    turned = complex_mul(step_one, (tw_cos, tw_sin))
    cos_one, sin_one = phases(counting(C1), counting(C1), C1)
    result = complex_dot("pa,...pb->...ab", (cos_one, sin_one), turned)
    return (result[0].reshape(lead + (C1 * C2,)), result[1].reshape(lead + (C1 * C2,)))


LANES = 128


def butterfly(values, sign):
    count = len(values)
    if count == 1:
        return list(values)
    even = butterfly(values[0::2], sign)
    odd = butterfly(values[1::2], sign)
    out = [None] * count
    for k in range(count // 2):
        o_re, o_im = odd[k]
        if k == 0:
            t = (o_re, o_im)
        elif 4 * k == count:
            t = (-sign * o_im, sign * o_re)
        else:
            c = math.cos(2.0 * math.pi * k / count)
            s = sign * math.sin(2.0 * math.pi * k / count)
            t = (o_re * c - o_im * s, o_re * s + o_im * c)
        e_re, e_im = even[k]
        out[k] = (e_re + t[0], e_im + t[1])
        out[k + count // 2] = (e_re - t[0], e_im - t[1])
    return out


def column_kernel(x_ref, phi_ref, tw1_ref, tw2_ref, back_ref, flag_ref, dft_ref, o_ref):
    parts, _, scen_dev, block, cols = x_ref.shape
    tiles = cols // LANES
    half = block // 2
    high = lax.Precision.HIGHEST
    keep = flag_ref[0] > 0.5
    plain = flag_ref[1] > 0.5
    dft_cos = dft_ref[0]
    dft_sin = dft_ref[1]

    def cmul(a, b):
        return (a[0] * b[0] - a[1] * b[1], a[0] * b[1] + a[1] * b[0])

    def transform(grid, sign):
        stage = [butterfly([grid[src][t] for src in range(parts)], sign) for t in range(tiles)]
        turned = []
        for k1 in range(parts):
            row = []
            for t in range(tiles):
                w = (tw1_ref[0, k1 * tiles + t], sign * tw1_ref[1, k1 * tiles + t])
                row.append(cmul(stage[t][k1], w))
            mixed = butterfly(row, sign)
            turned.append([cmul(mixed[m1], (tw2_ref[0, m1], sign * tw2_ref[1, m1])) for m1 in range(tiles)])
        flat_re = jnp.concatenate([turned[k][m][0] for k in range(parts) for m in range(tiles)], axis=0)
        flat_im = jnp.concatenate([turned[k][m][1] for k in range(parts) for m in range(tiles)], axis=0)
        dot = lambda a, b: jnp.dot(a, b, precision=high, preferred_element_type=jnp.float32)
        out_re = dot(flat_re, dft_cos) - sign * dot(flat_im, dft_sin)
        out_im = dot(flat_im, dft_cos) + sign * dot(flat_re, dft_sin)
        return out_re, out_im

    def inverse(flat, sign):
        dot = lambda a, b: jnp.dot(a, b, precision=high, preferred_element_type=jnp.float32)
        f_re, f_im = flat
        b_re = dot(f_re, dft_cos) - sign * dot(f_im, dft_sin)
        b_im = dot(f_im, dft_cos) + sign * dot(f_re, dft_sin)
        piece = lambda a, k, m: a[(k * tiles + m) * block:(k * tiles + m + 1) * block]
        stage = []
        for k1 in range(parts):
            row = [cmul((piece(b_re, k1, m), piece(b_im, k1, m)), (tw2_ref[0, m], sign * tw2_ref[1, m]))
                   for m in range(tiles)]
            mixed = butterfly(row, sign)
            stage.append([cmul(mixed[t], (tw1_ref[0, k1 * tiles + t], sign * tw1_ref[1, k1 * tiles + t]))
                          for t in range(tiles)])
        grid = [butterfly([stage[k1][t] for k1 in range(parts)], sign) for t in range(tiles)]
        return grid

    for sc in range(scen_dev):
        w_grid, c_grid = [], []
        for src in range(parts):
            w_row, c_row = [], []
            for t in range(tiles):
                lanes = slice(t * LANES, (t + 1) * LANES)
                t_re = x_ref[src, 0, sc, :, lanes]
                t_im = x_ref[src, 1, sc, :, lanes]
                swap_re = jnp.concatenate([t_re[half:], t_re[:half]], axis=0)
                swap_im = jnp.concatenate([t_im[half:], t_im[:half]], axis=0)
                p_re = jnp.where(keep, t_re, swap_re)
                p_im = jnp.where(keep, t_im, swap_im)
                f_re = jnp.where(plain, 1.0, phi_ref[0, src * tiles + t])
                f_im = jnp.where(plain, 0.0, -phi_ref[1, src * tiles + t])
                u_re = p_re * f_re + p_im * f_im
                u_im = p_re * f_im - p_im * f_re
                w_row.append((0.5 * (t_re + u_re), 0.5 * (t_im + u_im)))
                c_row.append((0.5 * (t_im - u_im), 0.5 * (u_re - t_re)))
            w_grid.append(w_row)
            c_grid.append(c_row)
        dist = transform(w_grid, -1.0)
        cot = transform(c_grid, -1.0)
        birth = cmul(dist, dist)
        adjoint = cmul(cot, (dist[0], -dist[1]))
        joined = (birth[0] - adjoint[1], birth[1] + adjoint[0])
        grid = inverse(joined, 1.0)
        for src in range(parts):
            for t in range(tiles):
                lanes = slice(t * LANES, (t + 1) * LANES)
                value = cmul(grid[t][src], (back_ref[0, src * tiles + t], back_ref[1, src * tiles + t]))
                o_ref[src, 0, sc, :, lanes] = value[0]
                o_ref[src, 1, sc, :, lanes] = value[1]


def column_stage(received, own_rows, place, nfft):
    parts, _, scen_dev, block, cols = received.shape
    tiles = cols // LANES
    width = parts * cols
    half = block // 2
    pos = counting(block)
    lane = counting(LANES)
    chunk = counting(parts * tiles)
    base = (chunk * LANES)[:, None] + lane[None, :]
    phi = jnp.stack(phases(jnp.ones((1,), jnp.int32), base.reshape(-1), width)).reshape(2, parts * tiles, 1, LANES)
    k1 = chunk // tiles
    within = (chunk % tiles) * LANES
    tw1 = jnp.stack(phases(jnp.ones((1,), jnp.int32), ((within[:, None] + lane[None, :]) * k1[:, None]).reshape(-1), width))
    tw1 = tw1.reshape(2, parts * tiles, 1, LANES)
    tw2 = jnp.stack(phases(counting(tiles), lane, cols)).reshape(2, tiles, 1, LANES)
    back = jnp.stack(phases(own_rows, counting(width), nfft))
    back = back.reshape(2, block, parts * tiles, LANES).transpose(0, 2, 1, 3)
    lead = place == 0
    keep = jnp.broadcast_to((lead & ((pos == 0) | (pos == half)))[:, None], (block, LANES))
    plain = jnp.broadcast_to((lead & (pos == 0))[:, None], (block, LANES))
    flags = jnp.stack([keep, plain]).astype(jnp.float32)
    dft = jnp.stack(phases(lane, lane, LANES))
    vmem = pl.BlockSpec(memory_space=pltpu.VMEM)
    return pl.pallas_call(
        column_kernel,
        out_shape=jax.ShapeDtypeStruct(received.shape, jnp.float32),
        in_specs=[vmem] * 7,
        out_specs=vmem,
    )(received, phi, tw1, tw2, back, flags, dft)


def exchange(value):
    return lax.all_to_all(value, "mass", 0, 0, tiled=True)


def shards(density, cotangent, rate):
    high = lax.Precision.HIGHEST
    scen_dev, bin_dev = density.shape
    arrays = 2 * scen_dev
    parts = lax.axis_size("mass")
    place = lax.axis_index("mass")
    width = C1 * C2
    rows = bin_dev // width
    half_rows = rows * parts
    full_rows = 2 * half_rows
    cols = width // parts
    block = full_rows // parts
    nbin = half_rows * width
    nfft = 2 * nbin
    beta = aggregation_coef / nbin
    offset = place * bin_dev
    mass = ((offset + counting(bin_dev)).astype(jnp.float32) + 0.5) / nbin
    weighted = mass[None, :] * density
    partial = jnp.concatenate([jnp.sum(weighted, axis=1), jnp.sum(cotangent * weighted, axis=1)])
    flux = rate[None, :] * weighted
    tile = jnp.zeros((8, cols), jnp.float32).at[0, :arrays].set(partial).at[1, :scen_dev].set(flux[:, -1])
    stacked = jnp.concatenate([weighted, cotangent], axis=0).reshape(arrays, rows, parts, cols)
    outgoing = stacked.transpose(2, 0, 1, 3).reshape(parts, arrays * rows, cols)
    outgoing = jnp.concatenate([outgoing, jnp.broadcast_to(tile, (parts, 8, cols))], axis=1)
    incoming_rows = exchange(outgoing)
    moments = jnp.sum(incoming_rows[:, arrays * rows, :arrays], axis=0)
    first, cross = moments[:scen_dev], moments[scen_dev:]
    neighbours = incoming_rows[:, arrays * rows + 1, :scen_dev]
    behind = lax.dynamic_index_in_dim(neighbours, (place + parts - 1) % parts, keepdims=False)
    incoming = jnp.where(place > 0, behind, 0.0)[:, None]
    spread = incoming_rows[:, : arrays * rows].reshape(parts, arrays, rows, cols)
    spread = spread.transpose(1, 0, 2, 3).reshape(arrays, half_rows, cols)
    half = block // 2
    pos = counting(block)
    own_rows = jnp.where(pos < half, half * place + pos, (full_rows - half * place - (pos - half)) % full_rows)
    own_rows = jnp.where((place == 0) & (pos == half), full_rows // 2, own_rows)
    table = np.arange(block)[None, :]
    order = np.where(table < half, half * np.arange(parts)[:, None] + table,
                     (full_rows - half * np.arange(parts)[:, None] - (table - half)) % full_rows)
    order[0, half] = full_rows // 2
    order = jnp.asarray(order.reshape(-1), jnp.int32)
    row_cos, row_sin = phases(order, counting(half_rows), full_rows)
    forward_rows = jnp.stack([jnp.stack([row_cos, row_sin], axis=1), jnp.stack([-row_sin, row_cos], axis=1)])
    packed = spread.reshape(2, scen_dev, half_rows, cols)
    freq = jnp.einsum("okir,isrw->oskw", forward_rows, packed, precision=high)
    column_index = place * cols + counting(cols)
    tw_cos, tw_sin = lax.optimization_barrier(phases(order, column_index, nfft))
    twisted = jnp.stack(complex_mul((freq[0], freq[1]), (tw_cos, -tw_sin)))
    twisted = twisted.reshape(2, scen_dev, parts, block, cols).transpose(2, 0, 1, 3, 4)
    untwisted = column_stage(exchange(twisted), own_rows, place, nfft)
    returned = exchange(untwisted).transpose(1, 2, 0, 3, 4).reshape(2, scen_dev, full_rows, cols)
    inv_cos, inv_sin = phases(counting(half_rows), order, full_rows)
    inverse_rows = jnp.stack([jnp.stack([inv_cos, -inv_sin], axis=1), jnp.stack([inv_sin, inv_cos], axis=1)])
    real_part = jnp.einsum("orik,iskw->osrw", inverse_rows, returned, precision=high)
    real_part = real_part.reshape(arrays, half_rows, cols)
    real_part = real_part.reshape(arrays, parts, rows, cols).transpose(1, 0, 2, 3)
    gathered = exchange(real_part).transpose(1, 2, 0, 3).reshape(arrays, bin_dev) / nfft
    birth = gathered[:scen_dev]
    corr = gathered[scen_dev:]
    inflow = jnp.concatenate([incoming, flux[:, :-1]], axis=1)
    tendency = 0.5 * beta * birth - beta * first[:, None] * weighted - flux + inflow
    arriving = from_behind(cotangent[:, :1], "mass", -1)
    following = jnp.concatenate([cotangent[:, 1:], arriving], axis=1)
    adjoint = mass[None, :] * (
        beta * corr
        - beta * first[:, None] * cotangent
        - beta * cross[:, None]
        - rate[None, :] * cotangent
        + rate[None, :] * following
    )
    local_grad = jnp.sum(weighted * (following - cotangent), axis=0)
    rate_gradient = local_grad
    groups = lax.axis_size("scen")
    if groups & (groups - 1) == 0:
        step = 1
        while step < groups:
            pairs = [(source, source ^ step) for source in range(groups)]
            rate_gradient = rate_gradient + lax.ppermute(rate_gradient, "scen", pairs)
            step *= 2
    else:
        rate_gradient = lax.psum(local_grad, "scen")
    return (tendency, adjoint, rate_gradient)


def solution(mesh):
    in_specs = (P("scen", "mass"), P("scen", "mass"), P("mass"))
    out_specs = (P("scen", "mass"), P("scen", "mass"), P("mass"))
    return jax.shard_map(shards, mesh=mesh, in_specs=in_specs, out_specs=out_specs, check_vma=False)
```

```python
import math

import jax
import numpy as np
import jax.numpy as jnp
from jax import lax
from jax.experimental import pallas as pl
from jax.experimental.pallas import tpu as pltpu
from jax.sharding import PartitionSpec as P

C1 = 32
C2 = 128


aggregation_coef = 12.0


def from_behind(value, axis, steps):
    count = lax.axis_size(axis)
    first, last = (max(0, -steps), min(count, count - steps))
    return lax.ppermute(value, axis, [(source, source + steps) for source in range(first, last)])


def phases(left, right, total):
    outer = left[:, None] * right[None, :] % total
    angle = outer.astype(jnp.float32) * (2.0 * math.pi / total)
    return (jnp.cos(angle), jnp.sin(angle))


def counting(count):
    return lax.iota(jnp.int32, count)


def complex_dot(form, table, values):
    table_re, table_im = table
    val_re, val_im = values
    high = lax.Precision.HIGHEST
    real_out = jnp.einsum(form, table_re, val_re, precision=high) - jnp.einsum(
        form, table_im, val_im, precision=high
    )
    imag_out = jnp.einsum(form, table_re, val_im, precision=high) + jnp.einsum(
        form, table_im, val_re, precision=high
    )
    return (real_out, imag_out)


def complex_mul(left, right):
    return (left[0] * right[0] - left[1] * right[1], left[0] * right[1] + left[1] * right[0])


def column_forward(values):
    lead = values[0].shape[:-1]
    shaped = (values[0].reshape(lead + (C1, C2)), values[1].reshape(lead + (C1, C2)))
    cos_one, sin_one = phases(counting(C1), counting(C1), C1)
    step_one = complex_dot("pa,...ab->...pb", (cos_one, -sin_one), shaped)
    tw_cos, tw_sin = phases(counting(C1), counting(C2), C1 * C2)
    turned = complex_mul(step_one, (tw_cos, -tw_sin))
    cos_two, sin_two = phases(counting(C2), counting(C2), C2)
    return complex_dot("qb,...pb->...pq", (cos_two, -sin_two), turned)


def column_inverse(values):
    lead = values[0].shape[:-2]
    cos_two, sin_two = phases(counting(C2), counting(C2), C2)
    step_one = complex_dot("qb,...pq->...pb", (cos_two, sin_two), values)
    tw_cos, tw_sin = phases(counting(C1), counting(C2), C1 * C2)
    turned = complex_mul(step_one, (tw_cos, tw_sin))
    cos_one, sin_one = phases(counting(C1), counting(C1), C1)
    result = complex_dot("pa,...pb->...ab", (cos_one, sin_one), turned)
    return (result[0].reshape(lead + (C1 * C2,)), result[1].reshape(lead + (C1 * C2,)))


LANES = 128


def butterfly(values, sign):
    count = len(values)
    if count == 1:
        return list(values)
    even = butterfly(values[0::2], sign)
    odd = butterfly(values[1::2], sign)
    out = [None] * count
    for k in range(count // 2):
        o_re, o_im = odd[k]
        if k == 0:
            t = (o_re, o_im)
        elif 4 * k == count:
            t = (-sign * o_im, sign * o_re)
        else:
            c = math.cos(2.0 * math.pi * k / count)
            s = sign * math.sin(2.0 * math.pi * k / count)
            t = (o_re * c - o_im * s, o_re * s + o_im * c)
        e_re, e_im = even[k]
        out[k] = (e_re + t[0], e_im + t[1])
        out[k + count // 2] = (e_re - t[0], e_im - t[1])
    return out


def column_kernel(x_ref, phi_ref, tw1_ref, tw2_ref, back_ref, flag_ref, dft_ref, o_ref):
    parts, _, scen_dev, block, cols = x_ref.shape
    tiles = cols // LANES
    half = block // 2
    high = lax.Precision.HIGHEST
    keep = flag_ref[0] > 0.5
    plain = flag_ref[1] > 0.5
    dft_cos = dft_ref[0]
    dft_sin = dft_ref[1]

    def cmul(a, b):
        return (a[0] * b[0] - a[1] * b[1], a[0] * b[1] + a[1] * b[0])

    def transform(grid, sign):
        stage = [butterfly([grid[src][t] for src in range(parts)], sign) for t in range(tiles)]
        turned = []
        for k1 in range(parts):
            row = []
            for t in range(tiles):
                w = (tw1_ref[0, k1 * tiles + t], sign * tw1_ref[1, k1 * tiles + t])
                row.append(cmul(stage[t][k1], w))
            mixed = butterfly(row, sign)
            turned.append([cmul(mixed[m1], (tw2_ref[0, m1], sign * tw2_ref[1, m1])) for m1 in range(tiles)])
        flat_re = jnp.concatenate([turned[k][m][0] for k in range(parts) for m in range(tiles)], axis=0)
        flat_im = jnp.concatenate([turned[k][m][1] for k in range(parts) for m in range(tiles)], axis=0)
        dot = lambda a, b: jnp.dot(a, b, precision=high, preferred_element_type=jnp.float32)
        out_re = dot(flat_re, dft_cos) - sign * dot(flat_im, dft_sin)
        out_im = dot(flat_im, dft_cos) + sign * dot(flat_re, dft_sin)
        return out_re, out_im

    def inverse(flat, sign):
        dot = lambda a, b: jnp.dot(a, b, precision=high, preferred_element_type=jnp.float32)
        f_re, f_im = flat
        b_re = dot(f_re, dft_cos) - sign * dot(f_im, dft_sin)
        b_im = dot(f_im, dft_cos) + sign * dot(f_re, dft_sin)
        piece = lambda a, k, m: a[(k * tiles + m) * block:(k * tiles + m + 1) * block]
        stage = []
        for k1 in range(parts):
            row = [cmul((piece(b_re, k1, m), piece(b_im, k1, m)), (tw2_ref[0, m], sign * tw2_ref[1, m]))
                   for m in range(tiles)]
            mixed = butterfly(row, sign)
            stage.append([cmul(mixed[t], (tw1_ref[0, k1 * tiles + t], sign * tw1_ref[1, k1 * tiles + t]))
                          for t in range(tiles)])
        grid = [butterfly([stage[k1][t] for k1 in range(parts)], sign) for t in range(tiles)]
        return grid

    for sc in range(scen_dev):
        w_grid, c_grid = [], []
        for src in range(parts):
            w_row, c_row = [], []
            for t in range(tiles):
                lanes = slice(t * LANES, (t + 1) * LANES)
                t_re = x_ref[src, 0, sc, :, lanes]
                t_im = x_ref[src, 1, sc, :, lanes]
                swap_re = jnp.concatenate([t_re[half:], t_re[:half]], axis=0)
                swap_im = jnp.concatenate([t_im[half:], t_im[:half]], axis=0)
                p_re = jnp.where(keep, t_re, swap_re)
                p_im = jnp.where(keep, t_im, swap_im)
                f_re = jnp.where(plain, 1.0, phi_ref[0, src * tiles + t])
                f_im = jnp.where(plain, 0.0, -phi_ref[1, src * tiles + t])
                u_re = p_re * f_re + p_im * f_im
                u_im = p_re * f_im - p_im * f_re
                w_row.append((0.5 * (t_re + u_re), 0.5 * (t_im + u_im)))
                c_row.append((0.5 * (t_im - u_im), 0.5 * (u_re - t_re)))
            w_grid.append(w_row)
            c_grid.append(c_row)
        dist = transform(w_grid, -1.0)
        cot = transform(c_grid, -1.0)
        birth = cmul(dist, dist)
        adjoint = cmul(cot, (dist[0], -dist[1]))
        joined = (birth[0] - adjoint[1], birth[1] + adjoint[0])
        grid = inverse(joined, 1.0)
        for src in range(parts):
            for t in range(tiles):
                lanes = slice(t * LANES, (t + 1) * LANES)
                value = cmul(grid[t][src], (back_ref[0, src * tiles + t], back_ref[1, src * tiles + t]))
                o_ref[src, 0, sc, :, lanes] = value[0]
                o_ref[src, 1, sc, :, lanes] = value[1]


def column_stage(received, own_rows, place, nfft):
    parts, _, scen_dev, block, cols = received.shape
    tiles = cols // LANES
    width = parts * cols
    half = block // 2
    pos = counting(block)

    def table(angle):
        return jnp.asarray(np.stack([np.cos(angle), np.sin(angle)]), jnp.float32)

    lane = np.arange(LANES)
    chunk = np.arange(parts * tiles)
    spots = chunk[:, None] * LANES + lane[None, :]
    phi = table(2.0 * np.pi * spots / width).reshape(2, parts * tiles, 1, LANES)
    tw1 = table(2.0 * np.pi * (((chunk % tiles) * LANES)[:, None] + lane[None, :]) * (chunk // tiles)[:, None] / width)
    tw1 = tw1.reshape(2, parts * tiles, 1, LANES)
    tw2 = table(2.0 * np.pi * np.arange(tiles)[:, None] * lane[None, :] / cols).reshape(2, tiles, 1, LANES)
    dft = table(2.0 * np.pi * ((lane[:, None] * lane[None, :]) % LANES) / LANES)
    coarse = phases(own_rows, counting(parts * tiles) * LANES, nfft)
    fine = phases(own_rows, counting(LANES), nfft)
    back = complex_mul((coarse[0].T[:, :, None], coarse[1].T[:, :, None]), (fine[0][None], fine[1][None]))
    back = jnp.stack(back)
    lead = place == 0
    keep = jnp.broadcast_to((lead & ((pos == 0) | (pos == half)))[:, None], (block, LANES))
    plain = jnp.broadcast_to((lead & (pos == 0))[:, None], (block, LANES))
    flags = jnp.stack([keep, plain]).astype(jnp.float32)
    vmem = pl.BlockSpec(memory_space=pltpu.VMEM)
    return pl.pallas_call(
        column_kernel,
        out_shape=jax.ShapeDtypeStruct(received.shape, jnp.float32),
        in_specs=[vmem] * 7,
        out_specs=vmem,
    )(received, phi, tw1, tw2, back, flags, dft)


def exchange(value):
    return lax.all_to_all(value, "mass", 0, 0, tiled=True)


def shards(density, cotangent, rate):
    high = lax.Precision.HIGHEST
    scen_dev, bin_dev = density.shape
    arrays = 2 * scen_dev
    parts = lax.axis_size("mass")
    place = lax.axis_index("mass")
    width = C1 * C2
    rows = bin_dev // width
    half_rows = rows * parts
    full_rows = 2 * half_rows
    cols = width // parts
    block = full_rows // parts
    nbin = half_rows * width
    nfft = 2 * nbin
    beta = aggregation_coef / nbin
    offset = place * bin_dev
    mass = ((offset + counting(bin_dev)).astype(jnp.float32) + 0.5) / nbin
    weighted = mass[None, :] * density
    partial = jnp.concatenate([jnp.sum(weighted, axis=1), jnp.sum(cotangent * weighted, axis=1)])
    flux = rate[None, :] * weighted
    tile = jnp.zeros((8, cols), jnp.float32).at[0, :arrays].set(partial).at[1, :scen_dev].set(flux[:, -1])
    stacked = jnp.concatenate([weighted, cotangent], axis=0).reshape(arrays, rows, parts, cols)
    outgoing = stacked.transpose(2, 0, 1, 3).reshape(parts, arrays * rows, cols)
    outgoing = jnp.concatenate([outgoing, jnp.broadcast_to(tile, (parts, 8, cols))], axis=1)
    incoming_rows = exchange(outgoing)
    moments = jnp.sum(incoming_rows[:, arrays * rows, :arrays], axis=0)
    first, cross = moments[:scen_dev], moments[scen_dev:]
    neighbours = incoming_rows[:, arrays * rows + 1, :scen_dev]
    behind = lax.dynamic_index_in_dim(neighbours, (place + parts - 1) % parts, keepdims=False)
    incoming = jnp.where(place > 0, behind, 0.0)[:, None]
    spread = incoming_rows[:, : arrays * rows].reshape(parts, arrays, rows, cols)
    spread = spread.transpose(1, 0, 2, 3).reshape(arrays, half_rows, cols)
    half = block // 2
    pos = counting(block)
    own_rows = jnp.where(pos < half, half * place + pos, (full_rows - half * place - (pos - half)) % full_rows)
    own_rows = jnp.where((place == 0) & (pos == half), full_rows // 2, own_rows)
    table = np.arange(block)[None, :]
    order = np.where(table < half, half * np.arange(parts)[:, None] + table,
                     (full_rows - half * np.arange(parts)[:, None] - (table - half)) % full_rows)
    order[0, half] = full_rows // 2
    order_np = order.reshape(-1)
    order = jnp.asarray(order_np, jnp.int32)
    row_angle = 2.0 * np.pi * ((order_np[:, None] * np.arange(half_rows)[None, :]) % full_rows) / full_rows
    row_cos, row_sin = jnp.asarray(np.cos(row_angle), jnp.float32), jnp.asarray(np.sin(row_angle), jnp.float32)
    forward_rows = jnp.stack([jnp.stack([row_cos, row_sin], axis=1), jnp.stack([-row_sin, row_cos], axis=1)])
    packed = spread.reshape(2, scen_dev, half_rows, cols)
    freq = jnp.einsum("okir,isrw->oskw", forward_rows, packed, precision=high)
    tiles = cols // LANES
    coarse_cos, coarse_sin = phases(order, place * cols + counting(tiles) * LANES, nfft)
    fine_angle = 2.0 * np.pi * ((order_np[:, None] * np.arange(LANES)[None, :]) % nfft) / nfft
    fine_cos = jnp.asarray(np.cos(fine_angle), jnp.float32)[:, None, :]
    fine_sin = jnp.asarray(np.sin(fine_angle), jnp.float32)[:, None, :]
    tw_cos, tw_sin = complex_mul((coarse_cos[:, :, None], coarse_sin[:, :, None]), (fine_cos, fine_sin))
    tw_cos, tw_sin = tw_cos.reshape(full_rows, cols), tw_sin.reshape(full_rows, cols)
    twisted = jnp.stack(complex_mul((freq[0], freq[1]), (tw_cos, -tw_sin)))
    twisted = twisted.reshape(2, scen_dev, parts, block, cols).transpose(2, 0, 1, 3, 4)
    untwisted = column_stage(exchange(twisted), own_rows, place, nfft)
    returned = exchange(untwisted).transpose(1, 2, 0, 3, 4).reshape(2, scen_dev, full_rows, cols)
    inv_cos, inv_sin = row_cos.T, row_sin.T
    inverse_rows = jnp.stack([jnp.stack([inv_cos, -inv_sin], axis=1), jnp.stack([inv_sin, inv_cos], axis=1)])
    real_part = jnp.einsum("orik,iskw->osrw", inverse_rows, returned, precision=high)
    real_part = real_part.reshape(arrays, half_rows, cols)
    real_part = real_part.reshape(arrays, parts, rows, cols).transpose(1, 0, 2, 3)
    gathered = exchange(real_part).transpose(1, 2, 0, 3).reshape(arrays, bin_dev) / nfft
    birth = gathered[:scen_dev]
    corr = gathered[scen_dev:]
    inflow = jnp.concatenate([incoming, flux[:, :-1]], axis=1)
    tendency = 0.5 * beta * birth - beta * first[:, None] * weighted - flux + inflow
    arriving = from_behind(cotangent[:, :1], "mass", -1)
    following = jnp.concatenate([cotangent[:, 1:], arriving], axis=1)
    adjoint = mass[None, :] * (
        beta * corr
        - beta * first[:, None] * cotangent
        - beta * cross[:, None]
        - rate[None, :] * cotangent
        + rate[None, :] * following
    )
    local_grad = jnp.sum(weighted * (following - cotangent), axis=0)
    rate_gradient = local_grad
    groups = lax.axis_size("scen")
    if groups & (groups - 1) == 0:
        step = 1
        while step < groups:
            pairs = [(source, source ^ step) for source in range(groups)]
            rate_gradient = rate_gradient + lax.ppermute(rate_gradient, "scen", pairs)
            step *= 2
    else:
        rate_gradient = lax.psum(local_grad, "scen")
    return (tendency, adjoint, rate_gradient)


def solution(mesh):
    in_specs = (P("scen", "mass"), P("scen", "mass"), P("mass"))
    out_specs = (P("scen", "mass"), P("scen", "mass"), P("mass"))
    return jax.shard_map(shards, mesh=mesh, in_specs=in_specs, out_specs=out_specs, check_vma=False)
```

```python
import functools
import math

import jax
import numpy as np
import jax.numpy as jnp
from jax import lax
from jax.experimental import pallas as pl
from jax.experimental.pallas import tpu as pltpu
from jax.sharding import PartitionSpec as P

C1 = 32
C2 = 128


aggregation_coef = 12.0


def from_behind(value, axis, steps):
    count = lax.axis_size(axis)
    first, last = (max(0, -steps), min(count, count - steps))
    return lax.ppermute(value, axis, [(source, source + steps) for source in range(first, last)])


def phases(left, right, total):
    outer = left[:, None] * right[None, :] % total
    angle = outer.astype(jnp.float32) * (2.0 * math.pi / total)
    return (jnp.cos(angle), jnp.sin(angle))


def counting(count):
    return lax.iota(jnp.int32, count)


def complex_dot(form, table, values):
    table_re, table_im = table
    val_re, val_im = values
    high = lax.Precision.HIGHEST
    real_out = jnp.einsum(form, table_re, val_re, precision=high) - jnp.einsum(
        form, table_im, val_im, precision=high
    )
    imag_out = jnp.einsum(form, table_re, val_im, precision=high) + jnp.einsum(
        form, table_im, val_re, precision=high
    )
    return (real_out, imag_out)


def complex_mul(left, right):
    return (left[0] * right[0] - left[1] * right[1], left[0] * right[1] + left[1] * right[0])


def column_forward(values):
    lead = values[0].shape[:-1]
    shaped = (values[0].reshape(lead + (C1, C2)), values[1].reshape(lead + (C1, C2)))
    cos_one, sin_one = phases(counting(C1), counting(C1), C1)
    step_one = complex_dot("pa,...ab->...pb", (cos_one, -sin_one), shaped)
    tw_cos, tw_sin = phases(counting(C1), counting(C2), C1 * C2)
    turned = complex_mul(step_one, (tw_cos, -tw_sin))
    cos_two, sin_two = phases(counting(C2), counting(C2), C2)
    return complex_dot("qb,...pb->...pq", (cos_two, -sin_two), turned)


def column_inverse(values):
    lead = values[0].shape[:-2]
    cos_two, sin_two = phases(counting(C2), counting(C2), C2)
    step_one = complex_dot("qb,...pq->...pb", (cos_two, sin_two), values)
    tw_cos, tw_sin = phases(counting(C1), counting(C2), C1 * C2)
    turned = complex_mul(step_one, (tw_cos, tw_sin))
    cos_one, sin_one = phases(counting(C1), counting(C1), C1)
    result = complex_dot("pa,...pb->...ab", (cos_one, sin_one), turned)
    return (result[0].reshape(lead + (C1 * C2,)), result[1].reshape(lead + (C1 * C2,)))


LANES = 128


def butterfly(values, sign):
    count = len(values)
    if count == 1:
        return list(values)
    even = butterfly(values[0::2], sign)
    odd = butterfly(values[1::2], sign)
    out = [None] * count
    for k in range(count // 2):
        o_re, o_im = odd[k]
        if k == 0:
            t = (o_re, o_im)
        elif 4 * k == count:
            t = (-sign * o_im, sign * o_re)
        else:
            c = math.cos(2.0 * math.pi * k / count)
            s = sign * math.sin(2.0 * math.pi * k / count)
            t = (o_re * c - o_im * s, o_re * s + o_im * c)
        e_re, e_im = even[k]
        out[k] = (e_re + t[0], e_im + t[1])
        out[k + count // 2] = (e_re - t[0], e_im - t[1])
    return out


def column_kernel(x_ref, phi_ref, tw1_ref, tw2_ref, back_ref, flag_ref, dft_ref, o_ref):
    parts, _, scen_dev, block, cols = x_ref.shape
    tiles = cols // LANES
    half = block // 2
    high = lax.Precision.HIGHEST
    keep = flag_ref[0] > 0.5
    plain = flag_ref[1] > 0.5
    dft_cos = dft_ref[0]
    dft_sin = dft_ref[1]

    def cmul(a, b):
        return (a[0] * b[0] - a[1] * b[1], a[0] * b[1] + a[1] * b[0])

    def transform(grid, sign):
        stage = [butterfly([grid[src][t] for src in range(parts)], sign) for t in range(tiles)]
        turned = []
        for k1 in range(parts):
            row = []
            for t in range(tiles):
                w = (tw1_ref[0, k1 * tiles + t], sign * tw1_ref[1, k1 * tiles + t])
                row.append(cmul(stage[t][k1], w))
            mixed = butterfly(row, sign)
            turned.append([cmul(mixed[m1], (tw2_ref[0, m1], sign * tw2_ref[1, m1])) for m1 in range(tiles)])
        flat_re = jnp.concatenate([turned[k][m][0] for k in range(parts) for m in range(tiles)], axis=0)
        flat_im = jnp.concatenate([turned[k][m][1] for k in range(parts) for m in range(tiles)], axis=0)
        dot = lambda a, b: jnp.dot(a, b, precision=high, preferred_element_type=jnp.float32)
        out_re = dot(flat_re, dft_cos) - sign * dot(flat_im, dft_sin)
        out_im = dot(flat_im, dft_cos) + sign * dot(flat_re, dft_sin)
        return out_re, out_im

    def inverse(flat, sign):
        dot = lambda a, b: jnp.dot(a, b, precision=high, preferred_element_type=jnp.float32)
        f_re, f_im = flat
        b_re = dot(f_re, dft_cos) - sign * dot(f_im, dft_sin)
        b_im = dot(f_im, dft_cos) + sign * dot(f_re, dft_sin)
        piece = lambda a, k, m: a[(k * tiles + m) * block:(k * tiles + m + 1) * block]
        stage = []
        for k1 in range(parts):
            row = [cmul((piece(b_re, k1, m), piece(b_im, k1, m)), (tw2_ref[0, m], sign * tw2_ref[1, m]))
                   for m in range(tiles)]
            mixed = butterfly(row, sign)
            stage.append([cmul(mixed[t], (tw1_ref[0, k1 * tiles + t], sign * tw1_ref[1, k1 * tiles + t]))
                          for t in range(tiles)])
        grid = [butterfly([stage[k1][t] for k1 in range(parts)], sign) for t in range(tiles)]
        return grid

    for sc in range(scen_dev):
        w_grid, c_grid = [], []
        for src in range(parts):
            w_row, c_row = [], []
            for t in range(tiles):
                lanes = slice(t * LANES, (t + 1) * LANES)
                t_re = x_ref[src, 0, sc, :, lanes]
                t_im = x_ref[src, 1, sc, :, lanes]
                swap_re = jnp.concatenate([t_re[half:], t_re[:half]], axis=0)
                swap_im = jnp.concatenate([t_im[half:], t_im[:half]], axis=0)
                p_re = jnp.where(keep, t_re, swap_re)
                p_im = jnp.where(keep, t_im, swap_im)
                f_re = jnp.where(plain, 1.0, phi_ref[0, src * tiles + t])
                f_im = jnp.where(plain, 0.0, -phi_ref[1, src * tiles + t])
                u_re = p_re * f_re + p_im * f_im
                u_im = p_re * f_im - p_im * f_re
                w_row.append((0.5 * (t_re + u_re), 0.5 * (t_im + u_im)))
                c_row.append((0.5 * (t_im - u_im), 0.5 * (u_re - t_re)))
            w_grid.append(w_row)
            c_grid.append(c_row)
        dist = transform(w_grid, -1.0)
        cot = transform(c_grid, -1.0)
        birth = cmul(dist, dist)
        adjoint = cmul(cot, (dist[0], -dist[1]))
        joined = (birth[0] - adjoint[1], birth[1] + adjoint[0])
        grid = inverse(joined, 1.0)
        for src in range(parts):
            for t in range(tiles):
                lanes = slice(t * LANES, (t + 1) * LANES)
                value = cmul(grid[t][src], (back_ref[0, src * tiles + t], back_ref[1, src * tiles + t]))
                o_ref[src, 0, sc, :, lanes] = value[0]
                o_ref[src, 1, sc, :, lanes] = value[1]


def column_stage(received, own_rows, place, nfft):
    parts, _, scen_dev, block, cols = received.shape
    tiles = cols // LANES
    width = parts * cols
    half = block // 2
    pos = counting(block)

    def table(angle):
        return jnp.asarray(np.stack([np.cos(angle), np.sin(angle)]), jnp.float32)

    lane = np.arange(LANES)
    chunk = np.arange(parts * tiles)
    spots = chunk[:, None] * LANES + lane[None, :]
    phi = table(2.0 * np.pi * spots / width).reshape(2, parts * tiles, 1, LANES)
    tw1 = table(2.0 * np.pi * (((chunk % tiles) * LANES)[:, None] + lane[None, :]) * (chunk // tiles)[:, None] / width)
    tw1 = tw1.reshape(2, parts * tiles, 1, LANES)
    tw2 = table(2.0 * np.pi * np.arange(tiles)[:, None] * lane[None, :] / cols).reshape(2, tiles, 1, LANES)
    dft = table(2.0 * np.pi * ((lane[:, None] * lane[None, :]) % LANES) / LANES)
    coarse = phases(own_rows, counting(parts * tiles) * LANES, nfft)
    fine = phases(own_rows, counting(LANES), nfft)
    back = complex_mul((coarse[0].T[:, :, None], coarse[1].T[:, :, None]), (fine[0][None], fine[1][None]))
    back = jnp.stack(back)
    lead = place == 0
    keep = jnp.broadcast_to((lead & ((pos == 0) | (pos == half)))[:, None], (block, LANES))
    plain = jnp.broadcast_to((lead & (pos == 0))[:, None], (block, LANES))
    flags = jnp.stack([keep, plain]).astype(jnp.float32)
    vmem = pl.BlockSpec(memory_space=pltpu.VMEM)
    return pl.pallas_call(
        column_kernel,
        out_shape=jax.ShapeDtypeStruct(received.shape, jnp.float32),
        in_specs=[vmem] * 7,
        out_specs=vmem,
    )(received, phi, tw1, tw2, back, flags, dft)


def prologue_kernel(nbin, base_ref, d_ref, c_ref, r_ref, o_ref):
    parts, _, cols = o_ref.shape
    scen_dev = d_ref.shape[0]
    lines = d_ref.shape[1]
    tiles = cols // LANES
    rows = (o_ref.shape[1] - 8) // (2 * scen_dev)
    per_row = lines // rows
    arrays = 2 * scen_dev
    base = base_ref[0]
    line = lax.broadcasted_iota(jnp.int32, (lines, LANES), 0)
    lane = lax.broadcasted_iota(jnp.int32, (lines, LANES), 1)
    mass = ((base + line * LANES + lane).astype(jnp.float32) + 0.5) / nbin
    sums = []
    flux_last = []
    for sc in range(scen_dev):
        weighted = mass * d_ref[sc]
        sums.append((jnp.sum(weighted), sc))
        sums.append((jnp.sum(c_ref[sc] * weighted), scen_dev + sc))
        flux_last.append(r_ref[lines - 1:lines, LANES - 1:LANES] * weighted[lines - 1:lines, LANES - 1:LANES])
    t_row = lax.broadcasted_iota(jnp.int32, (8, cols), 0)
    t_lane = lax.broadcasted_iota(jnp.int32, (8, cols), 1)
    tile = jnp.zeros((8, cols), jnp.float32)
    for value, slot in sums:
        tile = jnp.where((t_row == 0) & (t_lane == slot), value, tile)
    for sc in range(scen_dev):
        tile = jnp.where((t_row == 1) & (t_lane == sc), flux_last[sc], tile)
    s_line = lax.broadcasted_iota(jnp.int32, (rows, LANES), 0)
    s_lane = lax.broadcasted_iota(jnp.int32, (rows, LANES), 1)
    for j in range(parts):
        for t in range(tiles):
            first_line = j * tiles + t
            picked = s_line * per_row + first_line
            part_mass = ((base + picked * LANES + s_lane).astype(jnp.float32) + 0.5) / nbin
            for sc in range(scen_dev):
                dens = d_ref[sc, pl.ds(first_line, rows, stride=per_row), :]
                cot = c_ref[sc, pl.ds(first_line, rows, stride=per_row), :]
                o_ref[j, sc * rows:(sc + 1) * rows, t * LANES:(t + 1) * LANES] = part_mass * dens
                o_ref[j, (scen_dev + sc) * rows:(scen_dev + sc + 1) * rows, t * LANES:(t + 1) * LANES] = cot
        o_ref[j, arrays * rows:arrays * rows + 8, :] = tile


def prologue(density, cotangent, rate, offset, nbin, parts, rows, cols):
    scen_dev, bin_dev = density.shape
    lines = bin_dev // LANES
    base = jnp.reshape(offset, (1,)).astype(jnp.int32)
    vmem = pl.BlockSpec(memory_space=pltpu.VMEM)
    return pl.pallas_call(
        functools.partial(prologue_kernel, nbin),
        out_shape=jax.ShapeDtypeStruct((parts, 2 * scen_dev * rows + 8, cols), jnp.float32),
        in_specs=[pl.BlockSpec(memory_space=pltpu.SMEM), vmem, vmem, vmem],
        out_specs=vmem,
    )(base, density.reshape(scen_dev, lines, LANES), cotangent.reshape(scen_dev, lines, LANES),
      rate.reshape(lines, LANES))


def exchange(value):
    return lax.all_to_all(value, "mass", 0, 0, tiled=True)


def shards(density, cotangent, rate):
    high = lax.Precision.HIGHEST
    scen_dev, bin_dev = density.shape
    arrays = 2 * scen_dev
    parts = lax.axis_size("mass")
    place = lax.axis_index("mass")
    width = C1 * C2
    rows = bin_dev // width
    half_rows = rows * parts
    full_rows = 2 * half_rows
    cols = width // parts
    block = full_rows // parts
    nbin = half_rows * width
    nfft = 2 * nbin
    beta = aggregation_coef / nbin
    offset = place * bin_dev
    mass = ((offset + counting(bin_dev)).astype(jnp.float32) + 0.5) / nbin
    weighted = mass[None, :] * density
    flux = rate[None, :] * weighted
    outgoing = prologue(density, cotangent, rate, offset, nbin, parts, rows, cols)
    incoming_rows = exchange(outgoing)
    moments = jnp.sum(incoming_rows[:, arrays * rows, :arrays], axis=0)
    first, cross = moments[:scen_dev], moments[scen_dev:]
    neighbours = incoming_rows[:, arrays * rows + 1, :scen_dev]
    behind = lax.dynamic_index_in_dim(neighbours, (place + parts - 1) % parts, keepdims=False)
    incoming = jnp.where(place > 0, behind, 0.0)[:, None]
    spread = incoming_rows[:, : arrays * rows].reshape(parts, arrays, rows, cols)
    spread = spread.transpose(1, 0, 2, 3).reshape(arrays, half_rows, cols)
    half = block // 2
    pos = counting(block)
    own_rows = jnp.where(pos < half, half * place + pos, (full_rows - half * place - (pos - half)) % full_rows)
    own_rows = jnp.where((place == 0) & (pos == half), full_rows // 2, own_rows)
    table = np.arange(block)[None, :]
    order = np.where(table < half, half * np.arange(parts)[:, None] + table,
                     (full_rows - half * np.arange(parts)[:, None] - (table - half)) % full_rows)
    order[0, half] = full_rows // 2
    order_np = order.reshape(-1)
    order = jnp.asarray(order_np, jnp.int32)
    row_angle = 2.0 * np.pi * ((order_np[:, None] * np.arange(half_rows)[None, :]) % full_rows) / full_rows
    row_cos, row_sin = jnp.asarray(np.cos(row_angle), jnp.float32), jnp.asarray(np.sin(row_angle), jnp.float32)
    forward_rows = jnp.stack([jnp.stack([row_cos, row_sin], axis=1), jnp.stack([-row_sin, row_cos], axis=1)])
    packed = spread.reshape(2, scen_dev, half_rows, cols)
    freq = jnp.einsum("okir,isrw->oskw", forward_rows, packed, precision=high)
    tiles = cols // LANES
    coarse_cos, coarse_sin = phases(order, place * cols + counting(tiles) * LANES, nfft)
    fine_angle = 2.0 * np.pi * ((order_np[:, None] * np.arange(LANES)[None, :]) % nfft) / nfft
    fine_cos = jnp.asarray(np.cos(fine_angle), jnp.float32)[:, None, :]
    fine_sin = jnp.asarray(np.sin(fine_angle), jnp.float32)[:, None, :]
    tw_cos, tw_sin = complex_mul((coarse_cos[:, :, None], coarse_sin[:, :, None]), (fine_cos, fine_sin))
    tw_cos, tw_sin = tw_cos.reshape(full_rows, cols), tw_sin.reshape(full_rows, cols)
    twisted = jnp.stack(complex_mul((freq[0], freq[1]), (tw_cos, -tw_sin)))
    twisted = twisted.reshape(2, scen_dev, parts, block, cols).transpose(2, 0, 1, 3, 4)
    untwisted = column_stage(exchange(twisted), own_rows, place, nfft)
    returned = exchange(untwisted).transpose(1, 2, 0, 3, 4).reshape(2, scen_dev, full_rows, cols)
    inv_cos, inv_sin = row_cos.T, row_sin.T
    inverse_rows = jnp.stack([jnp.stack([inv_cos, -inv_sin], axis=1), jnp.stack([inv_sin, inv_cos], axis=1)])
    real_part = jnp.einsum("orik,iskw->osrw", inverse_rows, returned, precision=high)
    real_part = real_part.reshape(arrays, half_rows, cols)
    real_part = real_part.reshape(arrays, parts, rows, cols).transpose(1, 0, 2, 3)
    gathered = exchange(real_part).transpose(1, 2, 0, 3).reshape(arrays, bin_dev) / nfft
    birth = gathered[:scen_dev]
    corr = gathered[scen_dev:]
    inflow = jnp.concatenate([incoming, flux[:, :-1]], axis=1)
    tendency = 0.5 * beta * birth - beta * first[:, None] * weighted - flux + inflow
    arriving = from_behind(cotangent[:, :1], "mass", -1)
    following = jnp.concatenate([cotangent[:, 1:], arriving], axis=1)
    adjoint = mass[None, :] * (
        beta * corr
        - beta * first[:, None] * cotangent
        - beta * cross[:, None]
        - rate[None, :] * cotangent
        + rate[None, :] * following
    )
    local_grad = jnp.sum(weighted * (following - cotangent), axis=0)
    rate_gradient = local_grad
    groups = lax.axis_size("scen")
    if groups & (groups - 1) == 0:
        step = 1
        while step < groups:
            pairs = [(source, source ^ step) for source in range(groups)]
            rate_gradient = rate_gradient + lax.ppermute(rate_gradient, "scen", pairs)
            step *= 2
    else:
        rate_gradient = lax.psum(local_grad, "scen")
    return (tendency, adjoint, rate_gradient)


def solution(mesh):
    in_specs = (P("scen", "mass"), P("scen", "mass"), P("mass"))
    out_specs = (P("scen", "mass"), P("scen", "mass"), P("mass"))
    return jax.shard_map(shards, mesh=mesh, in_specs=in_specs, out_specs=out_specs, check_vma=False)
```

```python
import functools
import math

import jax
import numpy as np
import jax.numpy as jnp
from jax import lax
from jax.experimental import pallas as pl
from jax.experimental.pallas import tpu as pltpu
from jax.sharding import PartitionSpec as P

C1 = 32
C2 = 128


aggregation_coef = 12.0


def from_behind(value, axis, steps):
    count = lax.axis_size(axis)
    first, last = (max(0, -steps), min(count, count - steps))
    return lax.ppermute(value, axis, [(source, source + steps) for source in range(first, last)])


def phases(left, right, total):
    outer = left[:, None] * right[None, :] % total
    angle = outer.astype(jnp.float32) * (2.0 * math.pi / total)
    return (jnp.cos(angle), jnp.sin(angle))


def counting(count):
    return lax.iota(jnp.int32, count)


def complex_dot(form, table, values):
    table_re, table_im = table
    val_re, val_im = values
    high = lax.Precision.HIGHEST
    real_out = jnp.einsum(form, table_re, val_re, precision=high) - jnp.einsum(
        form, table_im, val_im, precision=high
    )
    imag_out = jnp.einsum(form, table_re, val_im, precision=high) + jnp.einsum(
        form, table_im, val_re, precision=high
    )
    return (real_out, imag_out)


def complex_mul(left, right):
    return (left[0] * right[0] - left[1] * right[1], left[0] * right[1] + left[1] * right[0])


def column_forward(values):
    lead = values[0].shape[:-1]
    shaped = (values[0].reshape(lead + (C1, C2)), values[1].reshape(lead + (C1, C2)))
    cos_one, sin_one = phases(counting(C1), counting(C1), C1)
    step_one = complex_dot("pa,...ab->...pb", (cos_one, -sin_one), shaped)
    tw_cos, tw_sin = phases(counting(C1), counting(C2), C1 * C2)
    turned = complex_mul(step_one, (tw_cos, -tw_sin))
    cos_two, sin_two = phases(counting(C2), counting(C2), C2)
    return complex_dot("qb,...pb->...pq", (cos_two, -sin_two), turned)


def column_inverse(values):
    lead = values[0].shape[:-2]
    cos_two, sin_two = phases(counting(C2), counting(C2), C2)
    step_one = complex_dot("qb,...pq->...pb", (cos_two, sin_two), values)
    tw_cos, tw_sin = phases(counting(C1), counting(C2), C1 * C2)
    turned = complex_mul(step_one, (tw_cos, tw_sin))
    cos_one, sin_one = phases(counting(C1), counting(C1), C1)
    result = complex_dot("pa,...pb->...ab", (cos_one, sin_one), turned)
    return (result[0].reshape(lead + (C1 * C2,)), result[1].reshape(lead + (C1 * C2,)))


LANES = 128


def butterfly(values, sign):
    count = len(values)
    if count == 1:
        return list(values)
    even = butterfly(values[0::2], sign)
    odd = butterfly(values[1::2], sign)
    out = [None] * count
    for k in range(count // 2):
        o_re, o_im = odd[k]
        if k == 0:
            t = (o_re, o_im)
        elif 4 * k == count:
            t = (-sign * o_im, sign * o_re)
        else:
            c = math.cos(2.0 * math.pi * k / count)
            s = sign * math.sin(2.0 * math.pi * k / count)
            t = (o_re * c - o_im * s, o_re * s + o_im * c)
        e_re, e_im = even[k]
        out[k] = (e_re + t[0], e_im + t[1])
        out[k + count // 2] = (e_re - t[0], e_im - t[1])
    return out


def column_kernel(x_ref, phi_ref, tw1_ref, tw2_ref, back_ref, flag_ref, dft_ref, o_ref):
    parts, _, scen_dev, block, cols = x_ref.shape
    tiles = cols // LANES
    half = block // 2
    high = lax.Precision.HIGHEST
    keep = flag_ref[0] > 0.5
    plain = flag_ref[1] > 0.5
    dft_cos = dft_ref[0]
    dft_sin = dft_ref[1]

    def cmul(a, b):
        return (a[0] * b[0] - a[1] * b[1], a[0] * b[1] + a[1] * b[0])

    def transform(grid, sign):
        stage = [butterfly([grid[src][t] for src in range(parts)], sign) for t in range(tiles)]
        turned = []
        for k1 in range(parts):
            row = []
            for t in range(tiles):
                w = (tw1_ref[0, k1 * tiles + t], sign * tw1_ref[1, k1 * tiles + t])
                row.append(cmul(stage[t][k1], w))
            mixed = butterfly(row, sign)
            turned.append([cmul(mixed[m1], (tw2_ref[0, m1], sign * tw2_ref[1, m1])) for m1 in range(tiles)])
        flat_re = jnp.concatenate([turned[k][m][0] for k in range(parts) for m in range(tiles)], axis=0)
        flat_im = jnp.concatenate([turned[k][m][1] for k in range(parts) for m in range(tiles)], axis=0)
        dot = lambda a, b: jnp.dot(a, b, precision=high, preferred_element_type=jnp.float32)
        out_re = dot(flat_re, dft_cos) - sign * dot(flat_im, dft_sin)
        out_im = dot(flat_im, dft_cos) + sign * dot(flat_re, dft_sin)
        return out_re, out_im

    def inverse(flat, sign):
        dot = lambda a, b: jnp.dot(a, b, precision=high, preferred_element_type=jnp.float32)
        f_re, f_im = flat
        b_re = dot(f_re, dft_cos) - sign * dot(f_im, dft_sin)
        b_im = dot(f_im, dft_cos) + sign * dot(f_re, dft_sin)
        piece = lambda a, k, m: a[(k * tiles + m) * block:(k * tiles + m + 1) * block]
        stage = []
        for k1 in range(parts):
            row = [cmul((piece(b_re, k1, m), piece(b_im, k1, m)), (tw2_ref[0, m], sign * tw2_ref[1, m]))
                   for m in range(tiles)]
            mixed = butterfly(row, sign)
            stage.append([cmul(mixed[t], (tw1_ref[0, k1 * tiles + t], sign * tw1_ref[1, k1 * tiles + t]))
                          for t in range(tiles)])
        grid = [butterfly([stage[k1][t] for k1 in range(parts)], sign) for t in range(tiles)]
        return grid

    for sc in range(scen_dev):
        w_grid, c_grid = [], []
        for src in range(parts):
            w_row, c_row = [], []
            for t in range(tiles):
                lanes = slice(t * LANES, (t + 1) * LANES)
                t_re = x_ref[src, 0, sc, :, lanes]
                t_im = x_ref[src, 1, sc, :, lanes]
                swap_re = jnp.concatenate([t_re[half:], t_re[:half]], axis=0)
                swap_im = jnp.concatenate([t_im[half:], t_im[:half]], axis=0)
                p_re = jnp.where(keep, t_re, swap_re)
                p_im = jnp.where(keep, t_im, swap_im)
                f_re = jnp.where(plain, 1.0, phi_ref[0, src * tiles + t])
                f_im = jnp.where(plain, 0.0, -phi_ref[1, src * tiles + t])
                u_re = p_re * f_re + p_im * f_im
                u_im = p_re * f_im - p_im * f_re
                w_row.append((0.5 * (t_re + u_re), 0.5 * (t_im + u_im)))
                c_row.append((0.5 * (t_im - u_im), 0.5 * (u_re - t_re)))
            w_grid.append(w_row)
            c_grid.append(c_row)
        dist = transform(w_grid, -1.0)
        cot = transform(c_grid, -1.0)
        birth = cmul(dist, dist)
        adjoint = cmul(cot, (dist[0], -dist[1]))
        joined = (birth[0] - adjoint[1], birth[1] + adjoint[0])
        grid = inverse(joined, 1.0)
        for src in range(parts):
            for t in range(tiles):
                lanes = slice(t * LANES, (t + 1) * LANES)
                value = cmul(grid[t][src], (back_ref[0, src * tiles + t], back_ref[1, src * tiles + t]))
                o_ref[src, 0, sc, :, lanes] = value[0]
                o_ref[src, 1, sc, :, lanes] = value[1]


def column_stage(received, own_rows, place, nfft):
    parts, _, scen_dev, block, cols = received.shape
    tiles = cols // LANES
    width = parts * cols
    half = block // 2
    pos = counting(block)

    def table(angle):
        return jnp.asarray(np.stack([np.cos(angle), np.sin(angle)]), jnp.float32)

    lane = np.arange(LANES)
    chunk = np.arange(parts * tiles)
    spots = chunk[:, None] * LANES + lane[None, :]
    phi = table(2.0 * np.pi * spots / width).reshape(2, parts * tiles, 1, LANES)
    tw1 = table(2.0 * np.pi * (((chunk % tiles) * LANES)[:, None] + lane[None, :]) * (chunk // tiles)[:, None] / width)
    tw1 = tw1.reshape(2, parts * tiles, 1, LANES)
    tw2 = table(2.0 * np.pi * np.arange(tiles)[:, None] * lane[None, :] / cols).reshape(2, tiles, 1, LANES)
    dft = table(2.0 * np.pi * ((lane[:, None] * lane[None, :]) % LANES) / LANES)
    coarse = phases(own_rows, counting(parts * tiles) * LANES, nfft)
    fine = phases(own_rows, counting(LANES), nfft)
    back = complex_mul((coarse[0].T[:, :, None], coarse[1].T[:, :, None]), (fine[0][None], fine[1][None]))
    back = jnp.stack(back)
    lead = place == 0
    keep = jnp.broadcast_to((lead & ((pos == 0) | (pos == half)))[:, None], (block, LANES))
    plain = jnp.broadcast_to((lead & (pos == 0))[:, None], (block, LANES))
    flags = jnp.stack([keep, plain]).astype(jnp.float32)
    vmem = pl.BlockSpec(memory_space=pltpu.VMEM)
    return pl.pallas_call(
        column_kernel,
        out_shape=jax.ShapeDtypeStruct(received.shape, jnp.float32),
        in_specs=[vmem] * 7,
        out_specs=vmem,
    )(received, phi, tw1, tw2, back, flags, dft)


def prologue_kernel(nbin, base_ref, d_ref, c_ref, r_ref, o_ref):
    parts, _, cols = o_ref.shape
    scen_dev = d_ref.shape[0]
    lines = d_ref.shape[1]
    tiles = cols // LANES
    rows = (o_ref.shape[1] - 8) // (2 * scen_dev)
    per_row = lines // rows
    arrays = 2 * scen_dev
    base = base_ref[0]
    line = lax.broadcasted_iota(jnp.int32, (lines, LANES), 0)
    lane = lax.broadcasted_iota(jnp.int32, (lines, LANES), 1)
    mass = ((base + line * LANES + lane).astype(jnp.float32) + 0.5) / nbin
    sums = []
    flux_last = []
    for sc in range(scen_dev):
        weighted = mass * d_ref[sc]
        sums.append((jnp.sum(weighted), sc))
        sums.append((jnp.sum(c_ref[sc] * weighted), scen_dev + sc))
        flux_last.append(r_ref[lines - 1:lines, LANES - 1:LANES] * weighted[lines - 1:lines, LANES - 1:LANES])
    t_row = lax.broadcasted_iota(jnp.int32, (8, cols), 0)
    t_lane = lax.broadcasted_iota(jnp.int32, (8, cols), 1)
    tile = jnp.zeros((8, cols), jnp.float32)
    for value, slot in sums:
        tile = jnp.where((t_row == 0) & (t_lane == slot), value, tile)
    for sc in range(scen_dev):
        tile = jnp.where((t_row == 1) & (t_lane == sc), flux_last[sc], tile)
    s_line = lax.broadcasted_iota(jnp.int32, (rows, LANES), 0)
    s_lane = lax.broadcasted_iota(jnp.int32, (rows, LANES), 1)
    for j in range(parts):
        for t in range(tiles):
            first_line = j * tiles + t
            picked = s_line * per_row + first_line
            part_mass = ((base + picked * LANES + s_lane).astype(jnp.float32) + 0.5) / nbin
            for sc in range(scen_dev):
                dens = d_ref[sc, pl.ds(first_line, rows, stride=per_row), :]
                cot = c_ref[sc, pl.ds(first_line, rows, stride=per_row), :]
                o_ref[j, sc * rows:(sc + 1) * rows, t * LANES:(t + 1) * LANES] = part_mass * dens
                o_ref[j, (scen_dev + sc) * rows:(scen_dev + sc + 1) * rows, t * LANES:(t + 1) * LANES] = cot
        o_ref[j, arrays * rows:arrays * rows + 8, :] = tile


def prologue(density, cotangent, rate, offset, nbin, parts, rows, cols):
    scen_dev, bin_dev = density.shape
    lines = bin_dev // LANES
    base = jnp.reshape(offset, (1,)).astype(jnp.int32)
    vmem = pl.BlockSpec(memory_space=pltpu.VMEM)
    return pl.pallas_call(
        functools.partial(prologue_kernel, nbin),
        out_shape=jax.ShapeDtypeStruct((parts, 2 * scen_dev * rows + 8, cols), jnp.float32),
        in_specs=[pl.BlockSpec(memory_space=pltpu.SMEM), vmem, vmem, vmem],
        out_specs=vmem,
    )(base, density.reshape(scen_dev, lines, LANES), cotangent.reshape(scen_dev, lines, LANES),
      rate.reshape(lines, LANES))


def exchange(value):
    return lax.all_to_all(value, "mass", 0, 0, tiled=True)


def shards(density, cotangent, rate):
    high = lax.Precision.HIGHEST
    scen_dev, bin_dev = density.shape
    arrays = 2 * scen_dev
    parts = lax.axis_size("mass")
    place = lax.axis_index("mass")
    width = C1 * C2
    rows = bin_dev // width
    half_rows = rows * parts
    full_rows = 2 * half_rows
    cols = width // parts
    block = full_rows // parts
    nbin = half_rows * width
    nfft = 2 * nbin
    beta = aggregation_coef / nbin
    offset = place * bin_dev
    mass = ((offset + counting(bin_dev)).astype(jnp.float32) + 0.5) / nbin
    weighted = mass[None, :] * density
    flux = rate[None, :] * weighted
    outgoing = prologue(density, cotangent, rate, offset, nbin, parts, rows, cols)
    incoming_rows = exchange(outgoing)
    moments = jnp.sum(incoming_rows[:, arrays * rows, :arrays], axis=0)
    first, cross = moments[:scen_dev], moments[scen_dev:]
    neighbours = incoming_rows[:, arrays * rows + 1, :scen_dev]
    behind = lax.dynamic_index_in_dim(neighbours, (place + parts - 1) % parts, keepdims=False)
    incoming = jnp.where(place > 0, behind, 0.0)[:, None]
    spread = incoming_rows[:, : arrays * rows].reshape(parts, arrays, rows, cols)
    spread = spread.transpose(1, 0, 2, 3).reshape(arrays, half_rows, cols)
    half = block // 2
    pos = counting(block)
    own_rows = jnp.where(pos < half, half * place + pos, (full_rows - half * place - (pos - half)) % full_rows)
    own_rows = jnp.where((place == 0) & (pos == half), full_rows // 2, own_rows)
    table = np.arange(block)[None, :]
    order = np.where(table < half, half * np.arange(parts)[:, None] + table,
                     (full_rows - half * np.arange(parts)[:, None] - (table - half)) % full_rows)
    order[0, half] = full_rows // 2
    order_np = order.reshape(-1)
    order = jnp.asarray(order_np, jnp.int32)
    row_angle = 2.0 * np.pi * ((order_np[:, None] * np.arange(half_rows)[None, :]) % full_rows) / full_rows
    row_cos, row_sin = jnp.asarray(np.cos(row_angle), jnp.float32), jnp.asarray(np.sin(row_angle), jnp.float32)
    forward_rows = jnp.stack([jnp.stack([row_cos, row_sin], axis=1), jnp.stack([-row_sin, row_cos], axis=1)])
    packed = spread.reshape(2, scen_dev, half_rows, cols)
    freq = jnp.einsum("okir,isrw->oskw", forward_rows, packed, precision=high)
    tiles = cols // LANES
    coarse_cos, coarse_sin = phases(order, place * cols + counting(tiles) * LANES, nfft)
    fine_angle = 2.0 * np.pi * ((order_np[:, None] * np.arange(LANES)[None, :]) % nfft) / nfft
    fine_cos = jnp.asarray(np.cos(fine_angle), jnp.float32)[:, None, :]
    fine_sin = jnp.asarray(np.sin(fine_angle), jnp.float32)[:, None, :]
    tw_cos, tw_sin = complex_mul((coarse_cos[:, :, None], coarse_sin[:, :, None]), (fine_cos, fine_sin))
    tw_cos, tw_sin = tw_cos.reshape(full_rows, cols), tw_sin.reshape(full_rows, cols)
    twisted = jnp.stack(complex_mul((freq[0], freq[1]), (tw_cos, -tw_sin)))
    twisted = twisted.reshape(2, scen_dev, parts, block, cols).transpose(2, 0, 1, 3, 4)
    arriving = from_behind(cotangent[:, :1], "mass", -1)
    following = jnp.concatenate([cotangent[:, 1:], arriving], axis=1)
    local_grad = jnp.sum(weighted * (following - cotangent), axis=0)
    rate_gradient = local_grad
    groups = lax.axis_size("scen")
    if groups & (groups - 1) == 0:
        step = 1
        while step < groups:
            pairs = [(source, source ^ step) for source in range(groups)]
            rate_gradient = rate_gradient + lax.ppermute(rate_gradient, "scen", pairs)
            step *= 2
    else:
        rate_gradient = lax.psum(local_grad, "scen")
    received, rate_gradient = lax.optimization_barrier((exchange(twisted), rate_gradient))
    untwisted = column_stage(received, own_rows, place, nfft)
    returned = exchange(untwisted).transpose(1, 2, 0, 3, 4).reshape(2, scen_dev, full_rows, cols)
    inv_cos, inv_sin = row_cos.T, row_sin.T
    inverse_rows = jnp.stack([jnp.stack([inv_cos, -inv_sin], axis=1), jnp.stack([inv_sin, inv_cos], axis=1)])
    real_part = jnp.einsum("orik,iskw->osrw", inverse_rows, returned, precision=high)
    real_part = real_part.reshape(arrays, half_rows, cols)
    real_part = real_part.reshape(arrays, parts, rows, cols).transpose(1, 0, 2, 3)
    gathered = exchange(real_part).transpose(1, 2, 0, 3).reshape(arrays, bin_dev) / nfft
    birth = gathered[:scen_dev]
    corr = gathered[scen_dev:]
    inflow = jnp.concatenate([incoming, flux[:, :-1]], axis=1)
    tendency = 0.5 * beta * birth - beta * first[:, None] * weighted - flux + inflow
    adjoint = mass[None, :] * (
        beta * corr
        - beta * first[:, None] * cotangent
        - beta * cross[:, None]
        - rate[None, :] * cotangent
        + rate[None, :] * following
    )
    return (tendency, adjoint, rate_gradient)


def solution(mesh):
    in_specs = (P("scen", "mass"), P("scen", "mass"), P("mass"))
    out_specs = (P("scen", "mass"), P("scen", "mass"), P("mass"))
    return jax.shard_map(shards, mesh=mesh, in_specs=in_specs, out_specs=out_specs, check_vma=False)
```

```python
import functools
import math

import jax
import numpy as np
import jax.numpy as jnp
from jax import lax
from jax.experimental import pallas as pl
from jax.experimental.pallas import tpu as pltpu
from jax.sharding import PartitionSpec as P

C1 = 32
C2 = 128


aggregation_coef = 12.0


def from_behind(value, axis, steps):
    count = lax.axis_size(axis)
    first, last = (max(0, -steps), min(count, count - steps))
    return lax.ppermute(value, axis, [(source, source + steps) for source in range(first, last)])


def phases(left, right, total):
    outer = left[:, None] * right[None, :] % total
    angle = outer.astype(jnp.float32) * (2.0 * math.pi / total)
    return (jnp.cos(angle), jnp.sin(angle))


def counting(count):
    return lax.iota(jnp.int32, count)


def complex_dot(form, table, values):
    table_re, table_im = table
    val_re, val_im = values
    high = lax.Precision.HIGHEST
    real_out = jnp.einsum(form, table_re, val_re, precision=high) - jnp.einsum(
        form, table_im, val_im, precision=high
    )
    imag_out = jnp.einsum(form, table_re, val_im, precision=high) + jnp.einsum(
        form, table_im, val_re, precision=high
    )
    return (real_out, imag_out)


def complex_mul(left, right):
    return (left[0] * right[0] - left[1] * right[1], left[0] * right[1] + left[1] * right[0])


def column_forward(values):
    lead = values[0].shape[:-1]
    shaped = (values[0].reshape(lead + (C1, C2)), values[1].reshape(lead + (C1, C2)))
    cos_one, sin_one = phases(counting(C1), counting(C1), C1)
    step_one = complex_dot("pa,...ab->...pb", (cos_one, -sin_one), shaped)
    tw_cos, tw_sin = phases(counting(C1), counting(C2), C1 * C2)
    turned = complex_mul(step_one, (tw_cos, -tw_sin))
    cos_two, sin_two = phases(counting(C2), counting(C2), C2)
    return complex_dot("qb,...pb->...pq", (cos_two, -sin_two), turned)


def column_inverse(values):
    lead = values[0].shape[:-2]
    cos_two, sin_two = phases(counting(C2), counting(C2), C2)
    step_one = complex_dot("qb,...pq->...pb", (cos_two, sin_two), values)
    tw_cos, tw_sin = phases(counting(C1), counting(C2), C1 * C2)
    turned = complex_mul(step_one, (tw_cos, tw_sin))
    cos_one, sin_one = phases(counting(C1), counting(C1), C1)
    result = complex_dot("pa,...pb->...ab", (cos_one, sin_one), turned)
    return (result[0].reshape(lead + (C1 * C2,)), result[1].reshape(lead + (C1 * C2,)))


LANES = 128


def butterfly(values, sign):
    count = len(values)
    if count == 1:
        return list(values)
    even = butterfly(values[0::2], sign)
    odd = butterfly(values[1::2], sign)
    out = [None] * count
    for k in range(count // 2):
        o_re, o_im = odd[k]
        if k == 0:
            t = (o_re, o_im)
        elif 4 * k == count:
            t = (-sign * o_im, sign * o_re)
        else:
            c = math.cos(2.0 * math.pi * k / count)
            s = sign * math.sin(2.0 * math.pi * k / count)
            t = (o_re * c - o_im * s, o_re * s + o_im * c)
        e_re, e_im = even[k]
        out[k] = (e_re + t[0], e_im + t[1])
        out[k + count // 2] = (e_re - t[0], e_im - t[1])
    return out


def column_kernel(x_ref, phi_ref, tw1_ref, tw2_ref, back_ref, flag_ref, dft_ref, o_ref):
    parts, _, scen_dev, block, cols = x_ref.shape
    tiles = cols // LANES
    half = block // 2
    high = lax.Precision.HIGHEST
    keep = flag_ref[0] > 0.5
    plain = flag_ref[1] > 0.5
    dft_cos = dft_ref[0]
    dft_sin = dft_ref[1]

    def cmul(a, b):
        return (a[0] * b[0] - a[1] * b[1], a[0] * b[1] + a[1] * b[0])

    def transform(grid, sign):
        stage = [butterfly([grid[src][t] for src in range(parts)], sign) for t in range(tiles)]
        turned = []
        for k1 in range(parts):
            row = []
            for t in range(tiles):
                w = (tw1_ref[0, k1 * tiles + t], sign * tw1_ref[1, k1 * tiles + t])
                row.append(cmul(stage[t][k1], w))
            mixed = butterfly(row, sign)
            turned.append([cmul(mixed[m1], (tw2_ref[0, m1], sign * tw2_ref[1, m1])) for m1 in range(tiles)])
        flat_re = jnp.concatenate([turned[k][m][0] for k in range(parts) for m in range(tiles)], axis=0)
        flat_im = jnp.concatenate([turned[k][m][1] for k in range(parts) for m in range(tiles)], axis=0)
        dot = lambda a, b: jnp.dot(a, b, precision=high, preferred_element_type=jnp.float32)
        out_re = dot(flat_re, dft_cos) - sign * dot(flat_im, dft_sin)
        out_im = dot(flat_im, dft_cos) + sign * dot(flat_re, dft_sin)
        return out_re, out_im

    def inverse(flat, sign):
        dot = lambda a, b: jnp.dot(a, b, precision=high, preferred_element_type=jnp.float32)
        f_re, f_im = flat
        b_re = dot(f_re, dft_cos) - sign * dot(f_im, dft_sin)
        b_im = dot(f_im, dft_cos) + sign * dot(f_re, dft_sin)
        piece = lambda a, k, m: a[(k * tiles + m) * block:(k * tiles + m + 1) * block]
        stage = []
        for k1 in range(parts):
            row = [cmul((piece(b_re, k1, m), piece(b_im, k1, m)), (tw2_ref[0, m], sign * tw2_ref[1, m]))
                   for m in range(tiles)]
            mixed = butterfly(row, sign)
            stage.append([cmul(mixed[t], (tw1_ref[0, k1 * tiles + t], sign * tw1_ref[1, k1 * tiles + t]))
                          for t in range(tiles)])
        grid = [butterfly([stage[k1][t] for k1 in range(parts)], sign) for t in range(tiles)]
        return grid

    for sc in range(scen_dev):
        w_grid, c_grid = [], []
        for src in range(parts):
            w_row, c_row = [], []
            for t in range(tiles):
                lanes = slice(t * LANES, (t + 1) * LANES)
                t_re = x_ref[src, 0, sc, :, lanes]
                t_im = x_ref[src, 1, sc, :, lanes]
                swap_re = jnp.concatenate([t_re[half:], t_re[:half]], axis=0)
                swap_im = jnp.concatenate([t_im[half:], t_im[:half]], axis=0)
                p_re = jnp.where(keep, t_re, swap_re)
                p_im = jnp.where(keep, t_im, swap_im)
                f_re = jnp.where(plain, 1.0, phi_ref[0, src * tiles + t])
                f_im = jnp.where(plain, 0.0, -phi_ref[1, src * tiles + t])
                u_re = p_re * f_re + p_im * f_im
                u_im = p_re * f_im - p_im * f_re
                w_row.append((0.5 * (t_re + u_re), 0.5 * (t_im + u_im)))
                c_row.append((0.5 * (t_im - u_im), 0.5 * (u_re - t_re)))
            w_grid.append(w_row)
            c_grid.append(c_row)
        dist = transform(w_grid, -1.0)
        cot = transform(c_grid, -1.0)
        birth = cmul(dist, dist)
        adjoint = cmul(cot, (dist[0], -dist[1]))
        joined = (birth[0] - adjoint[1], birth[1] + adjoint[0])
        grid = inverse(joined, 1.0)
        for src in range(parts):
            for t in range(tiles):
                lanes = slice(t * LANES, (t + 1) * LANES)
                value = cmul(grid[t][src], (back_ref[0, src * tiles + t], back_ref[1, src * tiles + t]))
                o_ref[src, 0, sc, :, lanes] = value[0]
                o_ref[src, 1, sc, :, lanes] = value[1]


def column_stage(received, own_rows, place, nfft):
    parts, _, scen_dev, block, cols = received.shape
    tiles = cols // LANES
    width = parts * cols
    half = block // 2
    pos = counting(block)

    def table(angle):
        return jnp.asarray(np.stack([np.cos(angle), np.sin(angle)]), jnp.float32)

    lane = np.arange(LANES)
    chunk = np.arange(parts * tiles)
    spots = chunk[:, None] * LANES + lane[None, :]
    phi = table(2.0 * np.pi * spots / width).reshape(2, parts * tiles, 1, LANES)
    tw1 = table(2.0 * np.pi * (((chunk % tiles) * LANES)[:, None] + lane[None, :]) * (chunk // tiles)[:, None] / width)
    tw1 = tw1.reshape(2, parts * tiles, 1, LANES)
    tw2 = table(2.0 * np.pi * np.arange(tiles)[:, None] * lane[None, :] / cols).reshape(2, tiles, 1, LANES)
    dft = table(2.0 * np.pi * ((lane[:, None] * lane[None, :]) % LANES) / LANES)
    coarse = phases(own_rows, counting(parts * tiles) * LANES, nfft)
    fine = phases(own_rows, counting(LANES), nfft)
    back = complex_mul((coarse[0].T[:, :, None], coarse[1].T[:, :, None]), (fine[0][None], fine[1][None]))
    back = jnp.stack(back)
    lead = place == 0
    keep = jnp.broadcast_to((lead & ((pos == 0) | (pos == half)))[:, None], (block, LANES))
    plain = jnp.broadcast_to((lead & (pos == 0))[:, None], (block, LANES))
    flags = jnp.stack([keep, plain]).astype(jnp.float32)
    vmem = pl.BlockSpec(memory_space=pltpu.VMEM)
    return pl.pallas_call(
        column_kernel,
        out_shape=jax.ShapeDtypeStruct(received.shape, jnp.float32),
        in_specs=[vmem] * 7,
        out_specs=vmem,
    )(received, phi, tw1, tw2, back, flags, dft)


def prologue_kernel(nbin, base_ref, d_ref, c_ref, r_ref, o_ref):
    parts, _, cols = o_ref.shape
    scen_dev = d_ref.shape[0]
    lines = d_ref.shape[1]
    tiles = cols // LANES
    rows = (o_ref.shape[1] - 8) // (2 * scen_dev)
    per_row = lines // rows
    arrays = 2 * scen_dev
    base = base_ref[0]
    line = lax.broadcasted_iota(jnp.int32, (lines, LANES), 0)
    lane = lax.broadcasted_iota(jnp.int32, (lines, LANES), 1)
    mass = ((base + line * LANES + lane).astype(jnp.float32) + 0.5) / nbin
    sums = []
    flux_last = []
    for sc in range(scen_dev):
        weighted = mass * d_ref[sc]
        sums.append((jnp.sum(weighted), sc))
        sums.append((jnp.sum(c_ref[sc] * weighted), scen_dev + sc))
        flux_last.append(r_ref[lines - 1:lines, LANES - 1:LANES] * weighted[lines - 1:lines, LANES - 1:LANES])
    t_row = lax.broadcasted_iota(jnp.int32, (8, cols), 0)
    t_lane = lax.broadcasted_iota(jnp.int32, (8, cols), 1)
    tile = jnp.zeros((8, cols), jnp.float32)
    for value, slot in sums:
        tile = jnp.where((t_row == 0) & (t_lane == slot), value, tile)
    for sc in range(scen_dev):
        tile = jnp.where((t_row == 1) & (t_lane == sc), flux_last[sc], tile)
    s_line = lax.broadcasted_iota(jnp.int32, (rows, LANES), 0)
    s_lane = lax.broadcasted_iota(jnp.int32, (rows, LANES), 1)
    for j in range(parts):
        for t in range(tiles):
            first_line = j * tiles + t
            picked = s_line * per_row + first_line
            part_mass = ((base + picked * LANES + s_lane).astype(jnp.float32) + 0.5) / nbin
            for sc in range(scen_dev):
                dens = d_ref[sc, pl.ds(first_line, rows, stride=per_row), :]
                cot = c_ref[sc, pl.ds(first_line, rows, stride=per_row), :]
                o_ref[j, sc * rows:(sc + 1) * rows, t * LANES:(t + 1) * LANES] = part_mass * dens
                o_ref[j, (scen_dev + sc) * rows:(scen_dev + sc + 1) * rows, t * LANES:(t + 1) * LANES] = cot
        o_ref[j, arrays * rows:arrays * rows + 8, :] = tile


def prologue(density, cotangent, rate, offset, nbin, parts, rows, cols):
    scen_dev, bin_dev = density.shape
    lines = bin_dev // LANES
    base = jnp.reshape(offset, (1,)).astype(jnp.int32)
    vmem = pl.BlockSpec(memory_space=pltpu.VMEM)
    return pl.pallas_call(
        functools.partial(prologue_kernel, nbin),
        out_shape=jax.ShapeDtypeStruct((parts, 2 * scen_dev * rows + 8, cols), jnp.float32),
        in_specs=[pl.BlockSpec(memory_space=pltpu.SMEM), vmem, vmem, vmem],
        out_specs=vmem,
    )(base, density.reshape(scen_dev, lines, LANES), cotangent.reshape(scen_dev, lines, LANES),
      rate.reshape(lines, LANES))


def exchange(value):
    return lax.all_to_all(value, "mass", 0, 0, tiled=True)


def shards(density, cotangent, rate):
    high = lax.Precision.HIGHEST
    scen_dev, bin_dev = density.shape
    arrays = 2 * scen_dev
    parts = lax.axis_size("mass")
    place = lax.axis_index("mass")
    width = C1 * C2
    rows = bin_dev // width
    half_rows = rows * parts
    full_rows = 2 * half_rows
    cols = width // parts
    block = full_rows // parts
    nbin = half_rows * width
    nfft = 2 * nbin
    beta = aggregation_coef / nbin
    offset = place * bin_dev
    mass = ((offset + counting(bin_dev)).astype(jnp.float32) + 0.5) / nbin
    weighted = mass[None, :] * density
    flux = rate[None, :] * weighted
    outgoing = prologue(density, cotangent, rate, offset, nbin, parts, rows, cols)
    incoming_rows = exchange(outgoing)
    moments = jnp.sum(incoming_rows[:, arrays * rows, :arrays], axis=0)
    first, cross = moments[:scen_dev], moments[scen_dev:]
    neighbours = incoming_rows[:, arrays * rows + 1, :scen_dev]
    behind = lax.dynamic_index_in_dim(neighbours, (place + parts - 1) % parts, keepdims=False)
    incoming = jnp.where(place > 0, behind, 0.0)[:, None]
    spread = incoming_rows[:, : arrays * rows].reshape(parts, arrays, rows, cols)
    spread = spread.transpose(1, 0, 2, 3).reshape(arrays, half_rows, cols)
    half = block // 2
    pos = counting(block)
    own_rows = jnp.where(pos < half, half * place + pos, (full_rows - half * place - (pos - half)) % full_rows)
    own_rows = jnp.where((place == 0) & (pos == half), full_rows // 2, own_rows)
    table = np.arange(block)[None, :]
    order = np.where(table < half, half * np.arange(parts)[:, None] + table,
                     (full_rows - half * np.arange(parts)[:, None] - (table - half)) % full_rows)
    order[0, half] = full_rows // 2
    order_np = order.reshape(-1)
    order = jnp.asarray(order_np, jnp.int32)
    row_angle = 2.0 * np.pi * ((order_np[:, None] * np.arange(half_rows)[None, :]) % full_rows) / full_rows
    row_cos, row_sin = jnp.asarray(np.cos(row_angle), jnp.float32), jnp.asarray(np.sin(row_angle), jnp.float32)
    forward_rows = jnp.stack([jnp.stack([row_cos, row_sin], axis=1), jnp.stack([-row_sin, row_cos], axis=1)])
    packed = spread.reshape(2, scen_dev, half_rows, cols)
    freq = jnp.einsum("okir,isrw->oskw", forward_rows, packed, precision=high)
    tiles = cols // LANES
    coarse_cos, coarse_sin = phases(order, place * cols + counting(tiles) * LANES, nfft)
    fine_angle = 2.0 * np.pi * ((order_np[:, None] * np.arange(LANES)[None, :]) % nfft) / nfft
    fine_cos = jnp.asarray(np.cos(fine_angle), jnp.float32)[:, None, :]
    fine_sin = jnp.asarray(np.sin(fine_angle), jnp.float32)[:, None, :]
    tw_cos, tw_sin = complex_mul((coarse_cos[:, :, None], coarse_sin[:, :, None]), (fine_cos, fine_sin))
    tw_cos, tw_sin = tw_cos.reshape(full_rows, cols), tw_sin.reshape(full_rows, cols)
    twisted = jnp.stack(complex_mul((freq[0], freq[1]), (tw_cos, -tw_sin)))
    twisted = twisted.reshape(2, scen_dev, parts, block, cols).transpose(2, 0, 1, 3, 4)
    arriving = from_behind(cotangent[:, :1], "mass", -1)
    following = jnp.concatenate([cotangent[:, 1:], arriving], axis=1)
    local_grad = jnp.sum(weighted * (following - cotangent), axis=0)
    rate_gradient = local_grad
    groups = lax.axis_size("scen")
    if groups & (groups - 1) == 0 and groups <= 4:
        member = lax.axis_index("scen")
        held = [local_grad] + [
            lax.ppermute(local_grad, "scen", [(source, source ^ k) for source in range(groups)])
            for k in range(1, groups)
        ]
        held = jnp.stack(held)
        ordered = jnp.take(held, jnp.bitwise_xor(member, counting(groups)), axis=0)
        rate_gradient = ordered[0]
        for k in range(1, groups):
            rate_gradient = rate_gradient + ordered[k]
    elif groups & (groups - 1) == 0:
        step = 1
        while step < groups:
            pairs = [(source, source ^ step) for source in range(groups)]
            rate_gradient = rate_gradient + lax.ppermute(rate_gradient, "scen", pairs)
            step *= 2
    else:
        rate_gradient = lax.psum(local_grad, "scen")
    untwisted = column_stage(exchange(twisted), own_rows, place, nfft)
    untwisted, rate_gradient = lax.optimization_barrier((untwisted, rate_gradient))
    returned = exchange(untwisted).transpose(1, 2, 0, 3, 4).reshape(2, scen_dev, full_rows, cols)
    inv_cos, inv_sin = row_cos.T, row_sin.T
    inverse_rows = jnp.stack([jnp.stack([inv_cos, -inv_sin], axis=1), jnp.stack([inv_sin, inv_cos], axis=1)])
    real_part = jnp.einsum("orik,iskw->osrw", inverse_rows, returned, precision=high)
    real_part = real_part.reshape(arrays, half_rows, cols)
    real_part = real_part.reshape(arrays, parts, rows, cols).transpose(1, 0, 2, 3)
    gathered = exchange(real_part).transpose(1, 2, 0, 3).reshape(arrays, bin_dev) / nfft
    birth = gathered[:scen_dev]
    corr = gathered[scen_dev:]
    inflow = jnp.concatenate([incoming, flux[:, :-1]], axis=1)
    tendency = 0.5 * beta * birth - beta * first[:, None] * weighted - flux + inflow
    adjoint = mass[None, :] * (
        beta * corr
        - beta * first[:, None] * cotangent
        - beta * cross[:, None]
        - rate[None, :] * cotangent
        + rate[None, :] * following
    )
    return (tendency, adjoint, rate_gradient)


def solution(mesh):
    in_specs = (P("scen", "mass"), P("scen", "mass"), P("mass"))
    out_specs = (P("scen", "mass"), P("scen", "mass"), P("mass"))
    return jax.shard_map(shards, mesh=mesh, in_specs=in_specs, out_specs=out_specs, check_vma=False)
```

```python
import functools
import math

import jax
import numpy as np
import jax.numpy as jnp
from jax import lax
from jax.experimental import pallas as pl
from jax.experimental.pallas import tpu as pltpu
from jax.sharding import PartitionSpec as P

C1 = 32
C2 = 128


aggregation_coef = 12.0


def from_behind(value, axis, steps):
    count = lax.axis_size(axis)
    first, last = (max(0, -steps), min(count, count - steps))
    return lax.ppermute(value, axis, [(source, source + steps) for source in range(first, last)])


def phases(left, right, total):
    outer = left[:, None] * right[None, :] % total
    angle = outer.astype(jnp.float32) * (2.0 * math.pi / total)
    return (jnp.cos(angle), jnp.sin(angle))


def counting(count):
    return lax.iota(jnp.int32, count)


def complex_dot(form, table, values):
    table_re, table_im = table
    val_re, val_im = values
    high = lax.Precision.HIGHEST
    real_out = jnp.einsum(form, table_re, val_re, precision=high) - jnp.einsum(
        form, table_im, val_im, precision=high
    )
    imag_out = jnp.einsum(form, table_re, val_im, precision=high) + jnp.einsum(
        form, table_im, val_re, precision=high
    )
    return (real_out, imag_out)


def complex_mul(left, right):
    return (left[0] * right[0] - left[1] * right[1], left[0] * right[1] + left[1] * right[0])


def column_forward(values):
    lead = values[0].shape[:-1]
    shaped = (values[0].reshape(lead + (C1, C2)), values[1].reshape(lead + (C1, C2)))
    cos_one, sin_one = phases(counting(C1), counting(C1), C1)
    step_one = complex_dot("pa,...ab->...pb", (cos_one, -sin_one), shaped)
    tw_cos, tw_sin = phases(counting(C1), counting(C2), C1 * C2)
    turned = complex_mul(step_one, (tw_cos, -tw_sin))
    cos_two, sin_two = phases(counting(C2), counting(C2), C2)
    return complex_dot("qb,...pb->...pq", (cos_two, -sin_two), turned)


def column_inverse(values):
    lead = values[0].shape[:-2]
    cos_two, sin_two = phases(counting(C2), counting(C2), C2)
    step_one = complex_dot("qb,...pq->...pb", (cos_two, sin_two), values)
    tw_cos, tw_sin = phases(counting(C1), counting(C2), C1 * C2)
    turned = complex_mul(step_one, (tw_cos, tw_sin))
    cos_one, sin_one = phases(counting(C1), counting(C1), C1)
    result = complex_dot("pa,...pb->...ab", (cos_one, sin_one), turned)
    return (result[0].reshape(lead + (C1 * C2,)), result[1].reshape(lead + (C1 * C2,)))


LANES = 128


def butterfly(values, sign):
    count = len(values)
    if count == 1:
        return list(values)
    even = butterfly(values[0::2], sign)
    odd = butterfly(values[1::2], sign)
    out = [None] * count
    for k in range(count // 2):
        o_re, o_im = odd[k]
        if k == 0:
            t = (o_re, o_im)
        elif 4 * k == count:
            t = (-sign * o_im, sign * o_re)
        else:
            c = math.cos(2.0 * math.pi * k / count)
            s = sign * math.sin(2.0 * math.pi * k / count)
            t = (o_re * c - o_im * s, o_re * s + o_im * c)
        e_re, e_im = even[k]
        out[k] = (e_re + t[0], e_im + t[1])
        out[k + count // 2] = (e_re - t[0], e_im - t[1])
    return out


def column_kernel(x_ref, phi_ref, tw1_ref, tw2_ref, back_ref, flag_ref, dft_ref, o_ref):
    parts, _, scen_dev, block, cols = x_ref.shape
    tiles = cols // LANES
    half = block // 2
    high = lax.Precision.HIGHEST
    keep = flag_ref[0] > 0.5
    plain = flag_ref[1] > 0.5
    dft_cos = dft_ref[0]
    dft_sin = dft_ref[1]

    def cmul(a, b):
        return (a[0] * b[0] - a[1] * b[1], a[0] * b[1] + a[1] * b[0])

    def transform(grid, sign):
        stage = [butterfly([grid[src][t] for src in range(parts)], sign) for t in range(tiles)]
        turned = []
        for k1 in range(parts):
            row = []
            for t in range(tiles):
                w = (tw1_ref[0, k1 * tiles + t], sign * tw1_ref[1, k1 * tiles + t])
                row.append(cmul(stage[t][k1], w))
            mixed = butterfly(row, sign)
            turned.append([cmul(mixed[m1], (tw2_ref[0, m1], sign * tw2_ref[1, m1])) for m1 in range(tiles)])
        flat_re = jnp.concatenate([turned[k][m][0] for k in range(parts) for m in range(tiles)], axis=0)
        flat_im = jnp.concatenate([turned[k][m][1] for k in range(parts) for m in range(tiles)], axis=0)
        dot = lambda a, b: jnp.dot(a, b, precision=high, preferred_element_type=jnp.float32)
        out_re = dot(flat_re, dft_cos) - sign * dot(flat_im, dft_sin)
        out_im = dot(flat_im, dft_cos) + sign * dot(flat_re, dft_sin)
        return out_re, out_im

    def inverse(flat, sign):
        dot = lambda a, b: jnp.dot(a, b, precision=high, preferred_element_type=jnp.float32)
        f_re, f_im = flat
        b_re = dot(f_re, dft_cos) - sign * dot(f_im, dft_sin)
        b_im = dot(f_im, dft_cos) + sign * dot(f_re, dft_sin)
        piece = lambda a, k, m: a[(k * tiles + m) * block:(k * tiles + m + 1) * block]
        stage = []
        for k1 in range(parts):
            row = [cmul((piece(b_re, k1, m), piece(b_im, k1, m)), (tw2_ref[0, m], sign * tw2_ref[1, m]))
                   for m in range(tiles)]
            mixed = butterfly(row, sign)
            stage.append([cmul(mixed[t], (tw1_ref[0, k1 * tiles + t], sign * tw1_ref[1, k1 * tiles + t]))
                          for t in range(tiles)])
        grid = [butterfly([stage[k1][t] for k1 in range(parts)], sign) for t in range(tiles)]
        return grid

    for sc in range(scen_dev):
        w_grid, c_grid = [], []
        for src in range(parts):
            w_row, c_row = [], []
            for t in range(tiles):
                lanes = slice(t * LANES, (t + 1) * LANES)
                t_re = x_ref[src, 0, sc, :, lanes]
                t_im = x_ref[src, 1, sc, :, lanes]
                swap_re = jnp.concatenate([t_re[half:], t_re[:half]], axis=0)
                swap_im = jnp.concatenate([t_im[half:], t_im[:half]], axis=0)
                p_re = jnp.where(keep, t_re, swap_re)
                p_im = jnp.where(keep, t_im, swap_im)
                f_re = jnp.where(plain, 1.0, phi_ref[0, src * tiles + t])
                f_im = jnp.where(plain, 0.0, -phi_ref[1, src * tiles + t])
                u_re = p_re * f_re + p_im * f_im
                u_im = p_re * f_im - p_im * f_re
                w_row.append((0.5 * (t_re + u_re), 0.5 * (t_im + u_im)))
                c_row.append((0.5 * (t_im - u_im), 0.5 * (u_re - t_re)))
            w_grid.append(w_row)
            c_grid.append(c_row)
        dist = transform(w_grid, -1.0)
        cot = transform(c_grid, -1.0)
        birth = cmul(dist, dist)
        adjoint = cmul(cot, (dist[0], -dist[1]))
        joined = (birth[0] - adjoint[1], birth[1] + adjoint[0])
        grid = inverse(joined, 1.0)
        for src in range(parts):
            for t in range(tiles):
                lanes = slice(t * LANES, (t + 1) * LANES)
                value = cmul(grid[t][src], (back_ref[0, src * tiles + t], back_ref[1, src * tiles + t]))
                o_ref[src, 0, sc, :, lanes] = value[0]
                o_ref[src, 1, sc, :, lanes] = value[1]


def column_stage(received, own_rows, place, nfft):
    parts, _, scen_dev, block, cols = received.shape
    tiles = cols // LANES
    width = parts * cols
    half = block // 2
    pos = counting(block)

    def table(angle):
        return jnp.asarray(np.stack([np.cos(angle), np.sin(angle)]), jnp.float32)

    lane = np.arange(LANES)
    chunk = np.arange(parts * tiles)
    spots = chunk[:, None] * LANES + lane[None, :]
    phi = table(2.0 * np.pi * spots / width).reshape(2, parts * tiles, 1, LANES)
    tw1 = table(2.0 * np.pi * (((chunk % tiles) * LANES)[:, None] + lane[None, :]) * (chunk // tiles)[:, None] / width)
    tw1 = tw1.reshape(2, parts * tiles, 1, LANES)
    tw2 = table(2.0 * np.pi * np.arange(tiles)[:, None] * lane[None, :] / cols).reshape(2, tiles, 1, LANES)
    dft = table(2.0 * np.pi * ((lane[:, None] * lane[None, :]) % LANES) / LANES)
    coarse = phases(own_rows, counting(parts * tiles) * LANES, nfft)
    fine = phases(own_rows, counting(LANES), nfft)
    back = complex_mul((coarse[0].T[:, :, None], coarse[1].T[:, :, None]), (fine[0][None], fine[1][None]))
    back = jnp.stack(back)
    lead = place == 0
    keep = jnp.broadcast_to((lead & ((pos == 0) | (pos == half)))[:, None], (block, LANES))
    plain = jnp.broadcast_to((lead & (pos == 0))[:, None], (block, LANES))
    flags = jnp.stack([keep, plain]).astype(jnp.float32)
    vmem = pl.BlockSpec(memory_space=pltpu.VMEM)
    return pl.pallas_call(
        column_kernel,
        out_shape=jax.ShapeDtypeStruct(received.shape, jnp.float32),
        in_specs=[vmem] * 7,
        out_specs=vmem,
    )(received, phi, tw1, tw2, back, flags, dft)


def prologue_kernel(nbin, base_ref, d_ref, c_ref, r_ref, o_ref):
    parts, _, cols = o_ref.shape
    scen_dev = d_ref.shape[0]
    lines = d_ref.shape[1]
    tiles = cols // LANES
    rows = (o_ref.shape[1] - 8) // (2 * scen_dev)
    per_row = lines // rows
    arrays = 2 * scen_dev
    base = base_ref[0]
    line = lax.broadcasted_iota(jnp.int32, (lines, LANES), 0)
    lane = lax.broadcasted_iota(jnp.int32, (lines, LANES), 1)
    mass = ((base + line * LANES + lane).astype(jnp.float32) + 0.5) / nbin
    sums = []
    flux_last = []
    for sc in range(scen_dev):
        weighted = mass * d_ref[sc]
        sums.append((jnp.sum(weighted), sc))
        sums.append((jnp.sum(c_ref[sc] * weighted), scen_dev + sc))
        flux_last.append(r_ref[lines - 1:lines, LANES - 1:LANES] * weighted[lines - 1:lines, LANES - 1:LANES])
    t_row = lax.broadcasted_iota(jnp.int32, (8, cols), 0)
    t_lane = lax.broadcasted_iota(jnp.int32, (8, cols), 1)
    tile = jnp.zeros((8, cols), jnp.float32)
    for value, slot in sums:
        tile = jnp.where((t_row == 0) & (t_lane == slot), value, tile)
    for sc in range(scen_dev):
        tile = jnp.where((t_row == 1) & (t_lane == sc), flux_last[sc], tile)
    s_line = lax.broadcasted_iota(jnp.int32, (rows, LANES), 0)
    s_lane = lax.broadcasted_iota(jnp.int32, (rows, LANES), 1)
    for j in range(parts):
        for t in range(tiles):
            first_line = j * tiles + t
            picked = s_line * per_row + first_line
            part_mass = ((base + picked * LANES + s_lane).astype(jnp.float32) + 0.5) / nbin
            for sc in range(scen_dev):
                dens = d_ref[sc, pl.ds(first_line, rows, stride=per_row), :]
                cot = c_ref[sc, pl.ds(first_line, rows, stride=per_row), :]
                o_ref[j, sc * rows:(sc + 1) * rows, t * LANES:(t + 1) * LANES] = part_mass * dens
                o_ref[j, (scen_dev + sc) * rows:(scen_dev + sc + 1) * rows, t * LANES:(t + 1) * LANES] = cot
        o_ref[j, arrays * rows:arrays * rows + 8, :] = tile


def prologue(density, cotangent, rate, offset, nbin, parts, rows, cols):
    scen_dev, bin_dev = density.shape
    lines = bin_dev // LANES
    base = jnp.reshape(offset, (1,)).astype(jnp.int32)
    vmem = pl.BlockSpec(memory_space=pltpu.VMEM)
    return pl.pallas_call(
        functools.partial(prologue_kernel, nbin),
        out_shape=jax.ShapeDtypeStruct((parts, 2 * scen_dev * rows + 8, cols), jnp.float32),
        in_specs=[pl.BlockSpec(memory_space=pltpu.SMEM), vmem, vmem, vmem],
        out_specs=vmem,
    )(base, density.reshape(scen_dev, lines, LANES), cotangent.reshape(scen_dev, lines, LANES),
      rate.reshape(lines, LANES))


def exchange(value):
    return lax.all_to_all(value, "mass", 0, 0, tiled=True)


def shards(density, cotangent, rate):
    high = lax.Precision.HIGHEST
    scen_dev, bin_dev = density.shape
    arrays = 2 * scen_dev
    parts = lax.axis_size("mass")
    place = lax.axis_index("mass")
    width = C1 * C2
    rows = bin_dev // width
    half_rows = rows * parts
    full_rows = 2 * half_rows
    cols = width // parts
    block = full_rows // parts
    nbin = half_rows * width
    nfft = 2 * nbin
    beta = aggregation_coef / nbin
    offset = place * bin_dev
    mass = ((offset + counting(bin_dev)).astype(jnp.float32) + 0.5) / nbin
    weighted = mass[None, :] * density
    flux = rate[None, :] * weighted
    outgoing = prologue(density, cotangent, rate, offset, nbin, parts, rows, cols)
    incoming_rows = exchange(outgoing)
    moments = jnp.sum(incoming_rows[:, arrays * rows, :arrays], axis=0)
    first, cross = moments[:scen_dev], moments[scen_dev:]
    neighbours = incoming_rows[:, arrays * rows + 1, :scen_dev]
    behind = lax.dynamic_index_in_dim(neighbours, (place + parts - 1) % parts, keepdims=False)
    incoming = jnp.where(place > 0, behind, 0.0)[:, None]
    spread = incoming_rows[:, : arrays * rows].reshape(parts, arrays, rows, cols)
    spread = spread.transpose(1, 0, 2, 3).reshape(arrays, half_rows, cols)
    half = block // 2
    pos = counting(block)
    own_rows = jnp.where(pos < half, half * place + pos, (full_rows - half * place - (pos - half)) % full_rows)
    own_rows = jnp.where((place == 0) & (pos == half), full_rows // 2, own_rows)
    table = np.arange(block)[None, :]
    order = np.where(table < half, half * np.arange(parts)[:, None] + table,
                     (full_rows - half * np.arange(parts)[:, None] - (table - half)) % full_rows)
    order[0, half] = full_rows // 2
    order_np = order.reshape(-1)
    order = jnp.asarray(order_np, jnp.int32)
    row_angle = 2.0 * np.pi * ((order_np[:, None] * np.arange(half_rows)[None, :]) % full_rows) / full_rows
    row_cos, row_sin = jnp.asarray(np.cos(row_angle), jnp.float32), jnp.asarray(np.sin(row_angle), jnp.float32)
    forward_rows = jnp.stack([jnp.stack([row_cos, row_sin], axis=1), jnp.stack([-row_sin, row_cos], axis=1)])
    packed = spread.reshape(2, scen_dev, half_rows, cols)
    freq = jnp.einsum("okir,isrw->oskw", forward_rows, packed, precision=high)
    tiles = cols // LANES
    coarse_cos, coarse_sin = phases(order, place * cols + counting(tiles) * LANES, nfft)
    fine_angle = 2.0 * np.pi * ((order_np[:, None] * np.arange(LANES)[None, :]) % nfft) / nfft
    fine_cos = jnp.asarray(np.cos(fine_angle), jnp.float32)[:, None, :]
    fine_sin = jnp.asarray(np.sin(fine_angle), jnp.float32)[:, None, :]
    tw_cos, tw_sin = complex_mul((coarse_cos[:, :, None], coarse_sin[:, :, None]), (fine_cos, fine_sin))
    tw_cos, tw_sin = tw_cos.reshape(full_rows, cols), tw_sin.reshape(full_rows, cols)
    twisted = jnp.stack(complex_mul((freq[0], freq[1]), (tw_cos, -tw_sin)))
    twisted = twisted.reshape(2, scen_dev, parts, block, cols).transpose(2, 0, 1, 3, 4)
    arriving = from_behind(cotangent[:, :1], "mass", -1)
    following = jnp.concatenate([cotangent[:, 1:], arriving], axis=1)
    local_grad = jnp.sum(weighted * (following - cotangent), axis=0)
    received, local_grad = lax.optimization_barrier((exchange(twisted), local_grad))
    rate_gradient = local_grad
    groups = lax.axis_size("scen")
    if groups & (groups - 1) == 0:
        step = 1
        while step < groups:
            pairs = [(source, source ^ step) for source in range(groups)]
            rate_gradient = rate_gradient + lax.ppermute(rate_gradient, "scen", pairs)
            step *= 2
    else:
        rate_gradient = lax.psum(local_grad, "scen")
    untwisted = column_stage(received, own_rows, place, nfft)
    returned = exchange(untwisted).transpose(1, 2, 0, 3, 4).reshape(2, scen_dev, full_rows, cols)
    inv_cos, inv_sin = row_cos.T, row_sin.T
    inverse_rows = jnp.stack([jnp.stack([inv_cos, -inv_sin], axis=1), jnp.stack([inv_sin, inv_cos], axis=1)])
    real_part = jnp.einsum("orik,iskw->osrw", inverse_rows, returned, precision=high)
    real_part = real_part.reshape(arrays, half_rows, cols)
    real_part = real_part.reshape(arrays, parts, rows, cols).transpose(1, 0, 2, 3)
    gathered = exchange(real_part).transpose(1, 2, 0, 3).reshape(arrays, bin_dev) / nfft
    birth = gathered[:scen_dev]
    corr = gathered[scen_dev:]
    inflow = jnp.concatenate([incoming, flux[:, :-1]], axis=1)
    tendency = 0.5 * beta * birth - beta * first[:, None] * weighted - flux + inflow
    adjoint = mass[None, :] * (
        beta * corr
        - beta * first[:, None] * cotangent
        - beta * cross[:, None]
        - rate[None, :] * cotangent
        + rate[None, :] * following
    )
    return (tendency, adjoint, rate_gradient)


def solution(mesh):
    in_specs = (P("scen", "mass"), P("scen", "mass"), P("mass"))
    out_specs = (P("scen", "mass"), P("scen", "mass"), P("mass"))
    return jax.shard_map(shards, mesh=mesh, in_specs=in_specs, out_specs=out_specs, check_vma=False)
```

```python
import functools
import math

import jax
import numpy as np
import jax.numpy as jnp
from jax import lax
from jax.experimental import pallas as pl
from jax.experimental.pallas import tpu as pltpu
from jax.sharding import PartitionSpec as P

C1 = 32
C2 = 128


aggregation_coef = 12.0


def from_behind(value, axis, steps):
    count = lax.axis_size(axis)
    first, last = (max(0, -steps), min(count, count - steps))
    return lax.ppermute(value, axis, [(source, source + steps) for source in range(first, last)])


def phases(left, right, total):
    outer = left[:, None] * right[None, :] % total
    angle = outer.astype(jnp.float32) * (2.0 * math.pi / total)
    return (jnp.cos(angle), jnp.sin(angle))


def counting(count):
    return lax.iota(jnp.int32, count)


def complex_dot(form, table, values):
    table_re, table_im = table
    val_re, val_im = values
    high = lax.Precision.HIGHEST
    real_out = jnp.einsum(form, table_re, val_re, precision=high) - jnp.einsum(
        form, table_im, val_im, precision=high
    )
    imag_out = jnp.einsum(form, table_re, val_im, precision=high) + jnp.einsum(
        form, table_im, val_re, precision=high
    )
    return (real_out, imag_out)


def complex_mul(left, right):
    return (left[0] * right[0] - left[1] * right[1], left[0] * right[1] + left[1] * right[0])


def column_forward(values):
    lead = values[0].shape[:-1]
    shaped = (values[0].reshape(lead + (C1, C2)), values[1].reshape(lead + (C1, C2)))
    cos_one, sin_one = phases(counting(C1), counting(C1), C1)
    step_one = complex_dot("pa,...ab->...pb", (cos_one, -sin_one), shaped)
    tw_cos, tw_sin = phases(counting(C1), counting(C2), C1 * C2)
    turned = complex_mul(step_one, (tw_cos, -tw_sin))
    cos_two, sin_two = phases(counting(C2), counting(C2), C2)
    return complex_dot("qb,...pb->...pq", (cos_two, -sin_two), turned)


def column_inverse(values):
    lead = values[0].shape[:-2]
    cos_two, sin_two = phases(counting(C2), counting(C2), C2)
    step_one = complex_dot("qb,...pq->...pb", (cos_two, sin_two), values)
    tw_cos, tw_sin = phases(counting(C1), counting(C2), C1 * C2)
    turned = complex_mul(step_one, (tw_cos, tw_sin))
    cos_one, sin_one = phases(counting(C1), counting(C1), C1)
    result = complex_dot("pa,...pb->...ab", (cos_one, sin_one), turned)
    return (result[0].reshape(lead + (C1 * C2,)), result[1].reshape(lead + (C1 * C2,)))


LANES = 128


def butterfly(values, sign):
    count = len(values)
    if count == 1:
        return list(values)
    even = butterfly(values[0::2], sign)
    odd = butterfly(values[1::2], sign)
    out = [None] * count
    for k in range(count // 2):
        o_re, o_im = odd[k]
        if k == 0:
            t = (o_re, o_im)
        elif 4 * k == count:
            t = (-sign * o_im, sign * o_re)
        else:
            c = math.cos(2.0 * math.pi * k / count)
            s = sign * math.sin(2.0 * math.pi * k / count)
            t = (o_re * c - o_im * s, o_re * s + o_im * c)
        e_re, e_im = even[k]
        out[k] = (e_re + t[0], e_im + t[1])
        out[k + count // 2] = (e_re - t[0], e_im - t[1])
    return out


def column_kernel(x_ref, phi_ref, tw1_ref, tw2_ref, back_ref, flag_ref, dft_ref, o_ref):
    parts, _, scen_dev, block, cols = x_ref.shape
    tiles = cols // LANES
    half = block // 2
    high = lax.Precision.HIGHEST
    keep = flag_ref[0] > 0.5
    plain = flag_ref[1] > 0.5
    dft_cos = dft_ref[0]
    dft_sin = dft_ref[1]

    def cmul(a, b):
        return (a[0] * b[0] - a[1] * b[1], a[0] * b[1] + a[1] * b[0])

    def transform(grid, sign):
        stage = [butterfly([grid[src][t] for src in range(parts)], sign) for t in range(tiles)]
        turned = []
        for k1 in range(parts):
            row = []
            for t in range(tiles):
                w = (tw1_ref[0, k1 * tiles + t], sign * tw1_ref[1, k1 * tiles + t])
                row.append(cmul(stage[t][k1], w))
            mixed = butterfly(row, sign)
            turned.append([cmul(mixed[m1], (tw2_ref[0, m1], sign * tw2_ref[1, m1])) for m1 in range(tiles)])
        flat_re = jnp.concatenate([turned[k][m][0] for k in range(parts) for m in range(tiles)], axis=0)
        flat_im = jnp.concatenate([turned[k][m][1] for k in range(parts) for m in range(tiles)], axis=0)
        dot = lambda a, b: jnp.dot(a, b, precision=high, preferred_element_type=jnp.float32)
        out_re = dot(flat_re, dft_cos) - sign * dot(flat_im, dft_sin)
        out_im = dot(flat_im, dft_cos) + sign * dot(flat_re, dft_sin)
        return out_re, out_im

    def inverse(flat, sign):
        dot = lambda a, b: jnp.dot(a, b, precision=high, preferred_element_type=jnp.float32)
        f_re, f_im = flat
        b_re = dot(f_re, dft_cos) - sign * dot(f_im, dft_sin)
        b_im = dot(f_im, dft_cos) + sign * dot(f_re, dft_sin)
        piece = lambda a, k, m: a[(k * tiles + m) * block:(k * tiles + m + 1) * block]
        stage = []
        for k1 in range(parts):
            row = [cmul((piece(b_re, k1, m), piece(b_im, k1, m)), (tw2_ref[0, m], sign * tw2_ref[1, m]))
                   for m in range(tiles)]
            mixed = butterfly(row, sign)
            stage.append([cmul(mixed[t], (tw1_ref[0, k1 * tiles + t], sign * tw1_ref[1, k1 * tiles + t]))
                          for t in range(tiles)])
        grid = [butterfly([stage[k1][t] for k1 in range(parts)], sign) for t in range(tiles)]
        return grid

    for sc in range(scen_dev):
        w_grid, c_grid = [], []
        for src in range(parts):
            w_row, c_row = [], []
            for t in range(tiles):
                lanes = slice(t * LANES, (t + 1) * LANES)
                t_re = x_ref[src, 0, sc, :, lanes]
                t_im = x_ref[src, 1, sc, :, lanes]
                swap_re = jnp.concatenate([t_re[half:], t_re[:half]], axis=0)
                swap_im = jnp.concatenate([t_im[half:], t_im[:half]], axis=0)
                p_re = jnp.where(keep, t_re, swap_re)
                p_im = jnp.where(keep, t_im, swap_im)
                f_re = jnp.where(plain, 1.0, phi_ref[0, src * tiles + t])
                f_im = jnp.where(plain, 0.0, -phi_ref[1, src * tiles + t])
                u_re = p_re * f_re + p_im * f_im
                u_im = p_re * f_im - p_im * f_re
                w_row.append((0.5 * (t_re + u_re), 0.5 * (t_im + u_im)))
                c_row.append((0.5 * (t_im - u_im), 0.5 * (u_re - t_re)))
            w_grid.append(w_row)
            c_grid.append(c_row)
        dist = transform(w_grid, -1.0)
        cot = transform(c_grid, -1.0)
        birth = cmul(dist, dist)
        adjoint = cmul(cot, (dist[0], -dist[1]))
        joined = (birth[0] - adjoint[1], birth[1] + adjoint[0])
        grid = inverse(joined, 1.0)
        for src in range(parts):
            for t in range(tiles):
                lanes = slice(t * LANES, (t + 1) * LANES)
                value = cmul(grid[t][src], (back_ref[0, src * tiles + t], back_ref[1, src * tiles + t]))
                o_ref[src, 0, sc, :, lanes] = value[0]
                o_ref[src, 1, sc, :, lanes] = value[1]


def column_stage(received, own_rows, place, nfft):
    parts, _, scen_dev, block, cols = received.shape
    tiles = cols // LANES
    width = parts * cols
    half = block // 2
    pos = counting(block)

    def table(angle):
        return jnp.asarray(np.stack([np.cos(angle), np.sin(angle)]), jnp.float32)

    lane = np.arange(LANES)
    chunk = np.arange(parts * tiles)
    spots = chunk[:, None] * LANES + lane[None, :]
    phi = table(2.0 * np.pi * spots / width).reshape(2, parts * tiles, 1, LANES)
    tw1 = table(2.0 * np.pi * (((chunk % tiles) * LANES)[:, None] + lane[None, :]) * (chunk // tiles)[:, None] / width)
    tw1 = tw1.reshape(2, parts * tiles, 1, LANES)
    tw2 = table(2.0 * np.pi * np.arange(tiles)[:, None] * lane[None, :] / cols).reshape(2, tiles, 1, LANES)
    dft = table(2.0 * np.pi * ((lane[:, None] * lane[None, :]) % LANES) / LANES)
    coarse = phases(own_rows, counting(parts * tiles) * LANES, nfft)
    fine = phases(own_rows, counting(LANES), nfft)
    back = complex_mul((coarse[0].T[:, :, None], coarse[1].T[:, :, None]), (fine[0][None], fine[1][None]))
    back = jnp.stack(back)
    lead = place == 0
    keep = jnp.broadcast_to((lead & ((pos == 0) | (pos == half)))[:, None], (block, LANES))
    plain = jnp.broadcast_to((lead & (pos == 0))[:, None], (block, LANES))
    flags = jnp.stack([keep, plain]).astype(jnp.float32)
    vmem = pl.BlockSpec(memory_space=pltpu.VMEM)
    return pl.pallas_call(
        column_kernel,
        out_shape=jax.ShapeDtypeStruct(received.shape, jnp.float32),
        in_specs=[vmem] * 7,
        out_specs=vmem,
    )(received, phi, tw1, tw2, back, flags, dft)


def prologue_kernel(nbin, base_ref, d_ref, c_ref, r_ref, o_ref):
    parts, _, cols = o_ref.shape
    scen_dev = d_ref.shape[0]
    lines = d_ref.shape[1]
    tiles = cols // LANES
    rows = (o_ref.shape[1] - 8) // (2 * scen_dev)
    per_row = lines // rows
    arrays = 2 * scen_dev
    base = base_ref[0]
    line = lax.broadcasted_iota(jnp.int32, (lines, LANES), 0)
    lane = lax.broadcasted_iota(jnp.int32, (lines, LANES), 1)
    mass = ((base + line * LANES + lane).astype(jnp.float32) + 0.5) / nbin
    sums = []
    flux_last = []
    for sc in range(scen_dev):
        weighted = mass * d_ref[sc]
        sums.append((jnp.sum(weighted), sc))
        sums.append((jnp.sum(c_ref[sc] * weighted), scen_dev + sc))
        flux_last.append(r_ref[lines - 1:lines, LANES - 1:LANES] * weighted[lines - 1:lines, LANES - 1:LANES])
        flux_last.append(c_ref[sc, 0:1, 0:1])
    t_row = lax.broadcasted_iota(jnp.int32, (8, cols), 0)
    t_lane = lax.broadcasted_iota(jnp.int32, (8, cols), 1)
    tile = jnp.zeros((8, cols), jnp.float32)
    for value, slot in sums:
        tile = jnp.where((t_row == 0) & (t_lane == slot), value, tile)
    for sc in range(scen_dev):
        tile = jnp.where((t_row == 1) & (t_lane == sc), flux_last[2 * sc], tile)
        tile = jnp.where((t_row == 1) & (t_lane == scen_dev + sc), flux_last[2 * sc + 1], tile)
    s_line = lax.broadcasted_iota(jnp.int32, (rows, LANES), 0)
    s_lane = lax.broadcasted_iota(jnp.int32, (rows, LANES), 1)
    for j in range(parts):
        for t in range(tiles):
            first_line = j * tiles + t
            picked = s_line * per_row + first_line
            part_mass = ((base + picked * LANES + s_lane).astype(jnp.float32) + 0.5) / nbin
            for sc in range(scen_dev):
                dens = d_ref[sc, pl.ds(first_line, rows, stride=per_row), :]
                cot = c_ref[sc, pl.ds(first_line, rows, stride=per_row), :]
                o_ref[j, sc * rows:(sc + 1) * rows, t * LANES:(t + 1) * LANES] = part_mass * dens
                o_ref[j, (scen_dev + sc) * rows:(scen_dev + sc + 1) * rows, t * LANES:(t + 1) * LANES] = cot
        o_ref[j, arrays * rows:arrays * rows + 8, :] = tile


def prologue(density, cotangent, rate, offset, nbin, parts, rows, cols):
    scen_dev, bin_dev = density.shape
    lines = bin_dev // LANES
    base = jnp.reshape(offset, (1,)).astype(jnp.int32)
    vmem = pl.BlockSpec(memory_space=pltpu.VMEM)
    return pl.pallas_call(
        functools.partial(prologue_kernel, nbin),
        out_shape=jax.ShapeDtypeStruct((parts, 2 * scen_dev * rows + 8, cols), jnp.float32),
        in_specs=[pl.BlockSpec(memory_space=pltpu.SMEM), vmem, vmem, vmem],
        out_specs=vmem,
    )(base, density.reshape(scen_dev, lines, LANES), cotangent.reshape(scen_dev, lines, LANES),
      rate.reshape(lines, LANES))


def exchange(value):
    return lax.all_to_all(value, "mass", 0, 0, tiled=True)


def shards(density, cotangent, rate):
    high = lax.Precision.HIGHEST
    scen_dev, bin_dev = density.shape
    arrays = 2 * scen_dev
    parts = lax.axis_size("mass")
    place = lax.axis_index("mass")
    width = C1 * C2
    rows = bin_dev // width
    half_rows = rows * parts
    full_rows = 2 * half_rows
    cols = width // parts
    block = full_rows // parts
    nbin = half_rows * width
    nfft = 2 * nbin
    beta = aggregation_coef / nbin
    offset = place * bin_dev
    mass = ((offset + counting(bin_dev)).astype(jnp.float32) + 0.5) / nbin
    weighted = mass[None, :] * density
    flux = rate[None, :] * weighted
    outgoing = prologue(density, cotangent, rate, offset, nbin, parts, rows, cols)
    incoming_rows = exchange(outgoing)
    moments = jnp.sum(incoming_rows[:, arrays * rows, :arrays], axis=0)
    first, cross = moments[:scen_dev], moments[scen_dev:]
    neighbours = incoming_rows[:, arrays * rows + 1, :arrays]
    behind = lax.dynamic_index_in_dim(neighbours, (place + parts - 1) % parts, keepdims=False)
    ahead = lax.dynamic_index_in_dim(neighbours, (place + 1) % parts, keepdims=False)
    incoming = jnp.where(place > 0, behind[:scen_dev], 0.0)[:, None]
    arriving = jnp.where(place < parts - 1, ahead[scen_dev:], 0.0)[:, None]
    spread = incoming_rows[:, : arrays * rows].reshape(parts, arrays, rows, cols)
    spread = spread.transpose(1, 0, 2, 3).reshape(arrays, half_rows, cols)
    half = block // 2
    pos = counting(block)
    own_rows = jnp.where(pos < half, half * place + pos, (full_rows - half * place - (pos - half)) % full_rows)
    own_rows = jnp.where((place == 0) & (pos == half), full_rows // 2, own_rows)
    table = np.arange(block)[None, :]
    order = np.where(table < half, half * np.arange(parts)[:, None] + table,
                     (full_rows - half * np.arange(parts)[:, None] - (table - half)) % full_rows)
    order[0, half] = full_rows // 2
    order_np = order.reshape(-1)
    order = jnp.asarray(order_np, jnp.int32)
    row_angle = 2.0 * np.pi * ((order_np[:, None] * np.arange(half_rows)[None, :]) % full_rows) / full_rows
    row_cos, row_sin = jnp.asarray(np.cos(row_angle), jnp.float32), jnp.asarray(np.sin(row_angle), jnp.float32)
    forward_rows = jnp.stack([jnp.stack([row_cos, row_sin], axis=1), jnp.stack([-row_sin, row_cos], axis=1)])
    packed = spread.reshape(2, scen_dev, half_rows, cols)
    freq = jnp.einsum("okir,isrw->oskw", forward_rows, packed, precision=high)
    tiles = cols // LANES
    coarse_cos, coarse_sin = phases(order, place * cols + counting(tiles) * LANES, nfft)
    fine_angle = 2.0 * np.pi * ((order_np[:, None] * np.arange(LANES)[None, :]) % nfft) / nfft
    fine_cos = jnp.asarray(np.cos(fine_angle), jnp.float32)[:, None, :]
    fine_sin = jnp.asarray(np.sin(fine_angle), jnp.float32)[:, None, :]
    tw_cos, tw_sin = complex_mul((coarse_cos[:, :, None], coarse_sin[:, :, None]), (fine_cos, fine_sin))
    tw_cos, tw_sin = tw_cos.reshape(full_rows, cols), tw_sin.reshape(full_rows, cols)
    twisted = jnp.stack(complex_mul((freq[0], freq[1]), (tw_cos, -tw_sin)))
    twisted = twisted.reshape(2, scen_dev, parts, block, cols).transpose(2, 0, 1, 3, 4)
    following = jnp.concatenate([cotangent[:, 1:], arriving], axis=1)
    local_grad = jnp.sum(weighted * (following - cotangent), axis=0)
    received, local_grad = lax.optimization_barrier((exchange(twisted), local_grad))
    rate_gradient = local_grad
    groups = lax.axis_size("scen")
    if groups & (groups - 1) == 0:
        step = 1
        while step < groups:
            pairs = [(source, source ^ step) for source in range(groups)]
            rate_gradient = rate_gradient + lax.ppermute(rate_gradient, "scen", pairs)
            step *= 2
    else:
        rate_gradient = lax.psum(local_grad, "scen")
    untwisted = column_stage(received, own_rows, place, nfft)
    returned = exchange(untwisted).transpose(1, 2, 0, 3, 4).reshape(2, scen_dev, full_rows, cols)
    inv_cos, inv_sin = row_cos.T, row_sin.T
    inverse_rows = jnp.stack([jnp.stack([inv_cos, -inv_sin], axis=1), jnp.stack([inv_sin, inv_cos], axis=1)])
    real_part = jnp.einsum("orik,iskw->osrw", inverse_rows, returned, precision=high)
    real_part = real_part.reshape(arrays, half_rows, cols)
    real_part = real_part.reshape(arrays, parts, rows, cols).transpose(1, 0, 2, 3)
    gathered = exchange(real_part).transpose(1, 2, 0, 3).reshape(arrays, bin_dev) / nfft
    birth = gathered[:scen_dev]
    corr = gathered[scen_dev:]
    inflow = jnp.concatenate([incoming, flux[:, :-1]], axis=1)
    tendency = 0.5 * beta * birth - beta * first[:, None] * weighted - flux + inflow
    adjoint = mass[None, :] * (
        beta * corr
        - beta * first[:, None] * cotangent
        - beta * cross[:, None]
        - rate[None, :] * cotangent
        + rate[None, :] * following
    )
    return (tendency, adjoint, rate_gradient)


def solution(mesh):
    in_specs = (P("scen", "mass"), P("scen", "mass"), P("mass"))
    out_specs = (P("scen", "mass"), P("scen", "mass"), P("mass"))
    return jax.shard_map(shards, mesh=mesh, in_specs=in_specs, out_specs=out_specs, check_vma=False)
```

```python
import functools
import math

import jax
import numpy as np
import jax.numpy as jnp
from jax import lax
from jax.experimental import pallas as pl
from jax.experimental.pallas import tpu as pltpu
from jax.sharding import PartitionSpec as P

C1 = 32
C2 = 128


aggregation_coef = 12.0


def from_behind(value, axis, steps):
    count = lax.axis_size(axis)
    first, last = (max(0, -steps), min(count, count - steps))
    return lax.ppermute(value, axis, [(source, source + steps) for source in range(first, last)])


def phases(left, right, total):
    outer = left[:, None] * right[None, :] % total
    angle = outer.astype(jnp.float32) * (2.0 * math.pi / total)
    return (jnp.cos(angle), jnp.sin(angle))


def counting(count):
    return lax.iota(jnp.int32, count)


def complex_dot(form, table, values):
    table_re, table_im = table
    val_re, val_im = values
    high = lax.Precision.HIGHEST
    real_out = jnp.einsum(form, table_re, val_re, precision=high) - jnp.einsum(
        form, table_im, val_im, precision=high
    )
    imag_out = jnp.einsum(form, table_re, val_im, precision=high) + jnp.einsum(
        form, table_im, val_re, precision=high
    )
    return (real_out, imag_out)


def complex_mul(left, right):
    return (left[0] * right[0] - left[1] * right[1], left[0] * right[1] + left[1] * right[0])


def column_forward(values):
    lead = values[0].shape[:-1]
    shaped = (values[0].reshape(lead + (C1, C2)), values[1].reshape(lead + (C1, C2)))
    cos_one, sin_one = phases(counting(C1), counting(C1), C1)
    step_one = complex_dot("pa,...ab->...pb", (cos_one, -sin_one), shaped)
    tw_cos, tw_sin = phases(counting(C1), counting(C2), C1 * C2)
    turned = complex_mul(step_one, (tw_cos, -tw_sin))
    cos_two, sin_two = phases(counting(C2), counting(C2), C2)
    return complex_dot("qb,...pb->...pq", (cos_two, -sin_two), turned)


def column_inverse(values):
    lead = values[0].shape[:-2]
    cos_two, sin_two = phases(counting(C2), counting(C2), C2)
    step_one = complex_dot("qb,...pq->...pb", (cos_two, sin_two), values)
    tw_cos, tw_sin = phases(counting(C1), counting(C2), C1 * C2)
    turned = complex_mul(step_one, (tw_cos, tw_sin))
    cos_one, sin_one = phases(counting(C1), counting(C1), C1)
    result = complex_dot("pa,...pb->...ab", (cos_one, sin_one), turned)
    return (result[0].reshape(lead + (C1 * C2,)), result[1].reshape(lead + (C1 * C2,)))


LANES = 128


def butterfly(values, sign):
    count = len(values)
    if count == 1:
        return list(values)
    even = butterfly(values[0::2], sign)
    odd = butterfly(values[1::2], sign)
    out = [None] * count
    for k in range(count // 2):
        o_re, o_im = odd[k]
        if k == 0:
            t = (o_re, o_im)
        elif 4 * k == count:
            t = (-sign * o_im, sign * o_re)
        else:
            c = math.cos(2.0 * math.pi * k / count)
            s = sign * math.sin(2.0 * math.pi * k / count)
            t = (o_re * c - o_im * s, o_re * s + o_im * c)
        e_re, e_im = even[k]
        out[k] = (e_re + t[0], e_im + t[1])
        out[k + count // 2] = (e_re - t[0], e_im - t[1])
    return out


def column_kernel(x_ref, phi_ref, tw1_ref, tw2_ref, back_ref, flag_ref, dft_ref, o_ref):
    parts, _, scen_dev, block, cols = x_ref.shape
    tiles = cols // LANES
    half = block // 2
    high = lax.Precision.HIGH
    keep = flag_ref[0] > 0.5
    plain = flag_ref[1] > 0.5
    dft_cos = dft_ref[0]
    dft_sin = dft_ref[1]

    def cmul(a, b):
        return (a[0] * b[0] - a[1] * b[1], a[0] * b[1] + a[1] * b[0])

    def transform(grid, sign):
        stage = [butterfly([grid[src][t] for src in range(parts)], sign) for t in range(tiles)]
        turned = []
        for k1 in range(parts):
            row = []
            for t in range(tiles):
                w = (tw1_ref[0, k1 * tiles + t], sign * tw1_ref[1, k1 * tiles + t])
                row.append(cmul(stage[t][k1], w))
            mixed = butterfly(row, sign)
            turned.append([cmul(mixed[m1], (tw2_ref[0, m1], sign * tw2_ref[1, m1])) for m1 in range(tiles)])
        flat_re = jnp.concatenate([turned[k][m][0] for k in range(parts) for m in range(tiles)], axis=0)
        flat_im = jnp.concatenate([turned[k][m][1] for k in range(parts) for m in range(tiles)], axis=0)
        dot = lambda a, b: jnp.dot(a, b, precision=high, preferred_element_type=jnp.float32)
        out_re = dot(flat_re, dft_cos) - sign * dot(flat_im, dft_sin)
        out_im = dot(flat_im, dft_cos) + sign * dot(flat_re, dft_sin)
        return out_re, out_im

    def inverse(flat, sign):
        dot = lambda a, b: jnp.dot(a, b, precision=high, preferred_element_type=jnp.float32)
        f_re, f_im = flat
        b_re = dot(f_re, dft_cos) - sign * dot(f_im, dft_sin)
        b_im = dot(f_im, dft_cos) + sign * dot(f_re, dft_sin)
        piece = lambda a, k, m: a[(k * tiles + m) * block:(k * tiles + m + 1) * block]
        stage = []
        for k1 in range(parts):
            row = [cmul((piece(b_re, k1, m), piece(b_im, k1, m)), (tw2_ref[0, m], sign * tw2_ref[1, m]))
                   for m in range(tiles)]
            mixed = butterfly(row, sign)
            stage.append([cmul(mixed[t], (tw1_ref[0, k1 * tiles + t], sign * tw1_ref[1, k1 * tiles + t]))
                          for t in range(tiles)])
        grid = [butterfly([stage[k1][t] for k1 in range(parts)], sign) for t in range(tiles)]
        return grid

    for sc in range(scen_dev):
        w_grid, c_grid = [], []
        for src in range(parts):
            w_row, c_row = [], []
            for t in range(tiles):
                lanes = slice(t * LANES, (t + 1) * LANES)
                t_re = x_ref[src, 0, sc, :, lanes]
                t_im = x_ref[src, 1, sc, :, lanes]
                swap_re = jnp.concatenate([t_re[half:], t_re[:half]], axis=0)
                swap_im = jnp.concatenate([t_im[half:], t_im[:half]], axis=0)
                p_re = jnp.where(keep, t_re, swap_re)
                p_im = jnp.where(keep, t_im, swap_im)
                f_re = jnp.where(plain, 1.0, phi_ref[0, src * tiles + t])
                f_im = jnp.where(plain, 0.0, -phi_ref[1, src * tiles + t])
                u_re = p_re * f_re + p_im * f_im
                u_im = p_re * f_im - p_im * f_re
                w_row.append((0.5 * (t_re + u_re), 0.5 * (t_im + u_im)))
                c_row.append((0.5 * (t_im - u_im), 0.5 * (u_re - t_re)))
            w_grid.append(w_row)
            c_grid.append(c_row)
        dist = transform(w_grid, -1.0)
        cot = transform(c_grid, -1.0)
        birth = cmul(dist, dist)
        adjoint = cmul(cot, (dist[0], -dist[1]))
        joined = (birth[0] - adjoint[1], birth[1] + adjoint[0])
        grid = inverse(joined, 1.0)
        for src in range(parts):
            for t in range(tiles):
                lanes = slice(t * LANES, (t + 1) * LANES)
                value = cmul(grid[t][src], (back_ref[0, src * tiles + t], back_ref[1, src * tiles + t]))
                o_ref[src, 0, sc, :, lanes] = value[0]
                o_ref[src, 1, sc, :, lanes] = value[1]


def column_stage(received, own_rows, place, nfft):
    parts, _, scen_dev, block, cols = received.shape
    tiles = cols // LANES
    width = parts * cols
    half = block // 2
    pos = counting(block)

    def table(angle):
        return jnp.asarray(np.stack([np.cos(angle), np.sin(angle)]), jnp.float32)

    lane = np.arange(LANES)
    chunk = np.arange(parts * tiles)
    spots = chunk[:, None] * LANES + lane[None, :]
    phi = table(2.0 * np.pi * spots / width).reshape(2, parts * tiles, 1, LANES)
    tw1 = table(2.0 * np.pi * (((chunk % tiles) * LANES)[:, None] + lane[None, :]) * (chunk // tiles)[:, None] / width)
    tw1 = tw1.reshape(2, parts * tiles, 1, LANES)
    tw2 = table(2.0 * np.pi * np.arange(tiles)[:, None] * lane[None, :] / cols).reshape(2, tiles, 1, LANES)
    dft = table(2.0 * np.pi * ((lane[:, None] * lane[None, :]) % LANES) / LANES)
    coarse = phases(own_rows, counting(parts * tiles) * LANES, nfft)
    fine = phases(own_rows, counting(LANES), nfft)
    back = complex_mul((coarse[0].T[:, :, None], coarse[1].T[:, :, None]), (fine[0][None], fine[1][None]))
    back = jnp.stack(back)
    lead = place == 0
    keep = jnp.broadcast_to((lead & ((pos == 0) | (pos == half)))[:, None], (block, LANES))
    plain = jnp.broadcast_to((lead & (pos == 0))[:, None], (block, LANES))
    flags = jnp.stack([keep, plain]).astype(jnp.float32)
    vmem = pl.BlockSpec(memory_space=pltpu.VMEM)
    return pl.pallas_call(
        column_kernel,
        out_shape=jax.ShapeDtypeStruct(received.shape, jnp.float32),
        in_specs=[vmem] * 7,
        out_specs=vmem,
    )(received, phi, tw1, tw2, back, flags, dft)


def prologue_kernel(nbin, base_ref, d_ref, c_ref, r_ref, o_ref):
    parts, _, cols = o_ref.shape
    scen_dev = d_ref.shape[0]
    lines = d_ref.shape[1]
    tiles = cols // LANES
    rows = (o_ref.shape[1] - 8) // (2 * scen_dev)
    per_row = lines // rows
    arrays = 2 * scen_dev
    base = base_ref[0]
    line = lax.broadcasted_iota(jnp.int32, (lines, LANES), 0)
    lane = lax.broadcasted_iota(jnp.int32, (lines, LANES), 1)
    mass = ((base + line * LANES + lane).astype(jnp.float32) + 0.5) / nbin
    sums = []
    flux_last = []
    for sc in range(scen_dev):
        weighted = mass * d_ref[sc]
        sums.append((jnp.sum(weighted), sc))
        sums.append((jnp.sum(c_ref[sc] * weighted), scen_dev + sc))
        flux_last.append(r_ref[lines - 1:lines, LANES - 1:LANES] * weighted[lines - 1:lines, LANES - 1:LANES])
        flux_last.append(c_ref[sc, 0:1, 0:1])
    t_row = lax.broadcasted_iota(jnp.int32, (8, cols), 0)
    t_lane = lax.broadcasted_iota(jnp.int32, (8, cols), 1)
    tile = jnp.zeros((8, cols), jnp.float32)
    for value, slot in sums:
        tile = jnp.where((t_row == 0) & (t_lane == slot), value, tile)
    for sc in range(scen_dev):
        tile = jnp.where((t_row == 1) & (t_lane == sc), flux_last[2 * sc], tile)
        tile = jnp.where((t_row == 1) & (t_lane == scen_dev + sc), flux_last[2 * sc + 1], tile)
    s_line = lax.broadcasted_iota(jnp.int32, (rows, LANES), 0)
    s_lane = lax.broadcasted_iota(jnp.int32, (rows, LANES), 1)
    for j in range(parts):
        for t in range(tiles):
            first_line = j * tiles + t
            picked = s_line * per_row + first_line
            part_mass = ((base + picked * LANES + s_lane).astype(jnp.float32) + 0.5) / nbin
            for sc in range(scen_dev):
                dens = d_ref[sc, pl.ds(first_line, rows, stride=per_row), :]
                cot = c_ref[sc, pl.ds(first_line, rows, stride=per_row), :]
                o_ref[j, sc * rows:(sc + 1) * rows, t * LANES:(t + 1) * LANES] = part_mass * dens
                o_ref[j, (scen_dev + sc) * rows:(scen_dev + sc + 1) * rows, t * LANES:(t + 1) * LANES] = cot
        o_ref[j, arrays * rows:arrays * rows + 8, :] = tile


def prologue(density, cotangent, rate, offset, nbin, parts, rows, cols):
    scen_dev, bin_dev = density.shape
    lines = bin_dev // LANES
    base = jnp.reshape(offset, (1,)).astype(jnp.int32)
    vmem = pl.BlockSpec(memory_space=pltpu.VMEM)
    return pl.pallas_call(
        functools.partial(prologue_kernel, nbin),
        out_shape=jax.ShapeDtypeStruct((parts, 2 * scen_dev * rows + 8, cols), jnp.float32),
        in_specs=[pl.BlockSpec(memory_space=pltpu.SMEM), vmem, vmem, vmem],
        out_specs=vmem,
    )(base, density.reshape(scen_dev, lines, LANES), cotangent.reshape(scen_dev, lines, LANES),
      rate.reshape(lines, LANES))


def exchange(value):
    return lax.all_to_all(value, "mass", 0, 0, tiled=True)


def shards(density, cotangent, rate):
    high = lax.Precision.HIGHEST
    scen_dev, bin_dev = density.shape
    arrays = 2 * scen_dev
    parts = lax.axis_size("mass")
    place = lax.axis_index("mass")
    width = C1 * C2
    rows = bin_dev // width
    half_rows = rows * parts
    full_rows = 2 * half_rows
    cols = width // parts
    block = full_rows // parts
    nbin = half_rows * width
    nfft = 2 * nbin
    beta = aggregation_coef / nbin
    offset = place * bin_dev
    mass = ((offset + counting(bin_dev)).astype(jnp.float32) + 0.5) / nbin
    weighted = mass[None, :] * density
    flux = rate[None, :] * weighted
    outgoing = prologue(density, cotangent, rate, offset, nbin, parts, rows, cols)
    incoming_rows = exchange(outgoing)
    moments = jnp.sum(incoming_rows[:, arrays * rows, :arrays], axis=0)
    first, cross = moments[:scen_dev], moments[scen_dev:]
    neighbours = incoming_rows[:, arrays * rows + 1, :arrays]
    behind = lax.dynamic_index_in_dim(neighbours, (place + parts - 1) % parts, keepdims=False)
    ahead = lax.dynamic_index_in_dim(neighbours, (place + 1) % parts, keepdims=False)
    incoming = jnp.where(place > 0, behind[:scen_dev], 0.0)[:, None]
    arriving = jnp.where(place < parts - 1, ahead[scen_dev:], 0.0)[:, None]
    spread = incoming_rows[:, : arrays * rows].reshape(parts, arrays, rows, cols)
    spread = spread.transpose(1, 0, 2, 3).reshape(arrays, half_rows, cols)
    half = block // 2
    pos = counting(block)
    own_rows = jnp.where(pos < half, half * place + pos, (full_rows - half * place - (pos - half)) % full_rows)
    own_rows = jnp.where((place == 0) & (pos == half), full_rows // 2, own_rows)
    table = np.arange(block)[None, :]
    order = np.where(table < half, half * np.arange(parts)[:, None] + table,
                     (full_rows - half * np.arange(parts)[:, None] - (table - half)) % full_rows)
    order[0, half] = full_rows // 2
    order_np = order.reshape(-1)
    order = jnp.asarray(order_np, jnp.int32)
    row_angle = 2.0 * np.pi * ((order_np[:, None] * np.arange(half_rows)[None, :]) % full_rows) / full_rows
    row_cos, row_sin = jnp.asarray(np.cos(row_angle), jnp.float32), jnp.asarray(np.sin(row_angle), jnp.float32)
    forward_rows = jnp.stack([jnp.stack([row_cos, row_sin], axis=1), jnp.stack([-row_sin, row_cos], axis=1)])
    packed = spread.reshape(2, scen_dev, half_rows, cols)
    freq = jnp.einsum("okir,isrw->oskw", forward_rows, packed, precision=lax.Precision.HIGH)
    tiles = cols // LANES
    coarse_cos, coarse_sin = phases(order, place * cols + counting(tiles) * LANES, nfft)
    fine_angle = 2.0 * np.pi * ((order_np[:, None] * np.arange(LANES)[None, :]) % nfft) / nfft
    fine_cos = jnp.asarray(np.cos(fine_angle), jnp.float32)[:, None, :]
    fine_sin = jnp.asarray(np.sin(fine_angle), jnp.float32)[:, None, :]
    tw_cos, tw_sin = complex_mul((coarse_cos[:, :, None], coarse_sin[:, :, None]), (fine_cos, fine_sin))
    tw_cos, tw_sin = tw_cos.reshape(full_rows, cols), tw_sin.reshape(full_rows, cols)
    twisted = jnp.stack(complex_mul((freq[0], freq[1]), (tw_cos, -tw_sin)))
    twisted = twisted.reshape(2, scen_dev, parts, block, cols).transpose(2, 0, 1, 3, 4)
    following = jnp.concatenate([cotangent[:, 1:], arriving], axis=1)
    local_grad = jnp.sum(weighted * (following - cotangent), axis=0)
    received, local_grad = lax.optimization_barrier((exchange(twisted), local_grad))
    rate_gradient = local_grad
    groups = lax.axis_size("scen")
    if groups & (groups - 1) == 0:
        step = 1
        while step < groups:
            pairs = [(source, source ^ step) for source in range(groups)]
            rate_gradient = rate_gradient + lax.ppermute(rate_gradient, "scen", pairs)
            step *= 2
    else:
        rate_gradient = lax.psum(local_grad, "scen")
    untwisted = column_stage(received, own_rows, place, nfft)
    returned = exchange(untwisted).transpose(1, 2, 0, 3, 4).reshape(2, scen_dev, full_rows, cols)
    inv_cos, inv_sin = row_cos.T, row_sin.T
    inverse_rows = jnp.stack([jnp.stack([inv_cos, -inv_sin], axis=1), jnp.stack([inv_sin, inv_cos], axis=1)])
    real_part = jnp.einsum("orik,iskw->osrw", inverse_rows, returned, precision=lax.Precision.HIGH)
    real_part = real_part.reshape(arrays, half_rows, cols)
    real_part = real_part.reshape(arrays, parts, rows, cols).transpose(1, 0, 2, 3)
    gathered = exchange(real_part).transpose(1, 2, 0, 3).reshape(arrays, bin_dev) / nfft
    birth = gathered[:scen_dev]
    corr = gathered[scen_dev:]
    inflow = jnp.concatenate([incoming, flux[:, :-1]], axis=1)
    tendency = 0.5 * beta * birth - beta * first[:, None] * weighted - flux + inflow
    adjoint = mass[None, :] * (
        beta * corr
        - beta * first[:, None] * cotangent
        - beta * cross[:, None]
        - rate[None, :] * cotangent
        + rate[None, :] * following
    )
    return (tendency, adjoint, rate_gradient)


def solution(mesh):
    in_specs = (P("scen", "mass"), P("scen", "mass"), P("mass"))
    out_specs = (P("scen", "mass"), P("scen", "mass"), P("mass"))
    return jax.shard_map(shards, mesh=mesh, in_specs=in_specs, out_specs=out_specs, check_vma=False)
```

```python
import functools
import math

import jax
import numpy as np
import jax.numpy as jnp
from jax import lax
from jax.experimental import pallas as pl
from jax.experimental.pallas import tpu as pltpu
from jax.sharding import PartitionSpec as P

C1 = 32
C2 = 128


aggregation_coef = 12.0


def from_behind(value, axis, steps):
    count = lax.axis_size(axis)
    first, last = (max(0, -steps), min(count, count - steps))
    return lax.ppermute(value, axis, [(source, source + steps) for source in range(first, last)])


def phases(left, right, total):
    outer = left[:, None] * right[None, :] % total
    angle = outer.astype(jnp.float32) * (2.0 * math.pi / total)
    return (jnp.cos(angle), jnp.sin(angle))


def counting(count):
    return lax.iota(jnp.int32, count)


def complex_dot(form, table, values):
    table_re, table_im = table
    val_re, val_im = values
    high = lax.Precision.HIGHEST
    real_out = jnp.einsum(form, table_re, val_re, precision=high) - jnp.einsum(
        form, table_im, val_im, precision=high
    )
    imag_out = jnp.einsum(form, table_re, val_im, precision=high) + jnp.einsum(
        form, table_im, val_re, precision=high
    )
    return (real_out, imag_out)


def complex_mul(left, right):
    return (left[0] * right[0] - left[1] * right[1], left[0] * right[1] + left[1] * right[0])


def column_forward(values):
    lead = values[0].shape[:-1]
    shaped = (values[0].reshape(lead + (C1, C2)), values[1].reshape(lead + (C1, C2)))
    cos_one, sin_one = phases(counting(C1), counting(C1), C1)
    step_one = complex_dot("pa,...ab->...pb", (cos_one, -sin_one), shaped)
    tw_cos, tw_sin = phases(counting(C1), counting(C2), C1 * C2)
    turned = complex_mul(step_one, (tw_cos, -tw_sin))
    cos_two, sin_two = phases(counting(C2), counting(C2), C2)
    return complex_dot("qb,...pb->...pq", (cos_two, -sin_two), turned)


def column_inverse(values):
    lead = values[0].shape[:-2]
    cos_two, sin_two = phases(counting(C2), counting(C2), C2)
    step_one = complex_dot("qb,...pq->...pb", (cos_two, sin_two), values)
    tw_cos, tw_sin = phases(counting(C1), counting(C2), C1 * C2)
    turned = complex_mul(step_one, (tw_cos, tw_sin))
    cos_one, sin_one = phases(counting(C1), counting(C1), C1)
    result = complex_dot("pa,...pb->...ab", (cos_one, sin_one), turned)
    return (result[0].reshape(lead + (C1 * C2,)), result[1].reshape(lead + (C1 * C2,)))


LANES = 128


def butterfly(values, sign):
    count = len(values)
    if count == 1:
        return list(values)
    even = butterfly(values[0::2], sign)
    odd = butterfly(values[1::2], sign)
    out = [None] * count
    for k in range(count // 2):
        o_re, o_im = odd[k]
        if k == 0:
            t = (o_re, o_im)
        elif 4 * k == count:
            t = (-sign * o_im, sign * o_re)
        else:
            c = math.cos(2.0 * math.pi * k / count)
            s = sign * math.sin(2.0 * math.pi * k / count)
            t = (o_re * c - o_im * s, o_re * s + o_im * c)
        e_re, e_im = even[k]
        out[k] = (e_re + t[0], e_im + t[1])
        out[k + count // 2] = (e_re - t[0], e_im - t[1])
    return out


def column_kernel(x_ref, phi_ref, tw1_ref, tw2_ref, back_ref, flag_ref, dft_ref, o_ref):
    parts, _, scen_dev, block, cols = x_ref.shape
    tiles = cols // LANES
    half = block // 2
    high = lax.Precision.HIGH
    keep = flag_ref[0] > 0.5
    plain = flag_ref[1] > 0.5
    dft_cos = dft_ref[0]
    dft_sin = dft_ref[1]

    def cmul(a, b):
        return (a[0] * b[0] - a[1] * b[1], a[0] * b[1] + a[1] * b[0])

    def transform(grid, sign):
        stage = [butterfly([grid[src][t] for src in range(parts)], sign) for t in range(tiles)]
        turned = []
        for k1 in range(parts):
            row = []
            for t in range(tiles):
                w = (tw1_ref[0, k1 * tiles + t], sign * tw1_ref[1, k1 * tiles + t])
                row.append(cmul(stage[t][k1], w))
            mixed = butterfly(row, sign)
            turned.append([cmul(mixed[m1], (tw2_ref[0, m1], sign * tw2_ref[1, m1])) for m1 in range(tiles)])
        flat_re = jnp.concatenate([turned[k][m][0] for k in range(parts) for m in range(tiles)], axis=0)
        flat_im = jnp.concatenate([turned[k][m][1] for k in range(parts) for m in range(tiles)], axis=0)
        dot = lambda a, b: jnp.dot(a, b, precision=high, preferred_element_type=jnp.float32)
        out_re = dot(flat_re, dft_cos) - sign * dot(flat_im, dft_sin)
        out_im = dot(flat_im, dft_cos) + sign * dot(flat_re, dft_sin)
        return out_re, out_im

    def inverse(flat, sign):
        dot = lambda a, b: jnp.dot(a, b, precision=high, preferred_element_type=jnp.float32)
        f_re, f_im = flat
        b_re = dot(f_re, dft_cos) - sign * dot(f_im, dft_sin)
        b_im = dot(f_im, dft_cos) + sign * dot(f_re, dft_sin)
        piece = lambda a, k, m: a[(k * tiles + m) * block:(k * tiles + m + 1) * block]
        stage = []
        for k1 in range(parts):
            row = [cmul((piece(b_re, k1, m), piece(b_im, k1, m)), (tw2_ref[0, m], sign * tw2_ref[1, m]))
                   for m in range(tiles)]
            mixed = butterfly(row, sign)
            stage.append([cmul(mixed[t], (tw1_ref[0, k1 * tiles + t], sign * tw1_ref[1, k1 * tiles + t]))
                          for t in range(tiles)])
        grid = [butterfly([stage[k1][t] for k1 in range(parts)], sign) for t in range(tiles)]
        return grid

    for sc in range(scen_dev):
        w_grid, c_grid = [], []
        for src in range(parts):
            w_row, c_row = [], []
            for t in range(tiles):
                lanes = slice(t * LANES, (t + 1) * LANES)
                t_re = x_ref[src, 0, sc, :, lanes]
                t_im = x_ref[src, 1, sc, :, lanes]
                swap_re = jnp.concatenate([t_re[half:], t_re[:half]], axis=0)
                swap_im = jnp.concatenate([t_im[half:], t_im[:half]], axis=0)
                p_re = jnp.where(keep, t_re, swap_re)
                p_im = jnp.where(keep, t_im, swap_im)
                f_re = jnp.where(plain, 1.0, phi_ref[0, src * tiles + t])
                f_im = jnp.where(plain, 0.0, -phi_ref[1, src * tiles + t])
                u_re = p_re * f_re + p_im * f_im
                u_im = p_re * f_im - p_im * f_re
                w_row.append((0.5 * (t_re + u_re), 0.5 * (t_im + u_im)))
                c_row.append((0.5 * (t_im - u_im), 0.5 * (u_re - t_re)))
            w_grid.append(w_row)
            c_grid.append(c_row)
        dist = transform(w_grid, -1.0)
        cot = transform(c_grid, -1.0)
        birth = cmul(dist, dist)
        adjoint = cmul(cot, (dist[0], -dist[1]))
        joined = (birth[0] - adjoint[1], birth[1] + adjoint[0])
        grid = inverse(joined, 1.0)
        for src in range(parts):
            for t in range(tiles):
                lanes = slice(t * LANES, (t + 1) * LANES)
                value = cmul(grid[t][src], (back_ref[0, src * tiles + t], back_ref[1, src * tiles + t]))
                o_ref[src, 0, sc, :, lanes] = value[0]
                o_ref[src, 1, sc, :, lanes] = value[1]


def column_stage(received, own_rows, place, nfft):
    parts, _, scen_dev, block, cols = received.shape
    tiles = cols // LANES
    width = parts * cols
    half = block // 2
    pos = counting(block)

    def table(angle):
        return jnp.asarray(np.stack([np.cos(angle), np.sin(angle)]), jnp.float32)

    lane = np.arange(LANES)
    chunk = np.arange(parts * tiles)
    spots = chunk[:, None] * LANES + lane[None, :]
    phi = table(2.0 * np.pi * spots / width).reshape(2, parts * tiles, 1, LANES)
    tw1 = table(2.0 * np.pi * (((chunk % tiles) * LANES)[:, None] + lane[None, :]) * (chunk // tiles)[:, None] / width)
    tw1 = tw1.reshape(2, parts * tiles, 1, LANES)
    tw2 = table(2.0 * np.pi * np.arange(tiles)[:, None] * lane[None, :] / cols).reshape(2, tiles, 1, LANES)
    dft = table(2.0 * np.pi * ((lane[:, None] * lane[None, :]) % LANES) / LANES)
    coarse = phases(own_rows, counting(parts * tiles) * LANES, nfft)
    fine = phases(own_rows, counting(LANES), nfft)
    back = complex_mul((coarse[0].T[:, :, None], coarse[1].T[:, :, None]), (fine[0][None], fine[1][None]))
    back = jnp.stack(back)
    lead = place == 0
    keep = jnp.broadcast_to((lead & ((pos == 0) | (pos == half)))[:, None], (block, LANES))
    plain = jnp.broadcast_to((lead & (pos == 0))[:, None], (block, LANES))
    flags = jnp.stack([keep, plain]).astype(jnp.float32)
    vmem = pl.BlockSpec(memory_space=pltpu.VMEM)
    return pl.pallas_call(
        column_kernel,
        out_shape=jax.ShapeDtypeStruct(received.shape, jnp.float32),
        in_specs=[vmem] * 7,
        out_specs=vmem,
    )(received, phi, tw1, tw2, back, flags, dft)


def prologue_kernel(nbin, base_ref, d_ref, c_ref, r_ref, o_ref):
    parts, _, cols = o_ref.shape
    scen_dev = d_ref.shape[0]
    lines = d_ref.shape[1]
    tiles = cols // LANES
    rows = (o_ref.shape[1] - 8) // (2 * scen_dev)
    per_row = lines // rows
    arrays = 2 * scen_dev
    base = base_ref[0]
    line = lax.broadcasted_iota(jnp.int32, (lines, LANES), 0)
    lane = lax.broadcasted_iota(jnp.int32, (lines, LANES), 1)
    mass = ((base + line * LANES + lane).astype(jnp.float32) + 0.5) / nbin
    sums = []
    flux_last = []
    for sc in range(scen_dev):
        weighted = mass * d_ref[sc]
        sums.append((jnp.sum(weighted), sc))
        sums.append((jnp.sum(c_ref[sc] * weighted), scen_dev + sc))
        flux_last.append(r_ref[lines - 1:lines, LANES - 1:LANES] * weighted[lines - 1:lines, LANES - 1:LANES])
        flux_last.append(c_ref[sc, 0:1, 0:1])
    t_row = lax.broadcasted_iota(jnp.int32, (8, cols), 0)
    t_lane = lax.broadcasted_iota(jnp.int32, (8, cols), 1)
    tile = jnp.zeros((8, cols), jnp.float32)
    for value, slot in sums:
        tile = jnp.where((t_row == 0) & (t_lane == slot), value, tile)
    for sc in range(scen_dev):
        tile = jnp.where((t_row == 1) & (t_lane == sc), flux_last[2 * sc], tile)
        tile = jnp.where((t_row == 1) & (t_lane == scen_dev + sc), flux_last[2 * sc + 1], tile)
    s_line = lax.broadcasted_iota(jnp.int32, (rows, LANES), 0)
    s_lane = lax.broadcasted_iota(jnp.int32, (rows, LANES), 1)
    for j in range(parts):
        for t in range(tiles):
            first_line = j * tiles + t
            picked = s_line * per_row + first_line
            part_mass = ((base + picked * LANES + s_lane).astype(jnp.float32) + 0.5) / nbin
            for sc in range(scen_dev):
                dens = d_ref[sc, pl.ds(first_line, rows, stride=per_row), :]
                cot = c_ref[sc, pl.ds(first_line, rows, stride=per_row), :]
                o_ref[j, sc * rows:(sc + 1) * rows, t * LANES:(t + 1) * LANES] = part_mass * dens
                o_ref[j, (scen_dev + sc) * rows:(scen_dev + sc + 1) * rows, t * LANES:(t + 1) * LANES] = cot
        o_ref[j, arrays * rows:arrays * rows + 8, :] = tile


def prologue(density, cotangent, rate, offset, nbin, parts, rows, cols):
    scen_dev, bin_dev = density.shape
    lines = bin_dev // LANES
    base = jnp.reshape(offset, (1,)).astype(jnp.int32)
    vmem = pl.BlockSpec(memory_space=pltpu.VMEM)
    return pl.pallas_call(
        functools.partial(prologue_kernel, nbin),
        out_shape=jax.ShapeDtypeStruct((parts, 2 * scen_dev * rows + 8, cols), jnp.float32),
        in_specs=[pl.BlockSpec(memory_space=pltpu.SMEM), vmem, vmem, vmem],
        out_specs=vmem,
    )(base, density.reshape(scen_dev, lines, LANES), cotangent.reshape(scen_dev, lines, LANES),
      rate.reshape(lines, LANES))


def exchange(value):
    return lax.all_to_all(value, "mass", 0, 0, tiled=True)


def shards(density, cotangent, rate):
    high = lax.Precision.HIGHEST
    scen_dev, bin_dev = density.shape
    arrays = 2 * scen_dev
    parts = lax.axis_size("mass")
    place = lax.axis_index("mass")
    width = C1 * C2
    rows = bin_dev // width
    half_rows = rows * parts
    full_rows = 2 * half_rows
    cols = width // parts
    block = full_rows // parts
    nbin = half_rows * width
    nfft = 2 * nbin
    beta = aggregation_coef / nbin
    offset = place * bin_dev
    mass = ((offset + counting(bin_dev)).astype(jnp.float32) + 0.5) / nbin
    weighted = mass[None, :] * density
    flux = rate[None, :] * weighted
    outgoing = prologue(density, cotangent, rate, offset, nbin, parts, rows, cols)
    incoming_rows = exchange(outgoing)
    moments = jnp.sum(incoming_rows[:, arrays * rows, :arrays], axis=0)
    first, cross = moments[:scen_dev], moments[scen_dev:]
    neighbours = incoming_rows[:, arrays * rows + 1, :arrays]
    behind = lax.dynamic_index_in_dim(neighbours, (place + parts - 1) % parts, keepdims=False)
    ahead = lax.dynamic_index_in_dim(neighbours, (place + 1) % parts, keepdims=False)
    incoming = jnp.where(place > 0, behind[:scen_dev], 0.0)[:, None]
    arriving = jnp.where(place < parts - 1, ahead[scen_dev:], 0.0)[:, None]
    spread = incoming_rows[:, : arrays * rows].reshape(parts, arrays, rows, cols)
    spread = spread.transpose(1, 0, 2, 3).reshape(arrays, half_rows, cols)
    half = block // 2
    pos = counting(block)
    own_rows = jnp.where(pos < half, half * place + pos, (full_rows - half * place - (pos - half)) % full_rows)
    own_rows = jnp.where((place == 0) & (pos == half), full_rows // 2, own_rows)
    table = np.arange(block)[None, :]
    order = np.where(table < half, half * np.arange(parts)[:, None] + table,
                     (full_rows - half * np.arange(parts)[:, None] - (table - half)) % full_rows)
    order[0, half] = full_rows // 2
    order_np = order.reshape(-1)
    order = jnp.asarray(order_np, jnp.int32)
    row_angle = 2.0 * np.pi * ((order_np[:, None] * np.arange(half_rows)[None, :]) % full_rows) / full_rows
    row_cos, row_sin = jnp.asarray(np.cos(row_angle), jnp.float32), jnp.asarray(np.sin(row_angle), jnp.float32)
    forward_rows = jnp.stack([jnp.stack([row_cos, row_sin], axis=1), jnp.stack([-row_sin, row_cos], axis=1)])
    packed = spread.reshape(2, scen_dev, half_rows, cols)
    forward_rows = forward_rows.reshape(2, parts, block, 2, half_rows)
    freq = jnp.einsum("ojkir,isrw->joskw", forward_rows, packed, precision=lax.Precision.HIGH)
    tiles = cols // LANES
    coarse_cos, coarse_sin = phases(order, place * cols + counting(tiles) * LANES, nfft)
    fine_angle = 2.0 * np.pi * ((order_np[:, None] * np.arange(LANES)[None, :]) % nfft) / nfft
    fine_cos = jnp.asarray(np.cos(fine_angle), jnp.float32)[:, None, :]
    fine_sin = jnp.asarray(np.sin(fine_angle), jnp.float32)[:, None, :]
    tw_cos, tw_sin = complex_mul((coarse_cos[:, :, None], coarse_sin[:, :, None]), (fine_cos, fine_sin))
    tw_cos, tw_sin = tw_cos.reshape(full_rows, cols), tw_sin.reshape(full_rows, cols)
    tw_cos = tw_cos.reshape(parts, 1, block, cols)
    tw_sin = tw_sin.reshape(parts, 1, block, cols)
    twisted = jnp.stack(complex_mul((freq[:, 0], freq[:, 1]), (tw_cos, -tw_sin)), axis=1)
    following = jnp.concatenate([cotangent[:, 1:], arriving], axis=1)
    local_grad = jnp.sum(weighted * (following - cotangent), axis=0)
    received, local_grad = lax.optimization_barrier((exchange(twisted), local_grad))
    rate_gradient = local_grad
    groups = lax.axis_size("scen")
    if groups & (groups - 1) == 0:
        step = 1
        while step < groups:
            pairs = [(source, source ^ step) for source in range(groups)]
            rate_gradient = rate_gradient + lax.ppermute(rate_gradient, "scen", pairs)
            step *= 2
    else:
        rate_gradient = lax.psum(local_grad, "scen")
    untwisted = column_stage(received, own_rows, place, nfft)
    returned = exchange(untwisted).transpose(1, 2, 0, 3, 4).reshape(2, scen_dev, full_rows, cols)
    inv_cos, inv_sin = row_cos.T, row_sin.T
    inverse_rows = jnp.stack([jnp.stack([inv_cos, -inv_sin], axis=1), jnp.stack([inv_sin, inv_cos], axis=1)])
    inverse_rows = inverse_rows.reshape(2, parts, rows, 2, full_rows)
    real_part = jnp.einsum("ojrik,iskw->josrw", inverse_rows, returned, precision=lax.Precision.HIGH)
    real_part = real_part.reshape(parts, arrays, rows, cols)
    gathered = exchange(real_part).transpose(1, 2, 0, 3).reshape(arrays, bin_dev) / nfft
    birth = gathered[:scen_dev]
    corr = gathered[scen_dev:]
    inflow = jnp.concatenate([incoming, flux[:, :-1]], axis=1)
    tendency = 0.5 * beta * birth - beta * first[:, None] * weighted - flux + inflow
    adjoint = mass[None, :] * (
        beta * corr
        - beta * first[:, None] * cotangent
        - beta * cross[:, None]
        - rate[None, :] * cotangent
        + rate[None, :] * following
    )
    return (tendency, adjoint, rate_gradient)


def solution(mesh):
    in_specs = (P("scen", "mass"), P("scen", "mass"), P("mass"))
    out_specs = (P("scen", "mass"), P("scen", "mass"), P("mass"))
    return jax.shard_map(shards, mesh=mesh, in_specs=in_specs, out_specs=out_specs, check_vma=False)
```

```python
import functools
import math

import jax
import numpy as np
import jax.numpy as jnp
from jax import lax
from jax.experimental import pallas as pl
from jax.experimental.pallas import tpu as pltpu
from jax.sharding import PartitionSpec as P

C1 = 32
C2 = 128


aggregation_coef = 12.0


def from_behind(value, axis, steps):
    count = lax.axis_size(axis)
    first, last = (max(0, -steps), min(count, count - steps))
    return lax.ppermute(value, axis, [(source, source + steps) for source in range(first, last)])


def phases(left, right, total):
    outer = left[:, None] * right[None, :] % total
    angle = outer.astype(jnp.float32) * (2.0 * math.pi / total)
    return (jnp.cos(angle), jnp.sin(angle))


def counting(count):
    return lax.iota(jnp.int32, count)


def complex_dot(form, table, values):
    table_re, table_im = table
    val_re, val_im = values
    high = lax.Precision.HIGHEST
    real_out = jnp.einsum(form, table_re, val_re, precision=high) - jnp.einsum(
        form, table_im, val_im, precision=high
    )
    imag_out = jnp.einsum(form, table_re, val_im, precision=high) + jnp.einsum(
        form, table_im, val_re, precision=high
    )
    return (real_out, imag_out)


def complex_mul(left, right):
    return (left[0] * right[0] - left[1] * right[1], left[0] * right[1] + left[1] * right[0])


def column_forward(values):
    lead = values[0].shape[:-1]
    shaped = (values[0].reshape(lead + (C1, C2)), values[1].reshape(lead + (C1, C2)))
    cos_one, sin_one = phases(counting(C1), counting(C1), C1)
    step_one = complex_dot("pa,...ab->...pb", (cos_one, -sin_one), shaped)
    tw_cos, tw_sin = phases(counting(C1), counting(C2), C1 * C2)
    turned = complex_mul(step_one, (tw_cos, -tw_sin))
    cos_two, sin_two = phases(counting(C2), counting(C2), C2)
    return complex_dot("qb,...pb->...pq", (cos_two, -sin_two), turned)


def column_inverse(values):
    lead = values[0].shape[:-2]
    cos_two, sin_two = phases(counting(C2), counting(C2), C2)
    step_one = complex_dot("qb,...pq->...pb", (cos_two, sin_two), values)
    tw_cos, tw_sin = phases(counting(C1), counting(C2), C1 * C2)
    turned = complex_mul(step_one, (tw_cos, tw_sin))
    cos_one, sin_one = phases(counting(C1), counting(C1), C1)
    result = complex_dot("pa,...pb->...ab", (cos_one, sin_one), turned)
    return (result[0].reshape(lead + (C1 * C2,)), result[1].reshape(lead + (C1 * C2,)))


LANES = 128


def butterfly(values, sign):
    count = len(values)
    if count == 1:
        return list(values)
    even = butterfly(values[0::2], sign)
    odd = butterfly(values[1::2], sign)
    out = [None] * count
    for k in range(count // 2):
        o_re, o_im = odd[k]
        if k == 0:
            t = (o_re, o_im)
        elif 4 * k == count:
            t = (-sign * o_im, sign * o_re)
        else:
            c = math.cos(2.0 * math.pi * k / count)
            s = sign * math.sin(2.0 * math.pi * k / count)
            t = (o_re * c - o_im * s, o_re * s + o_im * c)
        e_re, e_im = even[k]
        out[k] = (e_re + t[0], e_im + t[1])
        out[k + count // 2] = (e_re - t[0], e_im - t[1])
    return out


def column_kernel(x_ref, phi_ref, tw1_ref, tw2_ref, back_ref, flag_ref, dft_ref, o_ref):
    parts, _, scen_dev, block, cols = x_ref.shape
    tiles = cols // LANES
    half = block // 2
    high = lax.Precision.HIGH
    keep = flag_ref[0] > 0.5
    plain = flag_ref[1] > 0.5
    dft_cos = dft_ref[0]
    dft_sin = dft_ref[1]

    def cmul(a, b):
        return (a[0] * b[0] - a[1] * b[1], a[0] * b[1] + a[1] * b[0])

    def transform(grid, sign):
        stage = [butterfly([grid[src][t] for src in range(parts)], sign) for t in range(tiles)]
        turned = []
        for k1 in range(parts):
            row = []
            for t in range(tiles):
                w = (tw1_ref[0, k1 * tiles + t], sign * tw1_ref[1, k1 * tiles + t])
                row.append(cmul(stage[t][k1], w))
            mixed = butterfly(row, sign)
            turned.append([cmul(mixed[m1], (tw2_ref[0, m1], sign * tw2_ref[1, m1])) for m1 in range(tiles)])
        flat_re = jnp.concatenate([turned[k][m][0] for k in range(parts) for m in range(tiles)], axis=0)
        flat_im = jnp.concatenate([turned[k][m][1] for k in range(parts) for m in range(tiles)], axis=0)
        dot = lambda a, b: jnp.dot(a, b, precision=high, preferred_element_type=jnp.float32)
        out_re = dot(flat_re, dft_cos) - sign * dot(flat_im, dft_sin)
        out_im = dot(flat_im, dft_cos) + sign * dot(flat_re, dft_sin)
        return out_re, out_im

    def inverse(flat, sign):
        dot = lambda a, b: jnp.dot(a, b, precision=high, preferred_element_type=jnp.float32)
        f_re, f_im = flat
        b_re = dot(f_re, dft_cos) - sign * dot(f_im, dft_sin)
        b_im = dot(f_im, dft_cos) + sign * dot(f_re, dft_sin)
        piece = lambda a, k, m: a[(k * tiles + m) * block:(k * tiles + m + 1) * block]
        stage = []
        for k1 in range(parts):
            row = [cmul((piece(b_re, k1, m), piece(b_im, k1, m)), (tw2_ref[0, m], sign * tw2_ref[1, m]))
                   for m in range(tiles)]
            mixed = butterfly(row, sign)
            stage.append([cmul(mixed[t], (tw1_ref[0, k1 * tiles + t], sign * tw1_ref[1, k1 * tiles + t]))
                          for t in range(tiles)])
        grid = [butterfly([stage[k1][t] for k1 in range(parts)], sign) for t in range(tiles)]
        return grid

    for sc in range(scen_dev):
        w_grid, c_grid = [], []
        for src in range(parts):
            w_row, c_row = [], []
            for t in range(tiles):
                lanes = slice(t * LANES, (t + 1) * LANES)
                t_re = x_ref[src, 0, sc, :, lanes]
                t_im = x_ref[src, 1, sc, :, lanes]
                swap_re = jnp.concatenate([t_re[half:], t_re[:half]], axis=0)
                swap_im = jnp.concatenate([t_im[half:], t_im[:half]], axis=0)
                p_re = jnp.where(keep, t_re, swap_re)
                p_im = jnp.where(keep, t_im, swap_im)
                f_re = jnp.where(plain, 1.0, phi_ref[0, src * tiles + t])
                f_im = jnp.where(plain, 0.0, -phi_ref[1, src * tiles + t])
                u_re = p_re * f_re + p_im * f_im
                u_im = p_re * f_im - p_im * f_re
                w_row.append((0.5 * (t_re + u_re), 0.5 * (t_im + u_im)))
                c_row.append((0.5 * (t_im - u_im), 0.5 * (u_re - t_re)))
            w_grid.append(w_row)
            c_grid.append(c_row)
        dist = transform(w_grid, -1.0)
        cot = transform(c_grid, -1.0)
        birth = cmul(dist, dist)
        adjoint = cmul(cot, (dist[0], -dist[1]))
        joined = (birth[0] - adjoint[1], birth[1] + adjoint[0])
        grid = inverse(joined, 1.0)
        for src in range(parts):
            for t in range(tiles):
                lanes = slice(t * LANES, (t + 1) * LANES)
                value = cmul(grid[t][src], (back_ref[0, src * tiles + t], back_ref[1, src * tiles + t]))
                o_ref[src, 0, sc, :, lanes] = value[0]
                o_ref[src, 1, sc, :, lanes] = value[1]


def column_stage(received, own_rows, place, nfft):
    parts, _, scen_dev, block, cols = received.shape
    tiles = cols // LANES
    width = parts * cols
    half = block // 2
    pos = counting(block)

    def table(angle):
        return jnp.asarray(np.stack([np.cos(angle), np.sin(angle)]), jnp.float32)

    lane = np.arange(LANES)
    chunk = np.arange(parts * tiles)
    spots = chunk[:, None] * LANES + lane[None, :]
    phi = table(2.0 * np.pi * spots / width).reshape(2, parts * tiles, 1, LANES)
    tw1 = table(2.0 * np.pi * (((chunk % tiles) * LANES)[:, None] + lane[None, :]) * (chunk // tiles)[:, None] / width)
    tw1 = tw1.reshape(2, parts * tiles, 1, LANES)
    tw2 = table(2.0 * np.pi * np.arange(tiles)[:, None] * lane[None, :] / cols).reshape(2, tiles, 1, LANES)
    dft = table(2.0 * np.pi * ((lane[:, None] * lane[None, :]) % LANES) / LANES)
    coarse = phases(own_rows, counting(parts * tiles) * LANES, nfft)
    fine = phases(own_rows, counting(LANES), nfft)
    back = complex_mul((coarse[0].T[:, :, None], coarse[1].T[:, :, None]), (fine[0][None], fine[1][None]))
    back = jnp.stack(back)
    lead = place == 0
    keep = jnp.broadcast_to((lead & ((pos == 0) | (pos == half)))[:, None], (block, LANES))
    plain = jnp.broadcast_to((lead & (pos == 0))[:, None], (block, LANES))
    flags = jnp.stack([keep, plain]).astype(jnp.float32)
    vmem = pl.BlockSpec(memory_space=pltpu.VMEM)
    return pl.pallas_call(
        column_kernel,
        out_shape=jax.ShapeDtypeStruct(received.shape, jnp.float32),
        in_specs=[vmem] * 7,
        out_specs=vmem,
    )(received, phi, tw1, tw2, back, flags, dft)


def prologue_kernel(nbin, base_ref, d_ref, c_ref, r_ref, o_ref):
    parts, _, cols = o_ref.shape
    scen_dev = d_ref.shape[0]
    lines = d_ref.shape[1]
    tiles = cols // LANES
    rows = (o_ref.shape[1] - 8) // (2 * scen_dev)
    per_row = lines // rows
    arrays = 2 * scen_dev
    base = base_ref[0]
    line = lax.broadcasted_iota(jnp.int32, (lines, LANES), 0)
    lane = lax.broadcasted_iota(jnp.int32, (lines, LANES), 1)
    mass = ((base + line * LANES + lane).astype(jnp.float32) + 0.5) / nbin
    sums = []
    flux_last = []
    for sc in range(scen_dev):
        weighted = mass * d_ref[sc]
        sums.append((jnp.sum(weighted), sc))
        sums.append((jnp.sum(c_ref[sc] * weighted), scen_dev + sc))
        flux_last.append(r_ref[lines - 1:lines, LANES - 1:LANES] * weighted[lines - 1:lines, LANES - 1:LANES])
        flux_last.append(c_ref[sc, 0:1, 0:1])
    t_row = lax.broadcasted_iota(jnp.int32, (8, cols), 0)
    t_lane = lax.broadcasted_iota(jnp.int32, (8, cols), 1)
    tile = jnp.zeros((8, cols), jnp.float32)
    for value, slot in sums:
        tile = jnp.where((t_row == 0) & (t_lane == slot), value, tile)
    for sc in range(scen_dev):
        tile = jnp.where((t_row == 1) & (t_lane == sc), flux_last[2 * sc], tile)
        tile = jnp.where((t_row == 1) & (t_lane == scen_dev + sc), flux_last[2 * sc + 1], tile)
    s_line = lax.broadcasted_iota(jnp.int32, (rows, LANES), 0)
    s_lane = lax.broadcasted_iota(jnp.int32, (rows, LANES), 1)
    for j in range(parts):
        for t in range(tiles):
            first_line = j * tiles + t
            picked = s_line * per_row + first_line
            part_mass = ((base + picked * LANES + s_lane).astype(jnp.float32) + 0.5) / nbin
            for sc in range(scen_dev):
                dens = d_ref[sc, pl.ds(first_line, rows, stride=per_row), :]
                cot = c_ref[sc, pl.ds(first_line, rows, stride=per_row), :]
                o_ref[j, sc * rows:(sc + 1) * rows, t * LANES:(t + 1) * LANES] = part_mass * dens
                o_ref[j, (scen_dev + sc) * rows:(scen_dev + sc + 1) * rows, t * LANES:(t + 1) * LANES] = cot
        o_ref[j, arrays * rows:arrays * rows + 8, :] = tile


def prologue(density, cotangent, rate, offset, nbin, parts, rows, cols):
    scen_dev, bin_dev = density.shape
    lines = bin_dev // LANES
    base = jnp.reshape(offset, (1,)).astype(jnp.int32)
    vmem = pl.BlockSpec(memory_space=pltpu.VMEM)
    return pl.pallas_call(
        functools.partial(prologue_kernel, nbin),
        out_shape=jax.ShapeDtypeStruct((parts, 2 * scen_dev * rows + 8, cols), jnp.float32),
        in_specs=[pl.BlockSpec(memory_space=pltpu.SMEM), vmem, vmem, vmem],
        out_specs=vmem,
    )(base, density.reshape(scen_dev, lines, LANES), cotangent.reshape(scen_dev, lines, LANES),
      rate.reshape(lines, LANES))


def exchange(value):
    return lax.all_to_all(value, "mass", 0, 0, tiled=True)


def shards(density, cotangent, rate):
    high = lax.Precision.HIGHEST
    scen_dev, bin_dev = density.shape
    arrays = 2 * scen_dev
    parts = lax.axis_size("mass")
    place = lax.axis_index("mass")
    width = C1 * C2
    rows = bin_dev // width
    half_rows = rows * parts
    full_rows = 2 * half_rows
    cols = width // parts
    block = full_rows // parts
    nbin = half_rows * width
    nfft = 2 * nbin
    beta = aggregation_coef / nbin
    offset = place * bin_dev
    mass = ((offset + counting(bin_dev)).astype(jnp.float32) + 0.5) / nbin
    weighted = mass[None, :] * density
    flux = rate[None, :] * weighted
    outgoing = prologue(density, cotangent, rate, offset, nbin, parts, rows, cols)
    incoming_rows = exchange(outgoing)
    moments = jnp.sum(incoming_rows[:, arrays * rows, :arrays], axis=0)
    first, cross = moments[:scen_dev], moments[scen_dev:]
    neighbours = incoming_rows[:, arrays * rows + 1, :arrays]
    behind = lax.dynamic_index_in_dim(neighbours, (place + parts - 1) % parts, keepdims=False)
    ahead = lax.dynamic_index_in_dim(neighbours, (place + 1) % parts, keepdims=False)
    incoming = jnp.where(place > 0, behind[:scen_dev], 0.0)[:, None]
    arriving = jnp.where(place < parts - 1, ahead[scen_dev:], 0.0)[:, None]
    spread = incoming_rows[:, : arrays * rows].reshape(parts, arrays, rows, cols)
    spread = spread.transpose(1, 0, 2, 3).reshape(arrays, half_rows, cols)
    half = block // 2
    pos = counting(block)
    own_rows = jnp.where(pos < half, half * place + pos, (full_rows - half * place - (pos - half)) % full_rows)
    own_rows = jnp.where((place == 0) & (pos == half), full_rows // 2, own_rows)
    table = np.arange(block)[None, :]
    order = np.where(table < half, half * np.arange(parts)[:, None] + table,
                     (full_rows - half * np.arange(parts)[:, None] - (table - half)) % full_rows)
    order[0, half] = full_rows // 2
    order_np = order.reshape(-1)
    order = jnp.asarray(order_np, jnp.int32)
    row_angle = 2.0 * np.pi * ((order_np[:, None] * np.arange(half_rows)[None, :]) % full_rows) / full_rows
    row_cos, row_sin = jnp.asarray(np.cos(row_angle), jnp.float32), jnp.asarray(np.sin(row_angle), jnp.float32)
    forward_rows = jnp.stack([jnp.stack([row_cos, row_sin], axis=1), jnp.stack([-row_sin, row_cos], axis=1)])
    packed = spread.reshape(2, scen_dev, half_rows, cols)
    freq = jnp.einsum("okir,isrw->oskw", forward_rows, packed, precision=lax.Precision.HIGH)
    tiles = cols // LANES
    coarse_cos, coarse_sin = phases(order, place * cols + counting(tiles) * LANES, nfft)
    fine_angle = 2.0 * np.pi * ((order_np[:, None] * np.arange(LANES)[None, :]) % nfft) / nfft
    fine_cos = jnp.asarray(np.cos(fine_angle), jnp.float32)[:, None, :]
    fine_sin = jnp.asarray(np.sin(fine_angle), jnp.float32)[:, None, :]
    tw_cos, tw_sin = complex_mul((coarse_cos[:, :, None], coarse_sin[:, :, None]), (fine_cos, fine_sin))
    tw_cos, tw_sin = tw_cos.reshape(full_rows, cols), tw_sin.reshape(full_rows, cols)
    twisted = jnp.stack(complex_mul((freq[0], freq[1]), (tw_cos, -tw_sin)))
    twisted = twisted.reshape(2, scen_dev, parts, block, cols).transpose(2, 0, 1, 3, 4)
    following = jnp.concatenate([cotangent[:, 1:], arriving], axis=1)
    local_grad = jnp.sum(weighted * (following - cotangent), axis=0)
    received, local_grad = lax.optimization_barrier((exchange(twisted), local_grad))
    rate_gradient = local_grad
    groups = lax.axis_size("scen")
    if groups & (groups - 1) == 0:
        step = 1
        while step < groups:
            pairs = [(source, source ^ step) for source in range(groups)]
            rate_gradient = rate_gradient + lax.ppermute(rate_gradient, "scen", pairs)
            step *= 2
    else:
        rate_gradient = lax.psum(local_grad, "scen")
    untwisted = column_stage(received, own_rows, place, nfft)
    returned = exchange(untwisted).transpose(1, 2, 0, 3, 4).reshape(2, scen_dev, full_rows, cols)
    inv_cos, inv_sin = row_cos.T, row_sin.T
    inverse_rows = jnp.stack([jnp.stack([inv_cos, -inv_sin], axis=1), jnp.stack([inv_sin, inv_cos], axis=1)])
    real_part = jnp.einsum("orik,iskw->osrw", inverse_rows, returned, precision=lax.Precision.HIGH)
    real_part = real_part.reshape(arrays, half_rows, cols)
    real_part = real_part.reshape(arrays, parts, rows, cols).transpose(1, 0, 2, 3)
    gathered = exchange(real_part).transpose(1, 2, 0, 3).reshape(arrays, bin_dev) / nfft
    birth = gathered[:scen_dev]
    corr = gathered[scen_dev:]
    inflow = jnp.concatenate([incoming, flux[:, :-1]], axis=1)
    rest_t = -beta * first[:, None] * weighted - flux + inflow
    rest_a = (
        -beta * first[:, None] * cotangent
        - beta * cross[:, None]
        - rate[None, :] * cotangent
        + rate[None, :] * following
    )
    rest_t, rest_a = lax.optimization_barrier((rest_t, rest_a))
    tendency = 0.5 * beta * birth + rest_t
    adjoint = mass[None, :] * (beta * corr + rest_a)
    return (tendency, adjoint, rate_gradient)


def solution(mesh):
    in_specs = (P("scen", "mass"), P("scen", "mass"), P("mass"))
    out_specs = (P("scen", "mass"), P("scen", "mass"), P("mass"))
    return jax.shard_map(shards, mesh=mesh, in_specs=in_specs, out_specs=out_specs, check_vma=False)
```
